32 devices in a mesh: scene: 2 (over x), view: 16 (over z, y, core).
Axes of the slice: x: 2, y: 2, z: 4, core: 2. Of those that a mesh axis runs over, the one named last changes fastest.
Arguments:
- src_feat: bfloat16 [32, 32, 8192], P(('scene', 'view')), parts along dimension 0, may hold values from -6 to 6
- ref_feat: bfloat16 [32, 32, 512], P(('scene', 'view')), parts along dimension 0, may hold values from -6 to 6
- weight_table: bfloat16 [4, 128, 512], replicated, may hold values from -0.5 to 0.5
- src_block: int32 [32, 64, 4], P(('scene', 'view')), parts along dimension 0, may hold values from 0 to 63
- table_index: int32 [32, 64, 4], P(('scene', 'view')), parts along dimension 0, may hold values from 0 to 3, each once within a row
- block_count: int32 [32, 64], P(('scene', 'view')), parts along dimension 0, may hold values from 0 to 4, as said below
- depth_plane: int32 [32, 64], P(('scene', 'view')), parts along dimension 0, may hold values from 0 to 63
- kern_one: bfloat16 [3, 3, 3, 8, 8], replicated, may hold values from -0.4375 to 0.4375
- kern_two: bfloat16 [3, 3, 3, 8], replicated, may hold values from -0.4375 to 0.4375
Outputs:
- depth_score: float32 [128, 64, 128], P(('scene', 'view')), parts along dimension 0
The draws below stay inside these ranges and needn't reach their ends.
There are 2 independent parts, one for each index of `scene`. The reference program is written for one: setup_inputs(seed, part) draws one part's arguments, and reference() takes and returns one part's arrays. A program takes and returns all parts, laid end to end along the dimension named above; an argument that names none is the same for every part. Nothing has to cross between parts.
Inputs may be any that keep to these rules, and one draw needn't show every extreme that they name: `block_count`: each entry is the number of live block slots of a unit, 0 for an empty unit; the share of live units differs between source views. `table_index`: the 4 table indices of a unit are distinct.
All inputs are finite; a program needn't handle non-finite values.
Results may differ from the reference program's by a relative error of at most 0.019.
Values may be sent and summed in bfloat16 or wider, within the bound.
No kernel may reach another device: no remote copies, remote signals or barrier semaphores. Data moves between devices by JAX's collectives and lax.ppermute only.
A program may use at most 128 MiB of HBM per device.

```python
import jax
import jax.numpy as jnp
from jax import lax

CH = 32
GROUPS = 8
DEPTH = 64
BLK = 128
NBL = 4
TROWS = 4
TCOLS = 128
CAP = 4
SB = 64
TPIX = 512
SPIX = 8192
SOURCES = 16
TILES = 16
UNITS = 64
ROWS = 64


def draw_block_count(key, part):
    key_density, key_chance, key_count, key_position = jax.random.split(key, 4)
    density = jax.random.randint(key_density, (SOURCES, 1), 1, 5)
    chance_draw = jax.random.randint(key_chance, (SOURCES, UNITS), 0, 4)
    counts = jax.random.randint(key_count, (SOURCES, UNITS), 1, NBL + 1)
    counts = jnp.where(chance_draw < density, counts, 0)
    position = jax.random.randint(key_position, (), 0, SOURCES * UNITS)
    flattened = counts.reshape(-1).at[position].set(NBL)
    return flattened.reshape(SOURCES, UNITS).astype(jnp.int32)


def place_ends(drawn, rng, low, high):
    shape = drawn.shape
    place = [jax.random.randint(jax.random.fold_in(rng, axis), (), 0, shape[axis]) for axis in range(len(shape))]
    drawn = drawn.at[tuple(place)].set(low)
    longest = shape.index(max(shape))
    place[longest] = (place[longest] + 1) % shape[longest]
    return drawn.at[tuple(place)].set(high)


def shard_levels(rng, shape, pieces, low, largest):
    def one(axis_at, parts):
        steps = jax.random.uniform(jax.random.fold_in(jax.random.fold_in(rng, 6), axis_at), (parts,), jnp.float32, low / len(pieces), largest / len(pieces))
        return jnp.repeat(jnp.exp(steps), shape[axis_at] // parts).reshape((-1,) + (1,) * (len(shape) - axis_at - 1))

    factor_of = one(*pieces[0])
    for cut in pieces[1:]:
        factor_of = factor_of * one(*cut)
    return factor_of


def centred(stream_key, shape, spread, most, cuts=(), kind=jnp.bfloat16):
    values = jax.random.normal(stream_key, shape, jnp.float32) * spread
    if len(cuts) > 0:
        values = shard_levels(stream_key, shape, cuts, -0.22, 0.18) * values
    return jnp.clip(values, min=-most, max=most).astype(kind)


def setup_inputs(seed: int = 0, part: int = 0) -> dict:
    key_of = jax.random.split(jax.random.key(seed), 10)
    part_keys = jax.random.split(jax.random.fold_in(key_of[9], part), 10)
    src_feat = centred(part_keys[0], (SOURCES, CH, SPIX), 1.0, 6.0, ((0, 16),))
    ref_feat = centred(part_keys[1], (TILES, CH, TPIX), 1.0, 6.0, ((0, 16),))
    weight_table = centred(key_of[2], (NBL, BLK, TPIX), BLK ** -0.5, 0.5)
    src_block = place_ends(jax.random.randint(part_keys[3], (SOURCES, UNITS, NBL), 0, SB), jax.random.fold_in(part_keys[3], 1), 0, SB - 1).astype(jnp.int32)
    table_index = jax.vmap(lambda own: jax.random.permutation(own, NBL))(jax.random.split(part_keys[4], SOURCES * UNITS)).reshape((SOURCES, UNITS, NBL)).astype(jnp.int32)
    block_count = draw_block_count(jax.random.fold_in(jax.random.fold_in(key_of[9], part), 71), part)
    depth_plane = place_ends(jax.random.randint(part_keys[6], (SOURCES, UNITS), 0, DEPTH), jax.random.fold_in(part_keys[6], 1), 0, DEPTH - 1).astype(jnp.int32)
    kern_one = centred(key_of[7], (3, 3, 3, GROUPS, GROUPS), (27 * GROUPS) ** -0.5, 0.4375)
    kern_two = centred(key_of[8], (3, 3, 3, GROUPS), (27 * GROUPS) ** -0.5, 0.4375)
    return {"src_feat": src_feat, "ref_feat": ref_feat, "weight_table": weight_table, "src_block": src_block, "table_index": table_index, "block_count": block_count, "depth_plane": depth_plane, "kern_one": kern_one, "kern_two": kern_two}


def convolve_full(padded, kernel):
    rows_out = padded.shape[0] - 2
    depth_len = padded.shape[2]
    columns = padded.shape[3]
    framed = jnp.pad(padded.astype(jnp.float32), ((0, 0), (0, 0), (1, 1), (1, 1)))
    carried = jnp.zeros((rows_out, kernel.shape[-1], depth_len, columns), jnp.float32)
    for depth_off in range(3):
        for row_off in range(3):
            for col_off in range(3):
                window = framed[row_off:row_off + rows_out, :, depth_off:depth_off + depth_len, col_off:col_off + columns]
                carried = carried + jnp.einsum("rcdw,ce->redw", window, kernel[depth_off, row_off, col_off].astype(jnp.float32), precision=lax.Precision.HIGHEST)
    return carried


def convolve_final(padded, kernel):
    rows_out = padded.shape[0] - 2
    depth_len = padded.shape[2]
    columns = padded.shape[3]
    framed = jnp.pad(padded.astype(jnp.float32), ((0, 0), (0, 0), (1, 1), (1, 1)))
    carried = jnp.zeros((rows_out, depth_len, columns), jnp.float32)
    for depth_off in range(3):
        for row_off in range(3):
            for col_off in range(3):
                window = framed[row_off:row_off + rows_out, :, depth_off:depth_off + depth_len, col_off:col_off + columns]
                carried = carried + jnp.einsum("rcdw,c->rdw", window, kernel[depth_off, row_off, col_off].astype(jnp.float32), precision=lax.Precision.HIGHEST)
    return carried


def reference(src_feat, ref_feat, weight_table, src_block, table_index, block_count, depth_plane, kern_one, kern_two):
    weights_all = weight_table.astype(jnp.float32)
    references = ref_feat.astype(jnp.float32)
    owner_ids = jnp.arange(UNITS) // CAP

    def per_source(carried, packed):
        features, index_rows, order_rows, counts, depths = packed
        blocks = features.reshape(CH, SB, BLK).transpose(1, 0, 2).astype(jnp.float32)
        gathered = blocks[index_rows]
        live_mask = (jnp.arange(NBL)[None, :] < counts[:, None]).astype(jnp.float32)
        warped = jnp.zeros((UNITS, CH, TPIX), jnp.float32)
        for table_slot in range(NBL):
            chosen = live_mask * (order_rows == table_slot).astype(jnp.float32)
            arranged = jnp.einsum("uj,ujck->uck", chosen, gathered, precision=lax.Precision.HIGHEST)
            warped = warped + jnp.einsum("uck,kp->ucp", arranged, weights_all[table_slot], precision=lax.Precision.HIGHEST)
        warped = warped.astype(jnp.bfloat16)
        products = references[owner_ids] * warped.astype(jnp.float32)
        correlation = (products.reshape(UNITS, GROUPS, CH // GROUPS, TPIX).sum(axis=2) * (GROUPS / CH)).astype(jnp.bfloat16)
        depth_tags = jnp.where(counts > 0, depths, -1)
        onehot = (depth_tags[:, None] == jnp.arange(DEPTH)[None, :]).astype(jnp.float32).reshape(TILES, CAP, DEPTH)
        increment = jnp.einsum("tkd,tkx->tdx", onehot, correlation.astype(jnp.float32).reshape(TILES, CAP, GROUPS * TPIX), precision=lax.Precision.HIGHEST)
        return (carried[0] + increment, carried[1] + onehot.sum(axis=1)), None

    start = (jnp.zeros((TILES, DEPTH, GROUPS * TPIX), jnp.float32), jnp.zeros((TILES, DEPTH), jnp.float32))
    (summed, tallies), _ = lax.scan(per_source, start, (src_feat, src_block, table_index, block_count, depth_plane))
    cost_volume = (summed / jnp.maximum(tallies, 1.0)[:, :, None]).astype(jnp.bfloat16)
    volume = cost_volume.reshape(TILES, DEPTH, GROUPS, TROWS, TCOLS).transpose(0, 3, 2, 1, 4).reshape(ROWS, GROUPS, DEPTH, TCOLS)
    hidden = jax.nn.relu(convolve_full(jnp.pad(volume, ((1, 1), (0, 0), (0, 0), (0, 0))), kern_one)).astype(jnp.bfloat16)
    return convolve_final(jnp.pad(hidden, ((1, 1), (0, 0), (0, 0), (0, 0))), kern_two)
```

```python
import jax
import jax.numpy as jnp
from jax import lax
from jax.sharding import PartitionSpec as P

GROUPS = 8
DEPTH = 64
TROWS = 4


def with_halo(block, sides, width):
    for axis, dim in sides:
        count = lax.axis_size(axis)
        forward = [(i, i + 1) for i in range(count - 1)]
        backward = [(target, source) for source, target in forward]
        low = lax.ppermute(
            lax.slice_in_dim(block, block.shape[dim] - width, None, axis=dim), axis, forward
        )
        high = lax.ppermute(lax.slice_in_dim(block, 0, width, axis=dim), axis, backward)
        block = jnp.concatenate([low, block, high], axis=dim)
    return block


def convolve_full(padded, kernel):
    rows_out = padded.shape[0] - 2
    depth_len = padded.shape[2]
    columns = padded.shape[3]
    framed = jnp.pad(padded, ((0, 0), (0, 0), (1, 1), (1, 1)))
    carried = jnp.zeros((rows_out, kernel.shape[-1], depth_len, columns), jnp.float32)
    for depth_off in range(3):
        for row_off in range(3):
            for col_off in range(3):
                window = framed[
                    row_off : row_off + rows_out,
                    :,
                    depth_off : depth_off + depth_len,
                    col_off : col_off + columns,
                ]
                carried = carried + jnp.einsum(
                    "rcdw,ce->redw",
                    window,
                    kernel[depth_off, row_off, col_off],
                    preferred_element_type=jnp.float32,
                )
    return carried


def convolve_final(padded, kernel):
    rows_out = padded.shape[0] - 2
    depth_len = padded.shape[2]
    columns = padded.shape[3]
    framed = jnp.pad(padded, ((0, 0), (0, 0), (1, 1), (1, 1)))
    carried = jnp.zeros((rows_out, depth_len, columns), jnp.float32)
    for depth_off in range(3):
        for row_off in range(3):
            for col_off in range(3):
                window = framed[
                    row_off : row_off + rows_out,
                    :,
                    depth_off : depth_off + depth_len,
                    col_off : col_off + columns,
                ]
                carried = carried + jnp.einsum(
                    "rcdw,c->rdw",
                    window,
                    kernel[depth_off, row_off, col_off],
                    preferred_element_type=jnp.float32,
                )
    return carried


def pad_rows(volume):
    return with_halo(volume, (("view", 0),), 1)


def body(
    src_feat,
    ref_feat,
    weight_table,
    src_block,
    table_index,
    block_count,
    depth_plane,
    kern_one,
    kern_two,
):
    owners = lax.axis_size("view")
    features = src_feat[0]
    channels, spix = features.shape
    slots, block_width, tpix = weight_table.shape
    blocks = features.reshape(channels, spix // block_width, block_width).transpose(1, 0, 2)
    units = src_block.shape[1]
    cap = units // owners
    counts = block_count[0]
    live_slot = jnp.arange(slots)[None, :] < counts[:, None]
    chosen = (
        (table_index[0][:, :, None] == jnp.arange(slots)[None, None, :]) & live_slot[:, :, None]
    ).astype(jnp.bfloat16)
    depth_code = jnp.where(counts > 0, depth_plane[0], -1).astype(jnp.bfloat16)
    unit_rounds = 8
    per_round = units // unit_rounds
    index_groups = src_block[0].reshape(unit_rounds, per_round, slots)
    chosen_groups = chosen.reshape(unit_rounds, per_round, slots, slots)
    group_size = channels // GROUPS

    ref_all = lax.all_gather(ref_feat[0], "view")
    ref_units = jnp.repeat(ref_all, cap, axis=0).reshape(unit_rounds, per_round, channels, tpix)

    def resample(index_rows, chosen_rows, ref_rows):
        gathered = blocks[index_rows]
        arranged = jnp.einsum(
            "ujw,ujck->uwck", chosen_rows, gathered, preferred_element_type=jnp.float32
        ).astype(jnp.bfloat16)
        warped = jnp.einsum(
            "uwck,wkp->ucp", arranged, weight_table, preferred_element_type=jnp.float32
        ).astype(jnp.bfloat16)
        products = ref_rows.astype(jnp.float32) * warped.astype(jnp.float32)
        return (
            (products.reshape(per_round, GROUPS, group_size, tpix).sum(axis=2) * (GROUPS / channels))
            .astype(jnp.bfloat16)
            .reshape(per_round, GROUPS * tpix)
        )

    corr_all = lax.map(
        lambda packed: resample(packed[0], packed[1], packed[2]),
        (index_groups, chosen_groups, ref_units),
    ).reshape(units, GROUPS * tpix)
    tag_lanes = jnp.broadcast_to(depth_code[:, None], (units, 128))
    payload = jnp.concatenate([corr_all, tag_lanes], axis=1)
    arriving = lax.all_to_all(
        payload.reshape(owners, cap, GROUPS * tpix + 128),
        "view",
        split_axis=0,
        concat_axis=0,
        tiled=True,
    ).reshape(owners * cap, GROUPS * tpix + 128)
    received = arriving[:, : GROUPS * tpix]
    depth_tags = arriving[:, GROUPS * tpix]
    onehot = (
        depth_tags[None, :] == jnp.arange(DEPTH).astype(jnp.bfloat16)[:, None]
    ).astype(jnp.bfloat16)
    summed = jnp.dot(onehot, received, preferred_element_type=jnp.float32)
    tallies = jnp.sum(onehot.astype(jnp.float32), axis=1)
    cost_volume = (summed / jnp.maximum(tallies, 1.0)[:, None]).astype(jnp.bfloat16)
    columns = tpix // TROWS
    volume = cost_volume.reshape(DEPTH, GROUPS, TROWS, columns).transpose(2, 1, 0, 3)
    hidden = jax.nn.relu(convolve_full(pad_rows(volume), kern_one)).astype(jnp.bfloat16)
    scores = convolve_final(pad_rows(hidden), kern_two)
    return scores


def solution(mesh):
    in_specs = (
        P(("scene", "view"), None, None),
        P(("scene", "view"), None, None),
        P(),
        P(("scene", "view"), None, None),
        P(("scene", "view"), None, None),
        P(("scene", "view"), None),
        P(("scene", "view"), None),
        P(),
        P(),
    )
    out_specs = P(("scene", "view"), None, None)
    return jax.shard_map(body, mesh=mesh, in_specs=in_specs, out_specs=out_specs, check_vma=False)
```

```python
import jax
import jax.numpy as jnp
from jax import lax
from jax.sharding import PartitionSpec as P

GROUPS = 8
DEPTH = 64
TROWS = 4


def with_halo(block, sides, width):
    for axis, dim in sides:
        count = lax.axis_size(axis)
        forward = [(i, i + 1) for i in range(count - 1)]
        backward = [(target, source) for source, target in forward]
        low = lax.ppermute(
            lax.slice_in_dim(block, block.shape[dim] - width, None, axis=dim), axis, forward
        )
        high = lax.ppermute(lax.slice_in_dim(block, 0, width, axis=dim), axis, backward)
        block = jnp.concatenate([low, block, high], axis=dim)
    return block


def convolve_full(padded, kernel):
    rows_out = padded.shape[0] - 2
    depth_len = padded.shape[2]
    columns = padded.shape[3]
    framed = jnp.pad(padded, ((0, 0), (0, 0), (1, 1), (1, 1)))
    carried = jnp.zeros((rows_out, kernel.shape[-1], depth_len, columns), jnp.float32)
    for depth_off in range(3):
        for row_off in range(3):
            for col_off in range(3):
                window = framed[
                    row_off : row_off + rows_out,
                    :,
                    depth_off : depth_off + depth_len,
                    col_off : col_off + columns,
                ]
                carried = carried + jnp.einsum(
                    "rcdw,ce->redw",
                    window,
                    kernel[depth_off, row_off, col_off],
                    preferred_element_type=jnp.float32,
                )
    return carried


def convolve_final(padded, kernel):
    rows_out = padded.shape[0] - 2
    depth_len = padded.shape[2]
    columns = padded.shape[3]
    framed = jnp.pad(padded, ((0, 0), (0, 0), (1, 1), (1, 1)))
    carried = jnp.zeros((rows_out, depth_len, columns), jnp.float32)
    for depth_off in range(3):
        for row_off in range(3):
            for col_off in range(3):
                window = framed[
                    row_off : row_off + rows_out,
                    :,
                    depth_off : depth_off + depth_len,
                    col_off : col_off + columns,
                ]
                carried = carried + jnp.einsum(
                    "rcdw,c->rdw",
                    window,
                    kernel[depth_off, row_off, col_off],
                    preferred_element_type=jnp.float32,
                )
    return carried


def pad_rows(volume):
    return with_halo(volume, (("view", 0),), 1)


def body(
    src_feat,
    ref_feat,
    weight_table,
    src_block,
    table_index,
    block_count,
    depth_plane,
    kern_one,
    kern_two,
):
    owners = lax.axis_size("view")
    features = src_feat[0]
    channels, spix = features.shape
    slots, block_width, tpix = weight_table.shape
    blocks = features.reshape(channels, spix // block_width, block_width).transpose(1, 0, 2)
    units = src_block.shape[1]
    cap = units // owners
    counts = block_count[0]
    live_slot = jnp.arange(slots)[None, :] < counts[:, None]
    chosen = (
        (table_index[0][:, :, None] == jnp.arange(slots)[None, None, :]) & live_slot[:, :, None]
    ).astype(jnp.bfloat16)
    depth_code = jnp.where(counts > 0, depth_plane[0], -1).astype(jnp.bfloat16)
    unit_rounds = 8
    per_round = units // unit_rounds
    index_groups = src_block[0].reshape(unit_rounds, per_round, slots)
    chosen_groups = chosen.reshape(unit_rounds, per_round, slots, slots)
    group_size = channels // GROUPS

    ref_all = lax.all_to_all(
        jnp.broadcast_to(ref_feat, (owners,) + ref_feat.shape[1:]),
        "view",
        split_axis=0,
        concat_axis=0,
        tiled=True,
    )

    def resample(index_rows, chosen_rows):
        gathered = blocks[index_rows]
        arranged = jnp.einsum(
            "ujw,ujck->uwck", chosen_rows, gathered, preferred_element_type=jnp.float32
        ).astype(jnp.bfloat16)
        return jnp.einsum(
            "uwck,wkp->ucp", arranged, weight_table, preferred_element_type=jnp.float32
        ).astype(jnp.bfloat16)

    warped_all = lax.map(
        lambda packed: resample(packed[0], packed[1]), (index_groups, chosen_groups)
    ).reshape(owners, cap, channels, tpix)
    products = ref_all.astype(jnp.float32)[:, None] * warped_all.astype(jnp.float32)
    corr_all = (
        (products.reshape(units, GROUPS, group_size, tpix).sum(axis=2) * (GROUPS / channels))
        .astype(jnp.bfloat16)
        .reshape(units, GROUPS * tpix)
    )
    tag_lanes = jnp.broadcast_to(depth_code[:, None], (units, 128))
    payload = jnp.concatenate([corr_all, tag_lanes], axis=1)
    arriving = lax.all_to_all(
        payload.reshape(owners, cap, GROUPS * tpix + 128),
        "view",
        split_axis=0,
        concat_axis=0,
        tiled=True,
    ).reshape(owners * cap, GROUPS * tpix + 128)
    received = arriving[:, : GROUPS * tpix]
    depth_tags = arriving[:, GROUPS * tpix]
    onehot = (
        depth_tags[None, :] == jnp.arange(DEPTH).astype(jnp.bfloat16)[:, None]
    ).astype(jnp.bfloat16)
    summed = jnp.dot(onehot, received, preferred_element_type=jnp.float32)
    tallies = jnp.sum(onehot.astype(jnp.float32), axis=1)
    cost_volume = (summed / jnp.maximum(tallies, 1.0)[:, None]).astype(jnp.bfloat16)
    columns = tpix // TROWS
    volume = cost_volume.reshape(DEPTH, GROUPS, TROWS, columns).transpose(2, 1, 0, 3)
    hidden = jax.nn.relu(convolve_full(pad_rows(volume), kern_one)).astype(jnp.bfloat16)
    scores = convolve_final(pad_rows(hidden), kern_two)
    return scores


def solution(mesh):
    in_specs = (
        P(("scene", "view"), None, None),
        P(("scene", "view"), None, None),
        P(),
        P(("scene", "view"), None, None),
        P(("scene", "view"), None, None),
        P(("scene", "view"), None),
        P(("scene", "view"), None),
        P(),
        P(),
    )
    out_specs = P(("scene", "view"), None, None)
    return jax.shard_map(body, mesh=mesh, in_specs=in_specs, out_specs=out_specs, check_vma=False)
```

```python
import jax
import jax.numpy as jnp
from jax import lax
from jax.experimental import pallas as pl
from jax.experimental.pallas import tpu as pltpu
from jax.sharding import PartitionSpec as P

GROUPS = 8
DEPTH = 64
TROWS = 4


def with_halo(block, sides, width):
    for axis, dim in sides:
        count = lax.axis_size(axis)
        forward = [(i, i + 1) for i in range(count - 1)]
        backward = [(target, source) for source, target in forward]
        low = lax.ppermute(
            lax.slice_in_dim(block, block.shape[dim] - width, None, axis=dim), axis, forward
        )
        high = lax.ppermute(lax.slice_in_dim(block, 0, width, axis=dim), axis, backward)
        block = jnp.concatenate([low, block, high], axis=dim)
    return block


def convolve_full(padded, kernel):
    rows_out = padded.shape[0] - 2
    depth_len = padded.shape[2]
    columns = padded.shape[3]
    framed = jnp.pad(padded, ((0, 0), (0, 0), (1, 1), (1, 1)))
    carried = jnp.zeros((rows_out, kernel.shape[-1], depth_len, columns), jnp.float32)
    for depth_off in range(3):
        for row_off in range(3):
            for col_off in range(3):
                window = framed[
                    row_off : row_off + rows_out,
                    :,
                    depth_off : depth_off + depth_len,
                    col_off : col_off + columns,
                ]
                carried = carried + jnp.einsum(
                    "rcdw,ce->redw",
                    window,
                    kernel[depth_off, row_off, col_off],
                    preferred_element_type=jnp.float32,
                )
    return carried


def convolve_final(padded, kernel):
    rows_out = padded.shape[0] - 2
    depth_len = padded.shape[2]
    columns = padded.shape[3]
    framed = jnp.pad(padded, ((0, 0), (0, 0), (1, 1), (1, 1)))
    carried = jnp.zeros((rows_out, depth_len, columns), jnp.float32)
    for depth_off in range(3):
        for row_off in range(3):
            for col_off in range(3):
                window = framed[
                    row_off : row_off + rows_out,
                    :,
                    depth_off : depth_off + depth_len,
                    col_off : col_off + columns,
                ]
                carried = carried + jnp.einsum(
                    "rcdw,c->rdw",
                    window,
                    kernel[depth_off, row_off, col_off],
                    preferred_element_type=jnp.float32,
                )
    return carried


def correlate_kernel(blk_ref, blocks_ref, table_ref, ref_ref, out_ref, arranged, products):
    chunk = 8
    slots = table_ref.shape[0] // blocks_ref.shape[2]
    width = blocks_ref.shape[2]
    channels = blocks_ref.shape[1]
    units = out_ref.shape[0] // GROUPS
    cap = units // ref_ref.shape[0]
    group_size = channels // GROUPS
    rows = chunk * channels

    def step(c, carry):
        for u in range(chunk):
            unit = c * chunk + u
            for w in range(slots):
                arranged[u * channels : (u + 1) * channels, w * width : (w + 1) * width] = blocks_ref[
                    blk_ref[unit * slots + w]
                ]
        warped = jnp.dot(arranged[...], table_ref[...], preferred_element_type=jnp.float32)
        warped = warped.astype(jnp.bfloat16).astype(jnp.float32)
        lanes = products.shape[0]
        for u in range(chunk):
            unit = c * chunk + u
            tile = ref_ref[unit // cap].astype(jnp.float32)
            for j in range(lanes):
                products[j, u * channels : (u + 1) * channels, :] = (
                    warped[u * channels : (u + 1) * channels, j * 128 : (j + 1) * 128]
                    * tile[:, j * 128 : (j + 1) * 128]
                )
        start = pl.multiple_of(c * (chunk * GROUPS), chunk * GROUPS)
        for j in range(lanes):
            total = products[j, pl.ds(0, rows // group_size, stride=group_size), :]
            for k in range(1, group_size):
                total = total + products[j, pl.ds(k, rows // group_size, stride=group_size), :]
            out_ref[pl.ds(start, chunk * GROUPS), j * 128 : (j + 1) * 128] = (
                total * (GROUPS / channels)
            ).astype(out_ref.dtype)
        return carry

    lax.fori_loop(0, units // chunk, step, 0)


def correlate(blk, blocks, table, refs, units):
    channels, width = blocks.shape[1], blocks.shape[2]
    tpix = table.shape[1]
    chunk = 8
    return pl.pallas_call(
        correlate_kernel,
        out_shape=jax.ShapeDtypeStruct((units * GROUPS, tpix), jnp.bfloat16),
        in_specs=[
            pl.BlockSpec(memory_space=pltpu.SMEM),
            pl.BlockSpec(memory_space=pltpu.VMEM),
            pl.BlockSpec(memory_space=pltpu.VMEM),
            pl.BlockSpec(memory_space=pltpu.VMEM),
        ],
        out_specs=pl.BlockSpec(memory_space=pltpu.VMEM),
        scratch_shapes=[
            pltpu.VMEM((chunk * channels, table.shape[0]), jnp.bfloat16),
            pltpu.VMEM((tpix // 128, chunk * channels, 128), jnp.float32),
        ],
    )(blk, blocks, table, refs)


def pad_rows(volume):
    return with_halo(volume, (("view", 0),), 1)


def body(
    src_feat,
    ref_feat,
    weight_table,
    src_block,
    table_index,
    block_count,
    depth_plane,
    kern_one,
    kern_two,
):
    owners = lax.axis_size("view")
    features = src_feat[0]
    channels, spix = features.shape
    slots, block_width, tpix = weight_table.shape
    blocks = features.reshape(channels, spix // block_width, block_width).transpose(1, 0, 2)
    units = src_block.shape[1]
    cap = units // owners
    counts = block_count[0]
    nblocks = spix // block_width
    blocks = jnp.concatenate([blocks, jnp.zeros_like(blocks[:1])], axis=0)
    matches = table_index[0][:, :, None] == jnp.arange(slots)[None, None, :]
    live = (jnp.arange(slots)[None, :] < counts[:, None])[:, :, None] & matches
    picked = jnp.sum(jnp.where(matches, src_block[0][:, :, None], 0), axis=1)
    alive = jnp.any(live, axis=1)
    blk = jnp.where(alive, picked, nblocks).reshape(-1).astype(jnp.int32)
    depth_code = jnp.where(counts > 0, depth_plane[0], -1).astype(jnp.bfloat16)

    ref_all = lax.all_to_all(
        jnp.broadcast_to(ref_feat, (owners,) + ref_feat.shape[1:]),
        "view",
        split_axis=0,
        concat_axis=0,
        tiled=True,
    )
    corr_all = correlate(
        blk, blocks, weight_table.reshape(slots * block_width, tpix), ref_all, units
    ).reshape(units, GROUPS * tpix)
    tag_lanes = jnp.broadcast_to(depth_code[:, None], (units, 128))
    payload = jnp.concatenate([corr_all, tag_lanes], axis=1)
    arriving = lax.all_to_all(
        payload.reshape(owners, cap, GROUPS * tpix + 128),
        "view",
        split_axis=0,
        concat_axis=0,
        tiled=True,
    ).reshape(owners * cap, GROUPS * tpix + 128)
    received = arriving[:, : GROUPS * tpix]
    depth_tags = arriving[:, GROUPS * tpix]
    onehot = (
        depth_tags[None, :] == jnp.arange(DEPTH).astype(jnp.bfloat16)[:, None]
    ).astype(jnp.bfloat16)
    summed = jnp.dot(onehot, received, preferred_element_type=jnp.float32)
    tallies = jnp.sum(onehot.astype(jnp.float32), axis=1)
    cost_volume = (summed / jnp.maximum(tallies, 1.0)[:, None]).astype(jnp.bfloat16)
    columns = tpix // TROWS
    volume = cost_volume.reshape(DEPTH, GROUPS, TROWS, columns).transpose(2, 1, 0, 3)
    hidden = jax.nn.relu(convolve_full(pad_rows(volume), kern_one)).astype(jnp.bfloat16)
    scores = convolve_final(pad_rows(hidden), kern_two)
    return scores


def solution(mesh):
    in_specs = (
        P(("scene", "view"), None, None),
        P(("scene", "view"), None, None),
        P(),
        P(("scene", "view"), None, None),
        P(("scene", "view"), None, None),
        P(("scene", "view"), None),
        P(("scene", "view"), None),
        P(),
        P(),
    )
    out_specs = P(("scene", "view"), None, None)
    return jax.shard_map(body, mesh=mesh, in_specs=in_specs, out_specs=out_specs, check_vma=False)
```

```python
import functools

import jax
import jax.numpy as jnp
from jax import lax
from jax.experimental import pallas as pl
from jax.experimental.pallas import tpu as pltpu
from jax.sharding import PartitionSpec as P

GROUPS = 8
DEPTH = 64
TROWS = 4


def with_halo(block, sides, width):
    for axis, dim in sides:
        count = lax.axis_size(axis)
        forward = [(i, i + 1) for i in range(count - 1)]
        backward = [(target, source) for source, target in forward]
        low = lax.ppermute(
            lax.slice_in_dim(block, block.shape[dim] - width, None, axis=dim), axis, forward
        )
        high = lax.ppermute(lax.slice_in_dim(block, 0, width, axis=dim), axis, backward)
        block = jnp.concatenate([low, block, high], axis=dim)
    return block


def convolve_full(padded, kernel):
    rows_out = padded.shape[0] - 2
    depth_len = padded.shape[2]
    columns = padded.shape[3]
    framed = jnp.pad(padded, ((0, 0), (0, 0), (1, 1), (1, 1)))
    carried = jnp.zeros((rows_out, kernel.shape[-1], depth_len, columns), jnp.float32)
    for depth_off in range(3):
        for row_off in range(3):
            for col_off in range(3):
                window = framed[
                    row_off : row_off + rows_out,
                    :,
                    depth_off : depth_off + depth_len,
                    col_off : col_off + columns,
                ]
                carried = carried + jnp.einsum(
                    "rcdw,ce->redw",
                    window,
                    kernel[depth_off, row_off, col_off],
                    preferred_element_type=jnp.float32,
                )
    return carried


def convolve_final(padded, kernel):
    rows_out = padded.shape[0] - 2
    depth_len = padded.shape[2]
    columns = padded.shape[3]
    framed = jnp.pad(padded, ((0, 0), (0, 0), (1, 1), (1, 1)))
    carried = jnp.zeros((rows_out, depth_len, columns), jnp.float32)
    for depth_off in range(3):
        for row_off in range(3):
            for col_off in range(3):
                window = framed[
                    row_off : row_off + rows_out,
                    :,
                    depth_off : depth_off + depth_len,
                    col_off : col_off + columns,
                ]
                carried = carried + jnp.einsum(
                    "rcdw,c->rdw",
                    window,
                    kernel[depth_off, row_off, col_off],
                    preferred_element_type=jnp.float32,
                )
    return carried


def correlate_kernel(blk_ref, blocks_ref, table_ref, ref_ref, out_ref, arranged, products):
    chunk = 8
    slots = table_ref.shape[0] // blocks_ref.shape[2]
    width = blocks_ref.shape[2]
    channels = blocks_ref.shape[1]
    units = out_ref.shape[0] // GROUPS
    cap = units // ref_ref.shape[0]
    group_size = channels // GROUPS
    rows = chunk * channels

    def step(c, carry):
        for u in range(chunk):
            unit = c * chunk + u
            for w in range(slots):
                arranged[u * channels : (u + 1) * channels, w * width : (w + 1) * width] = blocks_ref[
                    blk_ref[unit * slots + w]
                ]
        warped = jnp.dot(arranged[...], table_ref[...], preferred_element_type=jnp.float32)
        warped = warped.astype(jnp.bfloat16).astype(jnp.float32)
        lanes = products.shape[0]
        for u in range(chunk):
            unit = c * chunk + u
            tile = ref_ref[unit // cap].astype(jnp.float32)
            for j in range(lanes):
                products[j, u * channels : (u + 1) * channels, :] = (
                    warped[u * channels : (u + 1) * channels, j * 128 : (j + 1) * 128]
                    * tile[:, j * 128 : (j + 1) * 128]
                )
        start = pl.multiple_of(c * (chunk * GROUPS), chunk * GROUPS)
        for j in range(lanes):
            total = products[j, pl.ds(0, rows // group_size, stride=group_size), :]
            for k in range(1, group_size):
                total = total + products[j, pl.ds(k, rows // group_size, stride=group_size), :]
            out_ref[pl.ds(start, chunk * GROUPS), j * 128 : (j + 1) * 128] = (
                total * (GROUPS / channels)
            ).astype(out_ref.dtype)
        return carry

    lax.fori_loop(0, units // chunk, step, 0)


def correlate(blk, blocks, table, refs, units):
    channels, width = blocks.shape[1], blocks.shape[2]
    tpix = table.shape[1]
    chunk = 8
    return pl.pallas_call(
        correlate_kernel,
        out_shape=jax.ShapeDtypeStruct((units * GROUPS, tpix), jnp.bfloat16),
        in_specs=[
            pl.BlockSpec(memory_space=pltpu.SMEM),
            pl.BlockSpec(memory_space=pltpu.VMEM),
            pl.BlockSpec(memory_space=pltpu.VMEM),
            pl.BlockSpec(memory_space=pltpu.VMEM),
        ],
        out_specs=pl.BlockSpec(memory_space=pltpu.VMEM),
        scratch_shapes=[
            pltpu.VMEM((chunk * channels, table.shape[0]), jnp.bfloat16),
            pltpu.VMEM((tpix // 128, chunk * channels, 128), jnp.float32),
        ],
    )(blk, blocks, table, refs)


def conv_kernel(x_ref, m_ref, out_ref, *, relu, rows, cols):
    width = rows * cols
    lane = lax.broadcasted_iota(jnp.int32, (m_ref.shape[2], width), 1) % cols
    acc = None
    for e in range(3):
        y = None
        for b in range(3):
            part = jnp.dot(
                m_ref[e, b], x_ref[:, b * cols : b * cols + width], preferred_element_type=jnp.float32
            )
            y = part if y is None else y + part
        if e == 0:
            y = jnp.where(lane >= 1, pltpu.roll(y, 1, 1), 0.0)
        elif e == 2:
            y = jnp.where(lane <= cols - 2, pltpu.roll(y, width - 1, 1), 0.0)
        acc = y if acc is None else acc + y
    if relu:
        out_ref[...] = jnp.maximum(acc, 0.0).astype(out_ref.dtype)
    else:
        for r in range(rows):
            out_ref[r] = acc[:, r * cols : (r + 1) * cols]


def banded(kernel, depth):
    shift = (
        jnp.arange(depth)[None, :, None] + jnp.arange(3)[:, None, None] - 1
        == jnp.arange(depth)[None, None, :]
    ).astype(kernel.dtype)
    if kernel.ndim == 5:
        mats = jnp.einsum("abeio,adz->ebodiz", kernel, shift, preferred_element_type=jnp.float32)
    else:
        mats = jnp.einsum("abei,adz->ebdiz", kernel, shift, preferred_element_type=jnp.float32)
    outs = mats.shape[2] * mats.shape[3] if kernel.ndim == 5 else mats.shape[2]
    return mats.astype(kernel.dtype).reshape(3, 3, outs, -1)


def conv_rows(framed, mats, relu, rows, cols):
    outs = mats.shape[2]
    if relu:
        out_shape = jax.ShapeDtypeStruct((outs, rows * cols), jnp.bfloat16)
    else:
        out_shape = jax.ShapeDtypeStruct((rows, outs, cols), jnp.float32)
    return pl.pallas_call(
        functools.partial(conv_kernel, relu=relu, rows=rows, cols=cols),
        out_shape=out_shape,
        in_specs=[pl.BlockSpec(memory_space=pltpu.VMEM), pl.BlockSpec(memory_space=pltpu.VMEM)],
        out_specs=pl.BlockSpec(memory_space=pltpu.VMEM),
    )(framed, mats)


def halo_cols(block, cols):
    count = lax.axis_size("view")
    forward = [(i, i + 1) for i in range(count - 1)]
    backward = [(target, source) for source, target in forward]
    low = lax.ppermute(block[:, block.shape[1] - cols :], "view", forward)
    high = lax.ppermute(block[:, :cols], "view", backward)
    return jnp.concatenate([low, block, high], axis=1)


def pad_rows(volume):
    return with_halo(volume, (("view", 0),), 1)


def body(
    src_feat,
    ref_feat,
    weight_table,
    src_block,
    table_index,
    block_count,
    depth_plane,
    kern_one,
    kern_two,
):
    owners = lax.axis_size("view")
    features = src_feat[0]
    channels, spix = features.shape
    slots, block_width, tpix = weight_table.shape
    blocks = features.reshape(channels, spix // block_width, block_width).transpose(1, 0, 2)
    units = src_block.shape[1]
    cap = units // owners
    counts = block_count[0]
    nblocks = spix // block_width
    blocks = jnp.concatenate([blocks, jnp.zeros_like(blocks[:1])], axis=0)
    matches = table_index[0][:, :, None] == jnp.arange(slots)[None, None, :]
    live = (jnp.arange(slots)[None, :] < counts[:, None])[:, :, None] & matches
    picked = jnp.sum(jnp.where(matches, src_block[0][:, :, None], 0), axis=1)
    alive = jnp.any(live, axis=1)
    blk = jnp.where(alive, picked, nblocks).reshape(-1).astype(jnp.int32)
    depth_code = jnp.where(counts > 0, depth_plane[0], -1).astype(jnp.bfloat16)

    ref_all = lax.all_to_all(
        jnp.broadcast_to(ref_feat, (owners,) + ref_feat.shape[1:]),
        "view",
        split_axis=0,
        concat_axis=0,
        tiled=True,
    )
    corr_all = correlate(
        blk, blocks, weight_table.reshape(slots * block_width, tpix), ref_all, units
    ).reshape(units, GROUPS * tpix)
    tag_lanes = jnp.broadcast_to(depth_code[:, None], (units, 128))
    payload = jnp.concatenate([corr_all, tag_lanes], axis=1)
    arriving = lax.all_to_all(
        payload.reshape(owners, cap, GROUPS * tpix + 128),
        "view",
        split_axis=0,
        concat_axis=0,
        tiled=True,
    ).reshape(owners * cap, GROUPS * tpix + 128)
    received = arriving[:, : GROUPS * tpix]
    depth_tags = arriving[:, GROUPS * tpix]
    onehot = (
        depth_tags[None, :] == jnp.arange(DEPTH).astype(jnp.bfloat16)[:, None]
    ).astype(jnp.bfloat16)
    summed = jnp.dot(onehot, received, preferred_element_type=jnp.float32)
    tallies = jnp.sum(onehot.astype(jnp.float32), axis=1)
    cost_volume = (summed / jnp.maximum(tallies, 1.0)[:, None]).astype(jnp.bfloat16)
    columns = tpix // TROWS
    volume = cost_volume.reshape(DEPTH, GROUPS, TROWS * columns).transpose(1, 0, 2)
    volume = volume.reshape(GROUPS * DEPTH, TROWS * columns)
    hidden = conv_rows(halo_cols(volume, columns), banded(kern_one, DEPTH), True, TROWS, columns)
    scores = conv_rows(halo_cols(hidden, columns), banded(kern_two, DEPTH), False, TROWS, columns)
    return scores


def solution(mesh):
    in_specs = (
        P(("scene", "view"), None, None),
        P(("scene", "view"), None, None),
        P(),
        P(("scene", "view"), None, None),
        P(("scene", "view"), None, None),
        P(("scene", "view"), None),
        P(("scene", "view"), None),
        P(),
        P(),
    )
    out_specs = P(("scene", "view"), None, None)
    return jax.shard_map(body, mesh=mesh, in_specs=in_specs, out_specs=out_specs, check_vma=False)
```

```python
import functools

import jax
import jax.numpy as jnp
from jax import lax
from jax.experimental import pallas as pl
from jax.experimental.pallas import tpu as pltpu
from jax.sharding import PartitionSpec as P

GROUPS = 8
DEPTH = 64
TROWS = 4


def with_halo(block, sides, width):
    for axis, dim in sides:
        count = lax.axis_size(axis)
        forward = [(i, i + 1) for i in range(count - 1)]
        backward = [(target, source) for source, target in forward]
        low = lax.ppermute(
            lax.slice_in_dim(block, block.shape[dim] - width, None, axis=dim), axis, forward
        )
        high = lax.ppermute(lax.slice_in_dim(block, 0, width, axis=dim), axis, backward)
        block = jnp.concatenate([low, block, high], axis=dim)
    return block


def convolve_full(padded, kernel):
    rows_out = padded.shape[0] - 2
    depth_len = padded.shape[2]
    columns = padded.shape[3]
    framed = jnp.pad(padded, ((0, 0), (0, 0), (1, 1), (1, 1)))
    carried = jnp.zeros((rows_out, kernel.shape[-1], depth_len, columns), jnp.float32)
    for depth_off in range(3):
        for row_off in range(3):
            for col_off in range(3):
                window = framed[
                    row_off : row_off + rows_out,
                    :,
                    depth_off : depth_off + depth_len,
                    col_off : col_off + columns,
                ]
                carried = carried + jnp.einsum(
                    "rcdw,ce->redw",
                    window,
                    kernel[depth_off, row_off, col_off],
                    preferred_element_type=jnp.float32,
                )
    return carried


def convolve_final(padded, kernel):
    rows_out = padded.shape[0] - 2
    depth_len = padded.shape[2]
    columns = padded.shape[3]
    framed = jnp.pad(padded, ((0, 0), (0, 0), (1, 1), (1, 1)))
    carried = jnp.zeros((rows_out, depth_len, columns), jnp.float32)
    for depth_off in range(3):
        for row_off in range(3):
            for col_off in range(3):
                window = framed[
                    row_off : row_off + rows_out,
                    :,
                    depth_off : depth_off + depth_len,
                    col_off : col_off + columns,
                ]
                carried = carried + jnp.einsum(
                    "rcdw,c->rdw",
                    window,
                    kernel[depth_off, row_off, col_off],
                    preferred_element_type=jnp.float32,
                )
    return carried


def correlate_kernel(blk_ref, blocks_ref, table_ref, ref_ref, out_ref, arranged, products):
    chunk = 8
    slots = table_ref.shape[0] // blocks_ref.shape[2]
    width = blocks_ref.shape[2]
    channels = blocks_ref.shape[1]
    units = out_ref.shape[0] // GROUPS
    cap = units // ref_ref.shape[0]
    group_size = channels // GROUPS
    rows = chunk * channels

    def step(c, carry):
        for u in range(chunk):
            unit = c * chunk + u
            for w in range(slots):
                arranged[u * channels : (u + 1) * channels, w * width : (w + 1) * width] = blocks_ref[
                    blk_ref[unit * slots + w]
                ]
        warped = jnp.dot(arranged[...], table_ref[...], preferred_element_type=jnp.float32)
        warped = warped.astype(jnp.bfloat16).astype(jnp.float32)
        lanes = products.shape[0]
        for u in range(chunk):
            unit = c * chunk + u
            tile = ref_ref[unit // cap].astype(jnp.float32)
            for j in range(lanes):
                products[j, u * channels : (u + 1) * channels, :] = (
                    warped[u * channels : (u + 1) * channels, j * 128 : (j + 1) * 128]
                    * tile[:, j * 128 : (j + 1) * 128]
                )
        start = pl.multiple_of(c * (chunk * GROUPS), chunk * GROUPS)
        for j in range(lanes):
            total = products[j, pl.ds(0, rows // group_size, stride=group_size), :]
            for k in range(1, group_size):
                total = total + products[j, pl.ds(k, rows // group_size, stride=group_size), :]
            out_ref[pl.ds(start, chunk * GROUPS), j * 128 : (j + 1) * 128] = (
                total * (GROUPS / channels)
            ).astype(out_ref.dtype)
        return carry

    lax.fori_loop(0, units // chunk, step, 0)


def correlate(blk, blocks, table, refs, units):
    channels, width = blocks.shape[1], blocks.shape[2]
    tpix = table.shape[1]
    chunk = 8
    return pl.pallas_call(
        correlate_kernel,
        out_shape=jax.ShapeDtypeStruct((units * GROUPS, tpix), jnp.bfloat16),
        in_specs=[
            pl.BlockSpec(memory_space=pltpu.SMEM),
            pl.BlockSpec(memory_space=pltpu.VMEM),
            pl.BlockSpec(memory_space=pltpu.VMEM),
            pl.BlockSpec(memory_space=pltpu.VMEM),
        ],
        out_specs=pl.BlockSpec(memory_space=pltpu.VMEM),
        scratch_shapes=[
            pltpu.VMEM((chunk * channels, table.shape[0]), jnp.bfloat16),
            pltpu.VMEM((tpix // 128, chunk * channels, 128), jnp.float32),
        ],
    )(blk, blocks, table, refs)


def conv_kernel(x_ref, m_ref, out_ref, *, relu, rows, cols, groups, chunk):
    width = rows * cols
    outs = m_ref.shape[2]
    depth = x_ref.shape[0] // groups - 2
    lane = lax.broadcasted_iota(jnp.int32, (outs, width), 1) % cols
    for k in range(depth // chunk):
        acc = None
        for e in range(3):
            y = None
            for b in range(3):
                window = x_ref[k * chunk * groups : (k * chunk + chunk + 2) * groups, b * cols : b * cols + width]
                part = jnp.dot(m_ref[e, b], window, preferred_element_type=jnp.float32)
                y = part if y is None else y + part
            if e == 0:
                y = jnp.where(lane >= 1, pltpu.roll(y, 1, 1), 0.0)
            elif e == 2:
                y = jnp.where(lane <= cols - 2, pltpu.roll(y, width - 1, 1), 0.0)
            acc = y if acc is None else acc + y
        if relu:
            out_ref[(k * chunk + 1) * outs // chunk : (k * chunk + chunk + 1) * outs // chunk, :] = (
                jnp.maximum(acc, 0.0).astype(out_ref.dtype)
            )
        else:
            for r in range(rows):
                out_ref[r, k * chunk : (k + 1) * chunk, :] = acc[:, r * cols : (r + 1) * cols]
    if relu:
        pad = jnp.zeros((outs // chunk, width), out_ref.dtype)
        out_ref[: outs // chunk, :] = pad
        out_ref[out_ref.shape[0] - outs // chunk :, :] = pad


def banded(kernel, chunk):
    shift = (
        jnp.arange(chunk)[None, :, None] + jnp.arange(3)[:, None, None]
        == jnp.arange(chunk + 2)[None, None, :]
    ).astype(kernel.dtype)
    if kernel.ndim == 5:
        mats = jnp.einsum("abeio,adz->ebdozi", kernel, shift, preferred_element_type=jnp.float32)
        outs = chunk * kernel.shape[4]
    else:
        mats = jnp.einsum("abei,adz->ebdzi", kernel, shift, preferred_element_type=jnp.float32)
        outs = chunk
    return mats.astype(kernel.dtype).reshape(3, 3, outs, -1)


def conv_rows(framed, mats, relu, rows, cols, chunk):
    outs = mats.shape[2]
    groups = mats.shape[3] // (chunk + 2)
    depth = framed.shape[0] // groups - 2
    if relu:
        out_shape = jax.ShapeDtypeStruct(((depth + 2) * outs // chunk, rows * cols), jnp.bfloat16)
    else:
        out_shape = jax.ShapeDtypeStruct((rows, depth, cols), jnp.float32)
    return pl.pallas_call(
        functools.partial(conv_kernel, relu=relu, rows=rows, cols=cols, groups=groups, chunk=chunk),
        out_shape=out_shape,
        in_specs=[pl.BlockSpec(memory_space=pltpu.VMEM), pl.BlockSpec(memory_space=pltpu.VMEM)],
        out_specs=pl.BlockSpec(memory_space=pltpu.VMEM),
    )(framed, mats)


def halo_cols(block, cols):
    count = lax.axis_size("view")
    forward = [(i, i + 1) for i in range(count - 1)]
    backward = [(target, source) for source, target in forward]
    low = lax.ppermute(block[:, block.shape[1] - cols :], "view", forward)
    high = lax.ppermute(block[:, :cols], "view", backward)
    return jnp.concatenate([low, block, high], axis=1)


def pad_rows(volume):
    return with_halo(volume, (("view", 0),), 1)


def body(
    src_feat,
    ref_feat,
    weight_table,
    src_block,
    table_index,
    block_count,
    depth_plane,
    kern_one,
    kern_two,
):
    owners = lax.axis_size("view")
    features = src_feat[0]
    channels, spix = features.shape
    slots, block_width, tpix = weight_table.shape
    blocks = features.reshape(channels, spix // block_width, block_width).transpose(1, 0, 2)
    units = src_block.shape[1]
    cap = units // owners
    counts = block_count[0]
    nblocks = spix // block_width
    blocks = jnp.concatenate([blocks, jnp.zeros_like(blocks[:1])], axis=0)
    matches = table_index[0][:, :, None] == jnp.arange(slots)[None, None, :]
    live = (jnp.arange(slots)[None, :] < counts[:, None])[:, :, None] & matches
    picked = jnp.sum(jnp.where(matches, src_block[0][:, :, None], 0), axis=1)
    alive = jnp.any(live, axis=1)
    blk = jnp.where(alive, picked, nblocks).reshape(-1).astype(jnp.int32)
    depth_code = jnp.where(counts > 0, depth_plane[0], -1).astype(jnp.bfloat16)

    ref_all = lax.all_to_all(
        jnp.broadcast_to(ref_feat, (owners,) + ref_feat.shape[1:]),
        "view",
        split_axis=0,
        concat_axis=0,
        tiled=True,
    )
    corr_all = correlate(
        blk, blocks, weight_table.reshape(slots * block_width, tpix), ref_all, units
    ).reshape(units, GROUPS * tpix)
    tag_lanes = jnp.broadcast_to(depth_code[:, None], (units, 128))
    payload = jnp.concatenate([corr_all, tag_lanes], axis=1)
    arriving = lax.all_to_all(
        payload.reshape(owners, cap, GROUPS * tpix + 128),
        "view",
        split_axis=0,
        concat_axis=0,
        tiled=True,
    ).reshape(owners * cap, GROUPS * tpix + 128)
    received = arriving[:, : GROUPS * tpix]
    depth_tags = arriving[:, GROUPS * tpix]
    onehot = (
        depth_tags[None, :] == jnp.arange(DEPTH).astype(jnp.bfloat16)[:, None]
    ).astype(jnp.bfloat16)
    summed = jnp.dot(onehot, received, preferred_element_type=jnp.float32)
    tallies = jnp.sum(onehot.astype(jnp.float32), axis=1)
    cost_volume = (summed / jnp.maximum(tallies, 1.0)[:, None]).astype(jnp.bfloat16)
    columns = tpix // TROWS
    volume = cost_volume.reshape(DEPTH * GROUPS, TROWS * columns)
    volume = jnp.pad(volume, ((GROUPS, GROUPS), (0, 0)))
    hidden = conv_rows(
        halo_cols(volume, columns), banded(kern_one, DEPTH // 4), True, TROWS, columns, DEPTH // 4
    )
    scores = conv_rows(
        halo_cols(hidden, columns), banded(kern_two, DEPTH), False, TROWS, columns, DEPTH
    )
    return scores


def solution(mesh):
    in_specs = (
        P(("scene", "view"), None, None),
        P(("scene", "view"), None, None),
        P(),
        P(("scene", "view"), None, None),
        P(("scene", "view"), None, None),
        P(("scene", "view"), None),
        P(("scene", "view"), None),
        P(),
        P(),
    )
    out_specs = P(("scene", "view"), None, None)
    return jax.shard_map(body, mesh=mesh, in_specs=in_specs, out_specs=out_specs, check_vma=False)
```

```python
import functools

import jax
import jax.numpy as jnp
from jax import lax
from jax.experimental import pallas as pl
from jax.experimental.pallas import tpu as pltpu
from jax.sharding import PartitionSpec as P

GROUPS = 8
DEPTH = 64
TROWS = 4


def with_halo(block, sides, width):
    for axis, dim in sides:
        count = lax.axis_size(axis)
        forward = [(i, i + 1) for i in range(count - 1)]
        backward = [(target, source) for source, target in forward]
        low = lax.ppermute(
            lax.slice_in_dim(block, block.shape[dim] - width, None, axis=dim), axis, forward
        )
        high = lax.ppermute(lax.slice_in_dim(block, 0, width, axis=dim), axis, backward)
        block = jnp.concatenate([low, block, high], axis=dim)
    return block


def convolve_full(padded, kernel):
    rows_out = padded.shape[0] - 2
    depth_len = padded.shape[2]
    columns = padded.shape[3]
    framed = jnp.pad(padded, ((0, 0), (0, 0), (1, 1), (1, 1)))
    carried = jnp.zeros((rows_out, kernel.shape[-1], depth_len, columns), jnp.float32)
    for depth_off in range(3):
        for row_off in range(3):
            for col_off in range(3):
                window = framed[
                    row_off : row_off + rows_out,
                    :,
                    depth_off : depth_off + depth_len,
                    col_off : col_off + columns,
                ]
                carried = carried + jnp.einsum(
                    "rcdw,ce->redw",
                    window,
                    kernel[depth_off, row_off, col_off],
                    preferred_element_type=jnp.float32,
                )
    return carried


def convolve_final(padded, kernel):
    rows_out = padded.shape[0] - 2
    depth_len = padded.shape[2]
    columns = padded.shape[3]
    framed = jnp.pad(padded, ((0, 0), (0, 0), (1, 1), (1, 1)))
    carried = jnp.zeros((rows_out, depth_len, columns), jnp.float32)
    for depth_off in range(3):
        for row_off in range(3):
            for col_off in range(3):
                window = framed[
                    row_off : row_off + rows_out,
                    :,
                    depth_off : depth_off + depth_len,
                    col_off : col_off + columns,
                ]
                carried = carried + jnp.einsum(
                    "rcdw,c->rdw",
                    window,
                    kernel[depth_off, row_off, col_off],
                    preferred_element_type=jnp.float32,
                )
    return carried


def correlate_kernel(blk_ref, blocks_ref, table_ref, ref_ref, out_ref, arranged, products):
    chunk = 8
    slots = table_ref.shape[0] // blocks_ref.shape[2]
    width = blocks_ref.shape[2]
    channels = blocks_ref.shape[1]
    units = out_ref.shape[0] // GROUPS
    cap = units // ref_ref.shape[0]
    group_size = channels // GROUPS
    rows = chunk * channels

    def step(c, carry):
        for u in range(chunk):
            unit = c * chunk + u
            for w in range(slots):
                arranged[u * channels : (u + 1) * channels, w * width : (w + 1) * width] = blocks_ref[
                    blk_ref[unit * slots + w]
                ]
        warped = jnp.dot(arranged[...], table_ref[...], preferred_element_type=jnp.float32)
        warped = warped.astype(jnp.bfloat16).astype(jnp.float32)
        lanes = products.shape[0]
        for u in range(chunk):
            unit = c * chunk + u
            tile = ref_ref[unit // cap].astype(jnp.float32)
            for j in range(lanes):
                products[j, u * channels : (u + 1) * channels, :] = (
                    warped[u * channels : (u + 1) * channels, j * 128 : (j + 1) * 128]
                    * tile[:, j * 128 : (j + 1) * 128]
                )
        start = pl.multiple_of(c * (chunk * GROUPS), chunk * GROUPS)
        for j in range(lanes):
            total = products[j, pl.ds(0, rows // group_size, stride=group_size), :]
            for k in range(1, group_size):
                total = total + products[j, pl.ds(k, rows // group_size, stride=group_size), :]
            out_ref[pl.ds(start, chunk * GROUPS), j * 128 : (j + 1) * 128] = (
                total * (GROUPS / channels)
            ).astype(out_ref.dtype)
        return carry

    lax.fori_loop(0, units // chunk, step, 0)


def correlate(blk, blocks, table, refs, units):
    channels, width = blocks.shape[1], blocks.shape[2]
    tpix = table.shape[1]
    chunk = 8
    return pl.pallas_call(
        correlate_kernel,
        out_shape=jax.ShapeDtypeStruct((units * GROUPS, tpix), jnp.bfloat16),
        in_specs=[
            pl.BlockSpec(memory_space=pltpu.SMEM),
            pl.BlockSpec(memory_space=pltpu.VMEM),
            pl.BlockSpec(memory_space=pltpu.VMEM),
            pl.BlockSpec(memory_space=pltpu.VMEM),
        ],
        out_specs=pl.BlockSpec(memory_space=pltpu.VMEM),
        scratch_shapes=[
            pltpu.VMEM((chunk * channels, table.shape[0]), jnp.bfloat16),
            pltpu.VMEM((tpix // 128, chunk * channels, 128), jnp.float32),
        ],
    )(blk, blocks, table, refs)


def conv_kernel(x_ref, m_ref, out_ref, *, relu, rows, cols, groups, chunk):
    width = rows * cols
    outs = m_ref.shape[2]
    depth = x_ref.shape[0] // groups - 2
    lane = lax.broadcasted_iota(jnp.int32, (outs, width), 1) % cols
    for k in range(depth // chunk):
        acc = None
        for e in range(3):
            y = None
            for b in range(3):
                window = x_ref[k * chunk * groups : (k * chunk + chunk + 2) * groups, b * cols : b * cols + width]
                part = jnp.dot(m_ref[b, e], window, preferred_element_type=jnp.float32)
                y = part if y is None else y + part
            if e == 0:
                y = jnp.where(lane >= 1, pltpu.roll(y, 1, 1), 0.0)
            elif e == 2:
                y = jnp.where(lane <= cols - 2, pltpu.roll(y, width - 1, 1), 0.0)
            acc = y if acc is None else acc + y
        if relu:
            out_ref[(k * chunk + 1) * outs // chunk : (k * chunk + chunk + 1) * outs // chunk, :] = (
                jnp.maximum(acc, 0.0).astype(out_ref.dtype)
            )
        else:
            for r in range(rows):
                out_ref[r, k * chunk : (k + 1) * chunk, :] = acc[:, r * cols : (r + 1) * cols]
    if relu:
        pad = jnp.zeros((outs // chunk, width), out_ref.dtype)
        out_ref[: outs // chunk, :] = pad
        out_ref[out_ref.shape[0] - outs // chunk :, :] = pad


def banded(kernel, chunk):
    groups = kernel.shape[3]
    cols = (chunk + 2) * groups
    taps = kernel.reshape((3, 9) + kernel.shape[3:])
    col = lax.iota(jnp.int32, cols)
    spread = (col[None, :] % groups == jnp.arange(groups)[:, None]).astype(kernel.dtype)
    if kernel.ndim == 5:
        outs = kernel.shape[4]
        rows = chunk * outs
        row = lax.iota(jnp.int32, rows)
        pick = (row[:, None] % outs == jnp.arange(outs)[None, :]).astype(kernel.dtype)
        lanes = jnp.einsum("xyio,ic->xyoc", taps, spread, preferred_element_type=jnp.float32)
        tiles = jnp.einsum(
            "ro,xyoc->xyrc", pick, lanes.astype(kernel.dtype), preferred_element_type=jnp.float32
        )
        depth_of_row = row // outs
    else:
        rows = chunk
        lanes = jnp.einsum("xyi,ic->xyc", taps, spread, preferred_element_type=jnp.float32)
        tiles = lanes[:, :, None, :]
        depth_of_row = lax.iota(jnp.int32, rows)
    band = col[None, None, :] // groups == depth_of_row[None, :, None] + jnp.arange(3)[:, None, None]
    mats = jnp.sum(jnp.where(band[:, None], tiles, 0.0), axis=0)
    return mats.astype(kernel.dtype).reshape(3, 3, rows, cols)


def conv_rows(framed, mats, relu, rows, cols, chunk):
    outs = mats.shape[2]
    groups = mats.shape[3] // (chunk + 2)
    depth = framed.shape[0] // groups - 2
    if relu:
        out_shape = jax.ShapeDtypeStruct(((depth + 2) * outs // chunk, rows * cols), jnp.bfloat16)
    else:
        out_shape = jax.ShapeDtypeStruct((rows, depth, cols), jnp.float32)
    return pl.pallas_call(
        functools.partial(conv_kernel, relu=relu, rows=rows, cols=cols, groups=groups, chunk=chunk),
        out_shape=out_shape,
        in_specs=[pl.BlockSpec(memory_space=pltpu.VMEM), pl.BlockSpec(memory_space=pltpu.VMEM)],
        out_specs=pl.BlockSpec(memory_space=pltpu.VMEM),
    )(framed, mats)


def halo_cols(block, cols):
    count = lax.axis_size("view")
    forward = [(i, i + 1) for i in range(count - 1)]
    backward = [(target, source) for source, target in forward]
    low = lax.ppermute(block[:, block.shape[1] - cols :], "view", forward)
    high = lax.ppermute(block[:, :cols], "view", backward)
    return jnp.concatenate([low, block, high], axis=1)


def pad_rows(volume):
    return with_halo(volume, (("view", 0),), 1)


def body(
    src_feat,
    ref_feat,
    weight_table,
    src_block,
    table_index,
    block_count,
    depth_plane,
    kern_one,
    kern_two,
):
    owners = lax.axis_size("view")
    features = src_feat[0]
    channels, spix = features.shape
    slots, block_width, tpix = weight_table.shape
    blocks = features.reshape(channels, spix // block_width, block_width).transpose(1, 0, 2)
    units = src_block.shape[1]
    cap = units // owners
    counts = block_count[0]
    nblocks = spix // block_width
    blocks = jnp.concatenate([blocks, jnp.zeros_like(blocks[:1])], axis=0)
    matches = table_index[0][:, :, None] == jnp.arange(slots)[None, None, :]
    live = (jnp.arange(slots)[None, :] < counts[:, None])[:, :, None] & matches
    picked = jnp.sum(jnp.where(matches, src_block[0][:, :, None], 0), axis=1)
    alive = jnp.any(live, axis=1)
    blk = jnp.where(alive, picked, nblocks).reshape(-1).astype(jnp.int32)
    depth_code = jnp.where(counts > 0, depth_plane[0], -1).astype(jnp.bfloat16)

    ref_all = lax.all_to_all(
        jnp.broadcast_to(ref_feat, (owners,) + ref_feat.shape[1:]),
        "view",
        split_axis=0,
        concat_axis=0,
        tiled=True,
    )
    corr_all = correlate(
        blk, blocks, weight_table.reshape(slots * block_width, tpix), ref_all, units
    ).reshape(units, GROUPS * tpix)
    tag_lanes = jnp.broadcast_to(depth_code[:, None], (units, 128))
    payload = jnp.concatenate([corr_all, tag_lanes], axis=1)
    arriving = lax.all_to_all(
        payload.reshape(owners, cap, GROUPS * tpix + 128),
        "view",
        split_axis=0,
        concat_axis=0,
        tiled=True,
    ).reshape(owners * cap, GROUPS * tpix + 128)
    received = arriving[:, : GROUPS * tpix]
    depth_tags = arriving[:, GROUPS * tpix]
    onehot = (
        depth_tags[None, :] == jnp.arange(DEPTH).astype(jnp.bfloat16)[:, None]
    ).astype(jnp.bfloat16)
    summed = jnp.dot(onehot, received, preferred_element_type=jnp.float32)
    tallies = jnp.sum(onehot.astype(jnp.float32), axis=1)
    cost_volume = (summed / jnp.maximum(tallies, 1.0)[:, None]).astype(jnp.bfloat16)
    columns = tpix // TROWS
    volume = cost_volume.reshape(DEPTH * GROUPS, TROWS * columns)
    volume = jnp.pad(volume, ((GROUPS, GROUPS), (0, 0)))
    hidden = conv_rows(
        halo_cols(volume, columns), banded(kern_one, DEPTH // 4), True, TROWS, columns, DEPTH // 4
    )
    scores = conv_rows(
        halo_cols(hidden, columns), banded(kern_two, DEPTH), False, TROWS, columns, DEPTH
    )
    return scores


def solution(mesh):
    in_specs = (
        P(("scene", "view"), None, None),
        P(("scene", "view"), None, None),
        P(),
        P(("scene", "view"), None, None),
        P(("scene", "view"), None, None),
        P(("scene", "view"), None),
        P(("scene", "view"), None),
        P(),
        P(),
    )
    out_specs = P(("scene", "view"), None, None)
    return jax.shard_map(body, mesh=mesh, in_specs=in_specs, out_specs=out_specs, check_vma=False)
```

```python
import functools

import jax
import jax.numpy as jnp
from jax import lax
from jax.experimental import pallas as pl
from jax.experimental.pallas import tpu as pltpu
from jax.sharding import PartitionSpec as P

GROUPS = 8
DEPTH = 64
TROWS = 4


def with_halo(block, sides, width):
    for axis, dim in sides:
        count = lax.axis_size(axis)
        forward = [(i, i + 1) for i in range(count - 1)]
        backward = [(target, source) for source, target in forward]
        low = lax.ppermute(
            lax.slice_in_dim(block, block.shape[dim] - width, None, axis=dim), axis, forward
        )
        high = lax.ppermute(lax.slice_in_dim(block, 0, width, axis=dim), axis, backward)
        block = jnp.concatenate([low, block, high], axis=dim)
    return block


def convolve_full(padded, kernel):
    rows_out = padded.shape[0] - 2
    depth_len = padded.shape[2]
    columns = padded.shape[3]
    framed = jnp.pad(padded, ((0, 0), (0, 0), (1, 1), (1, 1)))
    carried = jnp.zeros((rows_out, kernel.shape[-1], depth_len, columns), jnp.float32)
    for depth_off in range(3):
        for row_off in range(3):
            for col_off in range(3):
                window = framed[
                    row_off : row_off + rows_out,
                    :,
                    depth_off : depth_off + depth_len,
                    col_off : col_off + columns,
                ]
                carried = carried + jnp.einsum(
                    "rcdw,ce->redw",
                    window,
                    kernel[depth_off, row_off, col_off],
                    preferred_element_type=jnp.float32,
                )
    return carried


def convolve_final(padded, kernel):
    rows_out = padded.shape[0] - 2
    depth_len = padded.shape[2]
    columns = padded.shape[3]
    framed = jnp.pad(padded, ((0, 0), (0, 0), (1, 1), (1, 1)))
    carried = jnp.zeros((rows_out, depth_len, columns), jnp.float32)
    for depth_off in range(3):
        for row_off in range(3):
            for col_off in range(3):
                window = framed[
                    row_off : row_off + rows_out,
                    :,
                    depth_off : depth_off + depth_len,
                    col_off : col_off + columns,
                ]
                carried = carried + jnp.einsum(
                    "rcdw,c->rdw",
                    window,
                    kernel[depth_off, row_off, col_off],
                    preferred_element_type=jnp.float32,
                )
    return carried


def correlate_kernel(blk_ref, blocks_ref, table_ref, ref_ref, out_ref, arranged, products):
    chunk = 8
    slots = table_ref.shape[0] // blocks_ref.shape[2]
    width = blocks_ref.shape[2]
    channels = blocks_ref.shape[1]
    units = out_ref.shape[0] // GROUPS
    cap = units // ref_ref.shape[0]
    group_size = channels // GROUPS
    rows = chunk * channels

    def step(c, carry):
        for u in range(chunk):
            unit = c * chunk + u
            for w in range(slots):
                arranged[u * channels : (u + 1) * channels, w * width : (w + 1) * width] = blocks_ref[
                    blk_ref[unit * slots + w]
                ]
        warped = jnp.dot(arranged[...], table_ref[...], preferred_element_type=jnp.float32)
        warped = warped.astype(jnp.bfloat16).astype(jnp.float32)
        lanes = products.shape[0]
        for u in range(chunk):
            unit = c * chunk + u
            tile = ref_ref[unit // cap].astype(jnp.float32)
            for j in range(lanes):
                products[j, u * channels : (u + 1) * channels, :] = (
                    warped[u * channels : (u + 1) * channels, j * 128 : (j + 1) * 128]
                    * tile[:, j * 128 : (j + 1) * 128]
                )
        start = pl.multiple_of(c * (chunk * GROUPS), chunk * GROUPS)
        for j in range(lanes):
            total = products[j, pl.ds(0, rows // group_size, stride=group_size), :]
            for k in range(1, group_size):
                total = total + products[j, pl.ds(k, rows // group_size, stride=group_size), :]
            out_ref[pl.ds(start, chunk * GROUPS), j * 128 : (j + 1) * 128] = (
                total * (GROUPS / channels)
            ).astype(out_ref.dtype)
        return carry

    lax.fori_loop(0, units // chunk, step, 0)


def correlate(blk, blocks, table, refs, units):
    channels, width = blocks.shape[1], blocks.shape[2]
    tpix = table.shape[1]
    chunk = 8
    return pl.pallas_call(
        correlate_kernel,
        out_shape=jax.ShapeDtypeStruct((units * GROUPS, tpix), jnp.bfloat16),
        in_specs=[
            pl.BlockSpec(memory_space=pltpu.SMEM),
            pl.BlockSpec(memory_space=pltpu.VMEM),
            pl.BlockSpec(memory_space=pltpu.VMEM),
            pl.BlockSpec(memory_space=pltpu.VMEM),
        ],
        out_specs=pl.BlockSpec(memory_space=pltpu.VMEM),
        scratch_shapes=[
            pltpu.VMEM((chunk * channels, table.shape[0]), jnp.bfloat16),
            pltpu.VMEM((tpix // 128, chunk * channels, 128), jnp.float32),
        ],
    )(blk, blocks, table, refs)


def conv_kernel(x_ref, m_ref, out_ref, *, relu, rows, cols, groups, chunk):
    width = rows * cols
    outs = m_ref.shape[2]
    depth = x_ref.shape[0] // groups - 2
    lane = lax.broadcasted_iota(jnp.int32, (outs, width), 1) % cols
    for k in range(depth // chunk):
        acc = None
        for e in range(3):
            y = None
            for b in range(3):
                window = x_ref[k * chunk * groups : (k * chunk + chunk + 2) * groups, b * cols : b * cols + width]
                part = jnp.dot(m_ref[b, e], window, preferred_element_type=jnp.float32)
                y = part if y is None else y + part
            if e == 0:
                y = jnp.where(lane >= 1, pltpu.roll(y, 1, 1), 0.0)
            elif e == 2:
                y = jnp.where(lane <= cols - 2, pltpu.roll(y, width - 1, 1), 0.0)
            acc = y if acc is None else acc + y
        if relu:
            out_ref[(k * chunk + 1) * outs // chunk : (k * chunk + chunk + 1) * outs // chunk, :] = (
                jnp.maximum(acc, 0.0).astype(out_ref.dtype)
            )
        else:
            for r in range(rows):
                out_ref[r, k * chunk : (k + 1) * chunk, :] = acc[:, r * cols : (r + 1) * cols]
    if relu:
        pad = jnp.zeros((outs // chunk, width), out_ref.dtype)
        out_ref[: outs // chunk, :] = pad
        out_ref[out_ref.shape[0] - outs // chunk :, :] = pad


def banded(kernel, chunk):
    groups = kernel.shape[3]
    cols = (chunk + 2) * groups
    taps = kernel.reshape((3, 9) + kernel.shape[3:])
    col = lax.iota(jnp.int32, cols)
    spread = (col[None, :] % groups == jnp.arange(groups)[:, None]).astype(kernel.dtype)
    if kernel.ndim == 5:
        outs = kernel.shape[4]
        rows = chunk * outs
        row = lax.iota(jnp.int32, rows)
        pick = (row[:, None] % outs == jnp.arange(outs)[None, :]).astype(kernel.dtype)
        lanes = jnp.einsum("xyio,ic->xyoc", taps, spread, preferred_element_type=jnp.float32)
        tiles = jnp.einsum(
            "ro,xyoc->xyrc", pick, lanes.astype(kernel.dtype), preferred_element_type=jnp.float32
        )
        depth_of_row = row // outs
    else:
        rows = chunk
        lanes = jnp.einsum("xyi,ic->xyc", taps, spread, preferred_element_type=jnp.float32)
        tiles = lanes[:, :, None, :]
        depth_of_row = lax.iota(jnp.int32, rows)
    band = col[None, None, :] // groups == depth_of_row[None, :, None] + jnp.arange(3)[:, None, None]
    mats = jnp.sum(jnp.where(band[:, None], tiles, 0.0), axis=0)
    return mats.astype(kernel.dtype).reshape(3, 3, rows, cols)


def conv_rows(framed, mats, relu, rows, cols, chunk):
    outs = mats.shape[2]
    groups = mats.shape[3] // (chunk + 2)
    depth = framed.shape[0] // groups - 2
    if relu:
        out_shape = jax.ShapeDtypeStruct(((depth + 2) * outs // chunk, rows * cols), jnp.bfloat16)
    else:
        out_shape = jax.ShapeDtypeStruct((rows, depth, cols), jnp.float32)
    return pl.pallas_call(
        functools.partial(conv_kernel, relu=relu, rows=rows, cols=cols, groups=groups, chunk=chunk),
        out_shape=out_shape,
        in_specs=[pl.BlockSpec(memory_space=pltpu.VMEM), pl.BlockSpec(memory_space=pltpu.VMEM)],
        out_specs=pl.BlockSpec(memory_space=pltpu.VMEM),
    )(framed, mats)


def halo_cols(block, cols):
    count = lax.axis_size("view")
    forward = [(i, i + 1) for i in range(count - 1)]
    backward = [(target, source) for source, target in forward]
    low = lax.ppermute(block[:, block.shape[1] - cols :], "view", forward)
    high = lax.ppermute(block[:, :cols], "view", backward)
    return jnp.concatenate([low, block, high], axis=1)


def gather_view(block):
    count = lax.axis_size("view")
    if count & (count - 1):
        return lax.all_to_all(
            jnp.broadcast_to(block, (count,) + block.shape[1:]), "view", 0, 0, tiled=True
        )
    index = lax.axis_index("view")
    gathered = block[0]
    level = 0
    stride = count // 2
    while stride >= 1:
        other = lax.ppermute(gathered, "view", [(i, i ^ stride) for i in range(count)])
        low = (index // stride) % 2 == 0
        gathered = jnp.where(
            low, jnp.stack([gathered, other], axis=level), jnp.stack([other, gathered], axis=level)
        )
        level += 1
        stride //= 2
    return gathered.reshape((count,) + block.shape[1:])


def pad_rows(volume):
    return with_halo(volume, (("view", 0),), 1)


def body(
    src_feat,
    ref_feat,
    weight_table,
    src_block,
    table_index,
    block_count,
    depth_plane,
    kern_one,
    kern_two,
):
    owners = lax.axis_size("view")
    features = src_feat[0]
    channels, spix = features.shape
    slots, block_width, tpix = weight_table.shape
    blocks = features.reshape(channels, spix // block_width, block_width).transpose(1, 0, 2)
    units = src_block.shape[1]
    cap = units // owners
    counts = block_count[0]
    nblocks = spix // block_width
    blocks = jnp.concatenate([blocks, jnp.zeros_like(blocks[:1])], axis=0)
    matches = table_index[0][:, :, None] == jnp.arange(slots)[None, None, :]
    live = (jnp.arange(slots)[None, :] < counts[:, None])[:, :, None] & matches
    picked = jnp.sum(jnp.where(matches, src_block[0][:, :, None], 0), axis=1)
    alive = jnp.any(live, axis=1)
    blk = jnp.where(alive, picked, nblocks).reshape(-1).astype(jnp.int32)
    depth_code = jnp.where(counts > 0, depth_plane[0], -1).astype(jnp.bfloat16)

    ref_all = gather_view(ref_feat)
    corr_all = correlate(
        blk, blocks, weight_table.reshape(slots * block_width, tpix), ref_all, units
    ).reshape(units, GROUPS * tpix)
    tag_lanes = jnp.broadcast_to(depth_code[:, None], (units, 128))
    payload = jnp.concatenate([corr_all, tag_lanes], axis=1)
    arriving = lax.all_to_all(
        payload.reshape(owners, cap, GROUPS * tpix + 128),
        "view",
        split_axis=0,
        concat_axis=0,
        tiled=True,
    ).reshape(owners * cap, GROUPS * tpix + 128)
    received = arriving[:, : GROUPS * tpix]
    depth_tags = arriving[:, GROUPS * tpix]
    onehot = (
        depth_tags[None, :] == jnp.arange(DEPTH).astype(jnp.bfloat16)[:, None]
    ).astype(jnp.bfloat16)
    summed = jnp.dot(onehot, received, preferred_element_type=jnp.float32)
    tallies = jnp.sum(onehot.astype(jnp.float32), axis=1)
    cost_volume = (summed / jnp.maximum(tallies, 1.0)[:, None]).astype(jnp.bfloat16)
    columns = tpix // TROWS
    volume = cost_volume.reshape(DEPTH * GROUPS, TROWS * columns)
    volume = jnp.pad(volume, ((GROUPS, GROUPS), (0, 0)))
    hidden = conv_rows(
        halo_cols(volume, columns), banded(kern_one, DEPTH // 4), True, TROWS, columns, DEPTH // 4
    )
    scores = conv_rows(
        halo_cols(hidden, columns), banded(kern_two, DEPTH), False, TROWS, columns, DEPTH
    )
    return scores


def solution(mesh):
    in_specs = (
        P(("scene", "view"), None, None),
        P(("scene", "view"), None, None),
        P(),
        P(("scene", "view"), None, None),
        P(("scene", "view"), None, None),
        P(("scene", "view"), None),
        P(("scene", "view"), None),
        P(),
        P(),
    )
    out_specs = P(("scene", "view"), None, None)
    return jax.shard_map(body, mesh=mesh, in_specs=in_specs, out_specs=out_specs, check_vma=False)
```

```python
import functools

import jax
import jax.numpy as jnp
from jax import lax
from jax.experimental import pallas as pl
from jax.experimental.pallas import tpu as pltpu
from jax.sharding import PartitionSpec as P

GROUPS = 8
DEPTH = 64
TROWS = 4


def with_halo(block, sides, width):
    for axis, dim in sides:
        count = lax.axis_size(axis)
        forward = [(i, i + 1) for i in range(count - 1)]
        backward = [(target, source) for source, target in forward]
        low = lax.ppermute(
            lax.slice_in_dim(block, block.shape[dim] - width, None, axis=dim), axis, forward
        )
        high = lax.ppermute(lax.slice_in_dim(block, 0, width, axis=dim), axis, backward)
        block = jnp.concatenate([low, block, high], axis=dim)
    return block


def convolve_full(padded, kernel):
    rows_out = padded.shape[0] - 2
    depth_len = padded.shape[2]
    columns = padded.shape[3]
    framed = jnp.pad(padded, ((0, 0), (0, 0), (1, 1), (1, 1)))
    carried = jnp.zeros((rows_out, kernel.shape[-1], depth_len, columns), jnp.float32)
    for depth_off in range(3):
        for row_off in range(3):
            for col_off in range(3):
                window = framed[
                    row_off : row_off + rows_out,
                    :,
                    depth_off : depth_off + depth_len,
                    col_off : col_off + columns,
                ]
                carried = carried + jnp.einsum(
                    "rcdw,ce->redw",
                    window,
                    kernel[depth_off, row_off, col_off],
                    preferred_element_type=jnp.float32,
                )
    return carried


def convolve_final(padded, kernel):
    rows_out = padded.shape[0] - 2
    depth_len = padded.shape[2]
    columns = padded.shape[3]
    framed = jnp.pad(padded, ((0, 0), (0, 0), (1, 1), (1, 1)))
    carried = jnp.zeros((rows_out, depth_len, columns), jnp.float32)
    for depth_off in range(3):
        for row_off in range(3):
            for col_off in range(3):
                window = framed[
                    row_off : row_off + rows_out,
                    :,
                    depth_off : depth_off + depth_len,
                    col_off : col_off + columns,
                ]
                carried = carried + jnp.einsum(
                    "rcdw,c->rdw",
                    window,
                    kernel[depth_off, row_off, col_off],
                    preferred_element_type=jnp.float32,
                )
    return carried


def correlate_kernel(blk_ref, blocks_ref, table_ref, ref_ref, out_ref, arranged, products):
    chunk = 8
    slots = table_ref.shape[0] // blocks_ref.shape[2]
    width = blocks_ref.shape[2]
    channels = blocks_ref.shape[1]
    units = out_ref.shape[0] // GROUPS
    cap = units // ref_ref.shape[0]
    group_size = channels // GROUPS
    rows = chunk * channels

    def step(c, carry):
        for u in range(chunk):
            unit = c * chunk + u
            for w in range(slots):
                arranged[u * channels : (u + 1) * channels, w * width : (w + 1) * width] = blocks_ref[
                    blk_ref[unit * slots + w]
                ]
        warped = jnp.dot(arranged[...], table_ref[...], preferred_element_type=jnp.float32)
        warped = warped.astype(jnp.bfloat16).astype(jnp.float32)
        lanes = products.shape[0]
        for u in range(chunk):
            unit = c * chunk + u
            tile = ref_ref[unit // cap].astype(jnp.float32)
            for j in range(lanes):
                products[j, u * channels : (u + 1) * channels, :] = (
                    warped[u * channels : (u + 1) * channels, j * 128 : (j + 1) * 128]
                    * tile[:, j * 128 : (j + 1) * 128]
                )
        start = pl.multiple_of(c * (chunk * GROUPS), chunk * GROUPS)
        for j in range(lanes):
            total = products[j, pl.ds(0, rows // group_size, stride=group_size), :]
            for k in range(1, group_size):
                total = total + products[j, pl.ds(k, rows // group_size, stride=group_size), :]
            out_ref[pl.ds(start, chunk * GROUPS), j * 128 : (j + 1) * 128] = (
                total * (GROUPS / channels)
            ).astype(out_ref.dtype)
        return carry

    lax.fori_loop(0, units // chunk, step, 0)


def correlate(blk, blocks, table, refs, units):
    channels, width = blocks.shape[1], blocks.shape[2]
    tpix = table.shape[1]
    chunk = 8
    return pl.pallas_call(
        correlate_kernel,
        out_shape=jax.ShapeDtypeStruct((units * GROUPS, tpix), jnp.bfloat16),
        in_specs=[
            pl.BlockSpec(memory_space=pltpu.SMEM),
            pl.BlockSpec(memory_space=pltpu.VMEM),
            pl.BlockSpec(memory_space=pltpu.VMEM),
            pl.BlockSpec(memory_space=pltpu.VMEM),
        ],
        out_specs=pl.BlockSpec(memory_space=pltpu.VMEM),
        scratch_shapes=[
            pltpu.VMEM((chunk * channels, table.shape[0]), jnp.bfloat16),
            pltpu.VMEM((tpix // 128, chunk * channels, 128), jnp.float32),
        ],
    )(blk, blocks, table, refs)


def conv_kernel(*refs, relu, rows, cols, groups, chunk):
    if relu:
        ends_ref, x_ref, m_ref, out_ref = refs
    else:
        x_ref, m_ref, out_ref = refs
    width = rows * cols
    outs = m_ref.shape[2]
    depth = x_ref.shape[0] // groups - 2
    lane = lax.broadcasted_iota(jnp.int32, (outs, width), 1) % cols
    for k in range(depth // chunk):
        acc = None
        for e in range(3):
            y = None
            for b in range(3):
                window = x_ref[k * chunk * groups : (k * chunk + chunk + 2) * groups, b * cols : b * cols + width]
                part = jnp.dot(m_ref[b, e], window, preferred_element_type=jnp.float32)
                y = part if y is None else y + part
            if e == 0:
                y = jnp.where(lane >= 1, pltpu.roll(y, 1, 1), 0.0)
            elif e == 2:
                y = jnp.where(lane <= cols - 2, pltpu.roll(y, width - 1, 1), 0.0)
            acc = y if acc is None else acc + y
        if relu:
            block = lax.broadcasted_iota(jnp.int32, (outs, width), 1) // cols
            outside = ((block == 0) & (ends_ref[0] > 0)) | ((block == rows - 1) & (ends_ref[1] > 0))
            acc = jnp.where(outside, 0.0, acc)
            out_ref[(k * chunk + 1) * outs // chunk : (k * chunk + chunk + 1) * outs // chunk, :] = (
                jnp.maximum(acc, 0.0).astype(out_ref.dtype)
            )
        else:
            for r in range(rows):
                out_ref[r, k * chunk : (k + 1) * chunk, :] = acc[:, r * cols : (r + 1) * cols]
    if relu:
        pad = jnp.zeros((outs // chunk, width), out_ref.dtype)
        out_ref[: outs // chunk, :] = pad
        out_ref[out_ref.shape[0] - outs // chunk :, :] = pad


def banded(kernel, chunk):
    groups = kernel.shape[3]
    cols = (chunk + 2) * groups
    taps = kernel.reshape((3, 9) + kernel.shape[3:])
    col = lax.iota(jnp.int32, cols)
    spread = (col[None, :] % groups == jnp.arange(groups)[:, None]).astype(kernel.dtype)
    if kernel.ndim == 5:
        outs = kernel.shape[4]
        rows = chunk * outs
        row = lax.iota(jnp.int32, rows)
        pick = (row[:, None] % outs == jnp.arange(outs)[None, :]).astype(kernel.dtype)
        lanes = jnp.einsum("xyio,ic->xyoc", taps, spread, preferred_element_type=jnp.float32)
        tiles = jnp.einsum(
            "ro,xyoc->xyrc", pick, lanes.astype(kernel.dtype), preferred_element_type=jnp.float32
        )
        depth_of_row = row // outs
    else:
        rows = chunk
        lanes = jnp.einsum("xyi,ic->xyc", taps, spread, preferred_element_type=jnp.float32)
        tiles = lanes[:, :, None, :]
        depth_of_row = lax.iota(jnp.int32, rows)
    band = col[None, None, :] // groups == depth_of_row[None, :, None] + jnp.arange(3)[:, None, None]
    mats = jnp.sum(jnp.where(band[:, None], tiles, 0.0), axis=0)
    return mats.astype(kernel.dtype).reshape(3, 3, rows, cols)


def conv_rows(framed, mats, relu, rows, cols, chunk, ends=None):
    outs = mats.shape[2]
    groups = mats.shape[3] // (chunk + 2)
    depth = framed.shape[0] // groups - 2
    if relu:
        out_shape = jax.ShapeDtypeStruct(((depth + 2) * outs // chunk, rows * cols), jnp.bfloat16)
    else:
        out_shape = jax.ShapeDtypeStruct((rows, depth, cols), jnp.float32)
    operands = (framed, mats) if ends is None else (ends, framed, mats)
    in_specs = [pl.BlockSpec(memory_space=pltpu.VMEM), pl.BlockSpec(memory_space=pltpu.VMEM)]
    if ends is not None:
        in_specs = [pl.BlockSpec(memory_space=pltpu.SMEM)] + in_specs
    return pl.pallas_call(
        functools.partial(conv_kernel, relu=relu, rows=rows, cols=cols, groups=groups, chunk=chunk),
        out_shape=out_shape,
        in_specs=in_specs,
        out_specs=pl.BlockSpec(memory_space=pltpu.VMEM),
    )(*operands)


def halo_cols(block, cols):
    count = lax.axis_size("view")
    forward = [(i, i + 1) for i in range(count - 1)]
    backward = [(target, source) for source, target in forward]
    low = lax.ppermute(block[:, block.shape[1] - cols :], "view", forward)
    high = lax.ppermute(block[:, :cols], "view", backward)
    return jnp.concatenate([low, block, high], axis=1)


def gather_view(block):
    count = lax.axis_size("view")
    if count & (count - 1):
        return lax.all_to_all(
            jnp.broadcast_to(block, (count,) + block.shape[1:]), "view", 0, 0, tiled=True
        )
    index = lax.axis_index("view")
    gathered = block[0]
    level = 0
    stride = count // 2
    while stride >= 1:
        other = lax.ppermute(gathered, "view", [(i, i ^ stride) for i in range(count)])
        low = (index // stride) % 2 == 0
        gathered = jnp.where(
            low, jnp.stack([gathered, other], axis=level), jnp.stack([other, gathered], axis=level)
        )
        level += 1
        stride //= 2
    return gathered.reshape((count,) + block.shape[1:])


def pad_rows(volume):
    return with_halo(volume, (("view", 0),), 1)


def body(
    src_feat,
    ref_feat,
    weight_table,
    src_block,
    table_index,
    block_count,
    depth_plane,
    kern_one,
    kern_two,
):
    owners = lax.axis_size("view")
    features = src_feat[0]
    channels, spix = features.shape
    slots, block_width, tpix = weight_table.shape
    blocks = features.reshape(channels, spix // block_width, block_width).transpose(1, 0, 2)
    units = src_block.shape[1]
    cap = units // owners
    counts = block_count[0]
    nblocks = spix // block_width
    blocks = jnp.concatenate([blocks, jnp.zeros_like(blocks[:1])], axis=0)
    matches = table_index[0][:, :, None] == jnp.arange(slots)[None, None, :]
    live = (jnp.arange(slots)[None, :] < counts[:, None])[:, :, None] & matches
    picked = jnp.sum(jnp.where(matches, src_block[0][:, :, None], 0), axis=1)
    alive = jnp.any(live, axis=1)
    blk = jnp.where(alive, picked, nblocks).reshape(-1).astype(jnp.int32)
    depth_code = jnp.where(counts > 0, depth_plane[0], -1).astype(jnp.bfloat16)

    ref_all = gather_view(ref_feat)
    corr_all = correlate(
        blk, blocks, weight_table.reshape(slots * block_width, tpix), ref_all, units
    ).reshape(units, GROUPS * tpix)
    tag_lanes = jnp.broadcast_to(depth_code[:, None], (units, 128))
    payload = jnp.concatenate([corr_all, tag_lanes], axis=1)
    arriving = lax.all_to_all(
        payload.reshape(owners, cap, GROUPS * tpix + 128),
        "view",
        split_axis=0,
        concat_axis=0,
        tiled=True,
    ).reshape(owners * cap, GROUPS * tpix + 128)
    received = arriving[:, : GROUPS * tpix]
    depth_tags = arriving[:, GROUPS * tpix]
    onehot = (
        depth_tags[None, :] == jnp.arange(DEPTH).astype(jnp.bfloat16)[:, None]
    ).astype(jnp.bfloat16)
    summed = jnp.dot(onehot, received, preferred_element_type=jnp.float32)
    tallies = jnp.sum(onehot.astype(jnp.float32), axis=1)
    cost_volume = (summed / jnp.maximum(tallies, 1.0)[:, None]).astype(jnp.bfloat16)
    columns = tpix // TROWS
    volume = cost_volume.reshape(DEPTH * GROUPS, TROWS * columns)
    volume = jnp.pad(volume, ((GROUPS, GROUPS), (0, 0)))
    count = lax.axis_size("view")
    place = lax.axis_index("view")
    ends = jnp.stack([place == 0, place == count - 1]).astype(jnp.int32)
    hidden = conv_rows(
        halo_cols(volume, 2 * columns),
        banded(kern_one, DEPTH // 4),
        True,
        TROWS + 2,
        columns,
        DEPTH // 4,
        ends,
    )
    scores = conv_rows(hidden, banded(kern_two, DEPTH), False, TROWS, columns, DEPTH)
    return scores


def solution(mesh):
    in_specs = (
        P(("scene", "view"), None, None),
        P(("scene", "view"), None, None),
        P(),
        P(("scene", "view"), None, None),
        P(("scene", "view"), None, None),
        P(("scene", "view"), None),
        P(("scene", "view"), None),
        P(),
        P(),
    )
    out_specs = P(("scene", "view"), None, None)
    return jax.shard_map(body, mesh=mesh, in_specs=in_specs, out_specs=out_specs, check_vma=False)
```

```python
import functools

import jax
import jax.numpy as jnp
from jax import lax
from jax.experimental import pallas as pl
from jax.experimental.pallas import tpu as pltpu
from jax.sharding import PartitionSpec as P

GROUPS = 8
DEPTH = 64
TROWS = 4


def with_halo(block, sides, width):
    for axis, dim in sides:
        count = lax.axis_size(axis)
        forward = [(i, i + 1) for i in range(count - 1)]
        backward = [(target, source) for source, target in forward]
        low = lax.ppermute(
            lax.slice_in_dim(block, block.shape[dim] - width, None, axis=dim), axis, forward
        )
        high = lax.ppermute(lax.slice_in_dim(block, 0, width, axis=dim), axis, backward)
        block = jnp.concatenate([low, block, high], axis=dim)
    return block


def convolve_full(padded, kernel):
    rows_out = padded.shape[0] - 2
    depth_len = padded.shape[2]
    columns = padded.shape[3]
    framed = jnp.pad(padded, ((0, 0), (0, 0), (1, 1), (1, 1)))
    carried = jnp.zeros((rows_out, kernel.shape[-1], depth_len, columns), jnp.float32)
    for depth_off in range(3):
        for row_off in range(3):
            for col_off in range(3):
                window = framed[
                    row_off : row_off + rows_out,
                    :,
                    depth_off : depth_off + depth_len,
                    col_off : col_off + columns,
                ]
                carried = carried + jnp.einsum(
                    "rcdw,ce->redw",
                    window,
                    kernel[depth_off, row_off, col_off],
                    preferred_element_type=jnp.float32,
                )
    return carried


def convolve_final(padded, kernel):
    rows_out = padded.shape[0] - 2
    depth_len = padded.shape[2]
    columns = padded.shape[3]
    framed = jnp.pad(padded, ((0, 0), (0, 0), (1, 1), (1, 1)))
    carried = jnp.zeros((rows_out, depth_len, columns), jnp.float32)
    for depth_off in range(3):
        for row_off in range(3):
            for col_off in range(3):
                window = framed[
                    row_off : row_off + rows_out,
                    :,
                    depth_off : depth_off + depth_len,
                    col_off : col_off + columns,
                ]
                carried = carried + jnp.einsum(
                    "rcdw,c->rdw",
                    window,
                    kernel[depth_off, row_off, col_off],
                    preferred_element_type=jnp.float32,
                )
    return carried


def correlate_kernel(blk_ref, tag_ref, blocks_ref, table_ref, ref_ref, out_ref, arranged, products):
    chunk = 8
    slots = table_ref.shape[0] // blocks_ref.shape[2]
    width = blocks_ref.shape[2]
    channels = blocks_ref.shape[1]
    units = out_ref.shape[0]
    tpix = table_ref.shape[1]
    cap = units // ref_ref.shape[0]
    group_size = channels // GROUPS

    def step(c, carry):
        for u in range(chunk):
            unit = c * chunk + u
            for w in range(slots):
                arranged[u * channels : (u + 1) * channels, w * width : (w + 1) * width] = blocks_ref[
                    blk_ref[unit * slots + w]
                ]
        warped = jnp.dot(arranged[...], table_ref[...], preferred_element_type=jnp.float32)
        warped = warped.astype(jnp.bfloat16).astype(jnp.float32)
        lanes = products.shape[0]
        for u in range(chunk):
            unit = c * chunk + u
            tile = ref_ref[unit // cap].astype(jnp.float32)
            for j in range(lanes):
                products[j, u * channels : (u + 1) * channels, :] = (
                    warped[u * channels : (u + 1) * channels, j * 128 : (j + 1) * 128]
                    * tile[:, j * 128 : (j + 1) * 128]
                )
        start = pl.multiple_of(c * chunk, chunk)
        for g in range(GROUPS):
            for j in range(lanes):
                total = products[j, pl.ds(g * group_size, chunk, stride=channels), :]
                for k in range(1, group_size):
                    total = total + products[j, pl.ds(g * group_size + k, chunk, stride=channels), :]
                out_ref[pl.ds(start, chunk), g * tpix + j * 128 : g * tpix + (j + 1) * 128] = (
                    total * (GROUPS / channels)
                ).astype(out_ref.dtype)
        tags = jnp.concatenate(
            [jnp.full((1, 128), tag_ref[c * chunk + u], jnp.int32) for u in range(chunk)], axis=0
        )
        out_ref[pl.ds(start, chunk), GROUPS * tpix :] = tags.astype(jnp.float32).astype(out_ref.dtype)
        return carry

    lax.fori_loop(0, units // chunk, step, 0)


def correlate(blk, tags, blocks, table, refs, units):
    channels = blocks.shape[1]
    tpix = table.shape[1]
    chunk = 8
    return pl.pallas_call(
        correlate_kernel,
        out_shape=jax.ShapeDtypeStruct((units, GROUPS * tpix + 128), jnp.bfloat16),
        in_specs=[
            pl.BlockSpec(memory_space=pltpu.SMEM),
            pl.BlockSpec(memory_space=pltpu.SMEM),
            pl.BlockSpec(memory_space=pltpu.VMEM),
            pl.BlockSpec(memory_space=pltpu.VMEM),
            pl.BlockSpec(memory_space=pltpu.VMEM),
        ],
        out_specs=pl.BlockSpec(memory_space=pltpu.VMEM),
        scratch_shapes=[
            pltpu.VMEM((chunk * channels, table.shape[0]), jnp.bfloat16),
            pltpu.VMEM((tpix // 128, chunk * channels, 128), jnp.float32),
        ],
    )(blk, tags, blocks, table, refs)


def conv_kernel(*refs, relu, rows, cols, groups, chunk):
    if relu:
        ends_ref, x_ref, m_ref, out_ref = refs
    else:
        x_ref, m_ref, out_ref = refs
    width = rows * cols
    outs = m_ref.shape[2]
    depth = x_ref.shape[0] // groups - 2
    lane = lax.broadcasted_iota(jnp.int32, (outs, width), 1) % cols
    for k in range(depth // chunk):
        acc = None
        for e in range(3):
            y = None
            for b in range(3):
                window = x_ref[k * chunk * groups : (k * chunk + chunk + 2) * groups, b * cols : b * cols + width]
                part = jnp.dot(m_ref[b, e], window, preferred_element_type=jnp.float32)
                y = part if y is None else y + part
            if e == 0:
                y = jnp.where(lane >= 1, pltpu.roll(y, 1, 1), 0.0)
            elif e == 2:
                y = jnp.where(lane <= cols - 2, pltpu.roll(y, width - 1, 1), 0.0)
            acc = y if acc is None else acc + y
        if relu:
            block = lax.broadcasted_iota(jnp.int32, (outs, width), 1) // cols
            outside = ((block == 0) & (ends_ref[0] > 0)) | ((block == rows - 1) & (ends_ref[1] > 0))
            acc = jnp.where(outside, 0.0, acc)
            out_ref[(k * chunk + 1) * outs // chunk : (k * chunk + chunk + 1) * outs // chunk, :] = (
                jnp.maximum(acc, 0.0).astype(out_ref.dtype)
            )
        else:
            for r in range(rows):
                out_ref[r, k * chunk : (k + 1) * chunk, :] = acc[:, r * cols : (r + 1) * cols]
    if relu:
        pad = jnp.zeros((outs // chunk, width), out_ref.dtype)
        out_ref[: outs // chunk, :] = pad
        out_ref[out_ref.shape[0] - outs // chunk :, :] = pad


def banded(kernel, chunk):
    groups = kernel.shape[3]
    cols = (chunk + 2) * groups
    taps = kernel.reshape((3, 9) + kernel.shape[3:])
    col = lax.iota(jnp.int32, cols)
    spread = (col[None, :] % groups == jnp.arange(groups)[:, None]).astype(kernel.dtype)
    if kernel.ndim == 5:
        outs = kernel.shape[4]
        rows = chunk * outs
        row = lax.iota(jnp.int32, rows)
        pick = (row[:, None] % outs == jnp.arange(outs)[None, :]).astype(kernel.dtype)
        lanes = jnp.einsum("xyio,ic->xyoc", taps, spread, preferred_element_type=jnp.float32)
        tiles = jnp.einsum(
            "ro,xyoc->xyrc", pick, lanes.astype(kernel.dtype), preferred_element_type=jnp.float32
        )
        depth_of_row = row // outs
    else:
        rows = chunk
        lanes = jnp.einsum("xyi,ic->xyc", taps, spread, preferred_element_type=jnp.float32)
        tiles = lanes[:, :, None, :]
        depth_of_row = lax.iota(jnp.int32, rows)
    band = col[None, None, :] // groups == depth_of_row[None, :, None] + jnp.arange(3)[:, None, None]
    mats = jnp.sum(jnp.where(band[:, None], tiles, 0.0), axis=0)
    return mats.astype(kernel.dtype).reshape(3, 3, rows, cols)


def conv_rows(framed, mats, relu, rows, cols, chunk, ends=None):
    outs = mats.shape[2]
    groups = mats.shape[3] // (chunk + 2)
    depth = framed.shape[0] // groups - 2
    if relu:
        out_shape = jax.ShapeDtypeStruct(((depth + 2) * outs // chunk, rows * cols), jnp.bfloat16)
    else:
        out_shape = jax.ShapeDtypeStruct((rows, depth, cols), jnp.float32)
    operands = (framed, mats) if ends is None else (ends, framed, mats)
    in_specs = [pl.BlockSpec(memory_space=pltpu.VMEM), pl.BlockSpec(memory_space=pltpu.VMEM)]
    if ends is not None:
        in_specs = [pl.BlockSpec(memory_space=pltpu.SMEM)] + in_specs
    return pl.pallas_call(
        functools.partial(conv_kernel, relu=relu, rows=rows, cols=cols, groups=groups, chunk=chunk),
        out_shape=out_shape,
        in_specs=in_specs,
        out_specs=pl.BlockSpec(memory_space=pltpu.VMEM),
    )(*operands)


def halo_cols(block, cols):
    count = lax.axis_size("view")
    forward = [(i, i + 1) for i in range(count - 1)]
    backward = [(target, source) for source, target in forward]
    low = lax.ppermute(block[:, block.shape[1] - cols :], "view", forward)
    high = lax.ppermute(block[:, :cols], "view", backward)
    return jnp.concatenate([low, block, high], axis=1)


def gather_view(block):
    count = lax.axis_size("view")
    if count & (count - 1):
        return lax.all_to_all(
            jnp.broadcast_to(block, (count,) + block.shape[1:]), "view", 0, 0, tiled=True
        )
    index = lax.axis_index("view")
    gathered = block[0]
    level = 0
    stride = count // 2
    while stride >= 1:
        other = lax.ppermute(gathered, "view", [(i, i ^ stride) for i in range(count)])
        low = (index // stride) % 2 == 0
        gathered = jnp.where(
            low, jnp.stack([gathered, other], axis=level), jnp.stack([other, gathered], axis=level)
        )
        level += 1
        stride //= 2
    return gathered.reshape((count,) + block.shape[1:])


def pad_rows(volume):
    return with_halo(volume, (("view", 0),), 1)


def body(
    src_feat,
    ref_feat,
    weight_table,
    src_block,
    table_index,
    block_count,
    depth_plane,
    kern_one,
    kern_two,
):
    owners = lax.axis_size("view")
    features = src_feat[0]
    channels, spix = features.shape
    slots, block_width, tpix = weight_table.shape
    blocks = features.reshape(channels, spix // block_width, block_width).transpose(1, 0, 2)
    units = src_block.shape[1]
    cap = units // owners
    counts = block_count[0]
    nblocks = spix // block_width
    blocks = jnp.concatenate([blocks, jnp.zeros_like(blocks[:1])], axis=0)
    matches = table_index[0][:, :, None] == jnp.arange(slots)[None, None, :]
    live = (jnp.arange(slots)[None, :] < counts[:, None])[:, :, None] & matches
    picked = jnp.sum(jnp.where(matches, src_block[0][:, :, None], 0), axis=1)
    alive = jnp.any(live, axis=1)
    blk = jnp.where(alive, picked, nblocks).reshape(-1).astype(jnp.int32)
    depth_code = jnp.where(counts > 0, depth_plane[0], -1).astype(jnp.int32)

    ref_all = gather_view(ref_feat)
    payload = correlate(
        blk, depth_code, blocks, weight_table.reshape(slots * block_width, tpix), ref_all, units
    )
    arriving = lax.all_to_all(
        payload.reshape(owners, cap, GROUPS * tpix + 128),
        "view",
        split_axis=0,
        concat_axis=0,
        tiled=True,
    ).reshape(owners * cap, GROUPS * tpix + 128)
    received = arriving[:, : GROUPS * tpix]
    depth_tags = arriving[:, GROUPS * tpix]
    onehot = (
        depth_tags[None, :] == jnp.arange(DEPTH).astype(jnp.bfloat16)[:, None]
    ).astype(jnp.bfloat16)
    summed = jnp.dot(onehot, received, preferred_element_type=jnp.float32)
    tallies = jnp.sum(onehot.astype(jnp.float32), axis=1)
    cost_volume = (summed / jnp.maximum(tallies, 1.0)[:, None]).astype(jnp.bfloat16)
    columns = tpix // TROWS
    volume = cost_volume.reshape(DEPTH * GROUPS, TROWS * columns)
    volume = jnp.pad(volume, ((GROUPS, GROUPS), (0, 0)))
    count = lax.axis_size("view")
    place = lax.axis_index("view")
    ends = jnp.stack([place == 0, place == count - 1]).astype(jnp.int32)
    hidden = conv_rows(
        halo_cols(volume, 2 * columns),
        banded(kern_one, DEPTH // 4),
        True,
        TROWS + 2,
        columns,
        DEPTH // 4,
        ends,
    )
    scores = conv_rows(hidden, banded(kern_two, DEPTH), False, TROWS, columns, DEPTH)
    return scores


def solution(mesh):
    in_specs = (
        P(("scene", "view"), None, None),
        P(("scene", "view"), None, None),
        P(),
        P(("scene", "view"), None, None),
        P(("scene", "view"), None, None),
        P(("scene", "view"), None),
        P(("scene", "view"), None),
        P(),
        P(),
    )
    out_specs = P(("scene", "view"), None, None)
    return jax.shard_map(body, mesh=mesh, in_specs=in_specs, out_specs=out_specs, check_vma=False)
```

```python
import functools

import jax
import jax.numpy as jnp
from jax import lax
from jax.experimental import pallas as pl
from jax.experimental.pallas import tpu as pltpu
from jax.sharding import PartitionSpec as P

GROUPS = 8
DEPTH = 64
TROWS = 4


def with_halo(block, sides, width):
    for axis, dim in sides:
        count = lax.axis_size(axis)
        forward = [(i, i + 1) for i in range(count - 1)]
        backward = [(target, source) for source, target in forward]
        low = lax.ppermute(
            lax.slice_in_dim(block, block.shape[dim] - width, None, axis=dim), axis, forward
        )
        high = lax.ppermute(lax.slice_in_dim(block, 0, width, axis=dim), axis, backward)
        block = jnp.concatenate([low, block, high], axis=dim)
    return block


def convolve_full(padded, kernel):
    rows_out = padded.shape[0] - 2
    depth_len = padded.shape[2]
    columns = padded.shape[3]
    framed = jnp.pad(padded, ((0, 0), (0, 0), (1, 1), (1, 1)))
    carried = jnp.zeros((rows_out, kernel.shape[-1], depth_len, columns), jnp.float32)
    for depth_off in range(3):
        for row_off in range(3):
            for col_off in range(3):
                window = framed[
                    row_off : row_off + rows_out,
                    :,
                    depth_off : depth_off + depth_len,
                    col_off : col_off + columns,
                ]
                carried = carried + jnp.einsum(
                    "rcdw,ce->redw",
                    window,
                    kernel[depth_off, row_off, col_off],
                    preferred_element_type=jnp.float32,
                )
    return carried


def convolve_final(padded, kernel):
    rows_out = padded.shape[0] - 2
    depth_len = padded.shape[2]
    columns = padded.shape[3]
    framed = jnp.pad(padded, ((0, 0), (0, 0), (1, 1), (1, 1)))
    carried = jnp.zeros((rows_out, depth_len, columns), jnp.float32)
    for depth_off in range(3):
        for row_off in range(3):
            for col_off in range(3):
                window = framed[
                    row_off : row_off + rows_out,
                    :,
                    depth_off : depth_off + depth_len,
                    col_off : col_off + columns,
                ]
                carried = carried + jnp.einsum(
                    "rcdw,c->rdw",
                    window,
                    kernel[depth_off, row_off, col_off],
                    preferred_element_type=jnp.float32,
                )
    return carried


def correlate_kernel(blk_ref, blocks_ref, table_ref, ref_ref, out_ref, arranged, products):
    chunk = 8
    slots = table_ref.shape[0] // blocks_ref.shape[2]
    width = blocks_ref.shape[2]
    channels = blocks_ref.shape[1]
    units = out_ref.shape[0] // GROUPS
    cap = units // ref_ref.shape[0]
    group_size = channels // GROUPS
    rows = chunk * channels

    def step(c, carry):
        for u in range(chunk):
            unit = c * chunk + u
            for w in range(slots):
                arranged[u * channels : (u + 1) * channels, w * width : (w + 1) * width] = blocks_ref[
                    blk_ref[unit * slots + w]
                ]
        warped = jnp.dot(arranged[...], table_ref[...], preferred_element_type=jnp.float32)
        warped = warped.astype(jnp.bfloat16).astype(jnp.float32)
        lanes = products.shape[0]
        for u in range(chunk):
            unit = c * chunk + u
            tile = ref_ref[unit // cap].astype(jnp.float32)
            for j in range(lanes):
                products[j, u * channels : (u + 1) * channels, :] = (
                    warped[u * channels : (u + 1) * channels, j * 128 : (j + 1) * 128]
                    * tile[:, j * 128 : (j + 1) * 128]
                )
        start = pl.multiple_of(c * (chunk * GROUPS), chunk * GROUPS)
        for j in range(lanes):
            total = products[j, pl.ds(0, rows // group_size, stride=group_size), :]
            for k in range(1, group_size):
                total = total + products[j, pl.ds(k, rows // group_size, stride=group_size), :]
            out_ref[pl.ds(start, chunk * GROUPS), j * 128 : (j + 1) * 128] = (
                total * (GROUPS / channels)
            ).astype(out_ref.dtype)
        return carry

    lax.fori_loop(0, units // chunk, step, 0)


def correlate(blk, blocks, table, refs, units):
    channels, width = blocks.shape[1], blocks.shape[2]
    tpix = table.shape[1]
    chunk = 8
    return pl.pallas_call(
        correlate_kernel,
        out_shape=jax.ShapeDtypeStruct((units * GROUPS, tpix), jnp.bfloat16),
        in_specs=[
            pl.BlockSpec(memory_space=pltpu.SMEM),
            pl.BlockSpec(memory_space=pltpu.VMEM),
            pl.BlockSpec(memory_space=pltpu.VMEM),
            pl.BlockSpec(memory_space=pltpu.VMEM),
        ],
        out_specs=pl.BlockSpec(memory_space=pltpu.VMEM),
        scratch_shapes=[
            pltpu.VMEM((chunk * channels, table.shape[0]), jnp.bfloat16),
            pltpu.VMEM((tpix // 128, chunk * channels, 128), jnp.float32),
        ],
    )(blk, blocks, table, refs)


def conv_kernel(*refs, relu, rows, cols, groups, chunk):
    if relu:
        ends_ref, x_ref, m_ref, out_ref = refs
    else:
        x_ref, m_ref, out_ref = refs
    width = rows * cols
    outs = m_ref.shape[2]
    depth = x_ref.shape[0] // groups - 2
    lane = lax.broadcasted_iota(jnp.int32, (outs, width), 1) % cols
    for k in range(depth // chunk):
        acc = None
        for e in range(3):
            y = None
            for b in range(3):
                window = x_ref[k * chunk * groups : (k * chunk + chunk + 2) * groups, b * cols : b * cols + width]
                part = jnp.dot(m_ref[b, e], window, preferred_element_type=jnp.float32)
                y = part if y is None else y + part
            if e == 0:
                y = jnp.where(lane >= 1, pltpu.roll(y, 1, 1), 0.0)
            elif e == 2:
                y = jnp.where(lane <= cols - 2, pltpu.roll(y, width - 1, 1), 0.0)
            acc = y if acc is None else acc + y
        if relu:
            block = lax.broadcasted_iota(jnp.int32, (outs, width), 1) // cols
            outside = ((block == 0) & (ends_ref[0] > 0)) | ((block == rows - 1) & (ends_ref[1] > 0))
            acc = jnp.where(outside, 0.0, acc)
            out_ref[(k * chunk + 1) * outs // chunk : (k * chunk + chunk + 1) * outs // chunk, :] = (
                jnp.maximum(acc, 0.0).astype(out_ref.dtype)
            )
        else:
            for r in range(rows):
                out_ref[r, k * chunk : (k + 1) * chunk, :] = acc[:, r * cols : (r + 1) * cols]
    if relu:
        pad = jnp.zeros((outs // chunk, width), out_ref.dtype)
        out_ref[: outs // chunk, :] = pad
        out_ref[out_ref.shape[0] - outs // chunk :, :] = pad


def banded(kernel, chunk):
    groups = kernel.shape[3]
    cols = (chunk + 2) * groups
    taps = kernel.reshape((3, 9) + kernel.shape[3:])
    col = lax.iota(jnp.int32, cols)
    spread = (col[None, :] % groups == jnp.arange(groups)[:, None]).astype(kernel.dtype)
    if kernel.ndim == 5:
        outs = kernel.shape[4]
        rows = chunk * outs
        row = lax.iota(jnp.int32, rows)
        pick = (row[:, None] % outs == jnp.arange(outs)[None, :]).astype(kernel.dtype)
        lanes = jnp.einsum("xyio,ic->xyoc", taps, spread, preferred_element_type=jnp.float32)
        tiles = jnp.einsum(
            "ro,xyoc->xyrc", pick, lanes.astype(kernel.dtype), preferred_element_type=jnp.float32
        )
        depth_of_row = row // outs
    else:
        rows = chunk
        lanes = jnp.einsum("xyi,ic->xyc", taps, spread, preferred_element_type=jnp.float32)
        tiles = lanes[:, :, None, :]
        depth_of_row = lax.iota(jnp.int32, rows)
    band = col[None, None, :] // groups == depth_of_row[None, :, None] + jnp.arange(3)[:, None, None]
    mats = jnp.sum(jnp.where(band[:, None], tiles, 0.0), axis=0)
    return mats.astype(kernel.dtype).reshape(3, 3, rows, cols)


def conv_rows(framed, mats, relu, rows, cols, chunk, ends=None):
    outs = mats.shape[2]
    groups = mats.shape[3] // (chunk + 2)
    depth = framed.shape[0] // groups - 2
    if relu:
        out_shape = jax.ShapeDtypeStruct(((depth + 2) * outs // chunk, rows * cols), jnp.bfloat16)
    else:
        out_shape = jax.ShapeDtypeStruct((rows, depth, cols), jnp.float32)
    operands = (framed, mats) if ends is None else (ends, framed, mats)
    in_specs = [pl.BlockSpec(memory_space=pltpu.VMEM), pl.BlockSpec(memory_space=pltpu.VMEM)]
    if ends is not None:
        in_specs = [pl.BlockSpec(memory_space=pltpu.SMEM)] + in_specs
    return pl.pallas_call(
        functools.partial(conv_kernel, relu=relu, rows=rows, cols=cols, groups=groups, chunk=chunk),
        out_shape=out_shape,
        in_specs=in_specs,
        out_specs=pl.BlockSpec(memory_space=pltpu.VMEM),
    )(*operands)


def halo_cols(block, cols):
    count = lax.axis_size("view")
    forward = [(i, i + 1) for i in range(count - 1)]
    backward = [(target, source) for source, target in forward]
    low = lax.ppermute(block[:, block.shape[1] - cols :], "view", forward)
    high = lax.ppermute(block[:, :cols], "view", backward)
    return jnp.concatenate([low, block, high], axis=1)


def gather_view(block):
    count = lax.axis_size("view")
    if count & (count - 1):
        return lax.all_to_all(
            jnp.broadcast_to(block, (count,) + block.shape[1:]), "view", 0, 0, tiled=True
        )
    index = lax.axis_index("view")
    gathered = block[0]
    stride = 1
    while stride < count:
        other = lax.ppermute(gathered, "view", [(i, i ^ stride) for i in range(count)])
        low = (index // stride) % 2 == 0
        gathered = jnp.where(low, jnp.stack([gathered, other]), jnp.stack([other, gathered]))
        stride *= 2
    return gathered.reshape((count,) + block.shape[1:])


def pad_rows(volume):
    return with_halo(volume, (("view", 0),), 1)


def body(
    src_feat,
    ref_feat,
    weight_table,
    src_block,
    table_index,
    block_count,
    depth_plane,
    kern_one,
    kern_two,
):
    owners = lax.axis_size("view")
    features = src_feat[0]
    channels, spix = features.shape
    slots, block_width, tpix = weight_table.shape
    blocks = features.reshape(channels, spix // block_width, block_width).transpose(1, 0, 2)
    units = src_block.shape[1]
    cap = units // owners
    counts = block_count[0]
    nblocks = spix // block_width
    blocks = jnp.concatenate([blocks, jnp.zeros_like(blocks[:1])], axis=0)
    matches = table_index[0][:, :, None] == jnp.arange(slots)[None, None, :]
    live = (jnp.arange(slots)[None, :] < counts[:, None])[:, :, None] & matches
    picked = jnp.sum(jnp.where(matches, src_block[0][:, :, None], 0), axis=1)
    alive = jnp.any(live, axis=1)
    blk = jnp.where(alive, picked, nblocks).reshape(-1).astype(jnp.int32)
    depth_code = jnp.where(counts > 0, depth_plane[0], -1).astype(jnp.bfloat16)

    ref_all = gather_view(ref_feat)
    corr_all = correlate(
        blk, blocks, weight_table.reshape(slots * block_width, tpix), ref_all, units
    ).reshape(units, GROUPS * tpix)
    tag_lanes = jnp.broadcast_to(depth_code[:, None], (units, 128))
    payload = jnp.concatenate([corr_all, tag_lanes], axis=1)
    arriving = lax.all_to_all(
        payload.reshape(owners, cap, GROUPS * tpix + 128),
        "view",
        split_axis=0,
        concat_axis=0,
        tiled=True,
    ).reshape(owners * cap, GROUPS * tpix + 128)
    received = arriving[:, : GROUPS * tpix]
    depth_tags = arriving[:, GROUPS * tpix]
    onehot = (
        depth_tags[None, :] == jnp.arange(DEPTH).astype(jnp.bfloat16)[:, None]
    ).astype(jnp.bfloat16)
    summed = jnp.dot(onehot, received, preferred_element_type=jnp.float32)
    tallies = jnp.sum(onehot.astype(jnp.float32), axis=1)
    cost_volume = (summed / jnp.maximum(tallies, 1.0)[:, None]).astype(jnp.bfloat16)
    columns = tpix // TROWS
    volume = cost_volume.reshape(DEPTH * GROUPS, TROWS * columns)
    volume = jnp.pad(volume, ((GROUPS, GROUPS), (0, 0)))
    count = lax.axis_size("view")
    place = lax.axis_index("view")
    ends = jnp.stack([place == 0, place == count - 1]).astype(jnp.int32)
    hidden = conv_rows(
        halo_cols(volume, 2 * columns),
        banded(kern_one, DEPTH // 4),
        True,
        TROWS + 2,
        columns,
        DEPTH // 4,
        ends,
    )
    scores = conv_rows(hidden, banded(kern_two, DEPTH), False, TROWS, columns, DEPTH)
    return scores


def solution(mesh):
    in_specs = (
        P(("scene", "view"), None, None),
        P(("scene", "view"), None, None),
        P(),
        P(("scene", "view"), None, None),
        P(("scene", "view"), None, None),
        P(("scene", "view"), None),
        P(("scene", "view"), None),
        P(),
        P(),
    )
    out_specs = P(("scene", "view"), None, None)
    return jax.shard_map(body, mesh=mesh, in_specs=in_specs, out_specs=out_specs, check_vma=False)
```

```python
import functools

import jax
import jax.numpy as jnp
from jax import lax
from jax.experimental import pallas as pl
from jax.experimental.pallas import tpu as pltpu
from jax.sharding import PartitionSpec as P

GROUPS = 8
DEPTH = 64
TROWS = 4


def with_halo(block, sides, width):
    for axis, dim in sides:
        count = lax.axis_size(axis)
        forward = [(i, i + 1) for i in range(count - 1)]
        backward = [(target, source) for source, target in forward]
        low = lax.ppermute(
            lax.slice_in_dim(block, block.shape[dim] - width, None, axis=dim), axis, forward
        )
        high = lax.ppermute(lax.slice_in_dim(block, 0, width, axis=dim), axis, backward)
        block = jnp.concatenate([low, block, high], axis=dim)
    return block


def convolve_full(padded, kernel):
    rows_out = padded.shape[0] - 2
    depth_len = padded.shape[2]
    columns = padded.shape[3]
    framed = jnp.pad(padded, ((0, 0), (0, 0), (1, 1), (1, 1)))
    carried = jnp.zeros((rows_out, kernel.shape[-1], depth_len, columns), jnp.float32)
    for depth_off in range(3):
        for row_off in range(3):
            for col_off in range(3):
                window = framed[
                    row_off : row_off + rows_out,
                    :,
                    depth_off : depth_off + depth_len,
                    col_off : col_off + columns,
                ]
                carried = carried + jnp.einsum(
                    "rcdw,ce->redw",
                    window,
                    kernel[depth_off, row_off, col_off],
                    preferred_element_type=jnp.float32,
                )
    return carried


def convolve_final(padded, kernel):
    rows_out = padded.shape[0] - 2
    depth_len = padded.shape[2]
    columns = padded.shape[3]
    framed = jnp.pad(padded, ((0, 0), (0, 0), (1, 1), (1, 1)))
    carried = jnp.zeros((rows_out, depth_len, columns), jnp.float32)
    for depth_off in range(3):
        for row_off in range(3):
            for col_off in range(3):
                window = framed[
                    row_off : row_off + rows_out,
                    :,
                    depth_off : depth_off + depth_len,
                    col_off : col_off + columns,
                ]
                carried = carried + jnp.einsum(
                    "rcdw,c->rdw",
                    window,
                    kernel[depth_off, row_off, col_off],
                    preferred_element_type=jnp.float32,
                )
    return carried


def correlate_kernel(blk_ref, blocks_ref, table_ref, ref_ref, out_ref, arranged, products):
    chunk = 16
    slots = table_ref.shape[0] // blocks_ref.shape[2]
    width = blocks_ref.shape[2]
    channels = blocks_ref.shape[1]
    units = out_ref.shape[0] // GROUPS
    cap = units // ref_ref.shape[0]
    group_size = channels // GROUPS
    rows = chunk * channels

    def step(c, carry):
        for u in range(chunk):
            unit = c * chunk + u
            for w in range(slots):
                arranged[u * channels : (u + 1) * channels, w * width : (w + 1) * width] = blocks_ref[
                    blk_ref[unit * slots + w]
                ]
        warped = jnp.dot(arranged[...], table_ref[...], preferred_element_type=jnp.float32)
        warped = warped.astype(jnp.bfloat16).astype(jnp.float32)
        lanes = products.shape[0]
        for u in range(chunk):
            unit = c * chunk + u
            tile = ref_ref[unit // cap].astype(jnp.float32)
            for j in range(lanes):
                products[j, u * channels : (u + 1) * channels, :] = (
                    warped[u * channels : (u + 1) * channels, j * 128 : (j + 1) * 128]
                    * tile[:, j * 128 : (j + 1) * 128]
                )
        start = pl.multiple_of(c * (chunk * GROUPS), chunk * GROUPS)
        for j in range(lanes):
            total = products[j, pl.ds(0, rows // group_size, stride=group_size), :]
            for k in range(1, group_size):
                total = total + products[j, pl.ds(k, rows // group_size, stride=group_size), :]
            out_ref[pl.ds(start, chunk * GROUPS), j * 128 : (j + 1) * 128] = (
                total * (GROUPS / channels)
            ).astype(out_ref.dtype)
        return carry

    lax.fori_loop(0, units // chunk, step, 0, unroll=2)


def correlate(blk, blocks, table, refs, units):
    channels, width = blocks.shape[1], blocks.shape[2]
    tpix = table.shape[1]
    chunk = 16
    return pl.pallas_call(
        correlate_kernel,
        out_shape=jax.ShapeDtypeStruct((units * GROUPS, tpix), jnp.bfloat16),
        in_specs=[
            pl.BlockSpec(memory_space=pltpu.SMEM),
            pl.BlockSpec(memory_space=pltpu.VMEM),
            pl.BlockSpec(memory_space=pltpu.VMEM),
            pl.BlockSpec(memory_space=pltpu.VMEM),
        ],
        out_specs=pl.BlockSpec(memory_space=pltpu.VMEM),
        scratch_shapes=[
            pltpu.VMEM((chunk * channels, table.shape[0]), jnp.bfloat16),
            pltpu.VMEM((tpix // 128, chunk * channels, 128), jnp.float32),
        ],
    )(blk, blocks, table, refs)


def conv_kernel(*refs, relu, rows, cols, groups, chunk):
    if relu:
        ends_ref, x_ref, m_ref, out_ref = refs
    else:
        x_ref, m_ref, out_ref = refs
    width = rows * cols
    outs = m_ref.shape[2]
    depth = x_ref.shape[0] // groups - 2
    lane = lax.broadcasted_iota(jnp.int32, (outs, width), 1) % cols
    for k in range(depth // chunk):
        acc = None
        for e in range(3):
            y = None
            for b in range(3):
                window = x_ref[k * chunk * groups : (k * chunk + chunk + 2) * groups, b * cols : b * cols + width]
                part = jnp.dot(m_ref[b, e], window, preferred_element_type=jnp.float32)
                y = part if y is None else y + part
            if e == 0:
                y = jnp.where(lane >= 1, pltpu.roll(y, 1, 1), 0.0)
            elif e == 2:
                y = jnp.where(lane <= cols - 2, pltpu.roll(y, width - 1, 1), 0.0)
            acc = y if acc is None else acc + y
        if relu:
            block = lax.broadcasted_iota(jnp.int32, (outs, width), 1) // cols
            outside = ((block == 0) & (ends_ref[0] > 0)) | ((block == rows - 1) & (ends_ref[1] > 0))
            acc = jnp.where(outside, 0.0, acc)
            out_ref[(k * chunk + 1) * outs // chunk : (k * chunk + chunk + 1) * outs // chunk, :] = (
                jnp.maximum(acc, 0.0).astype(out_ref.dtype)
            )
        else:
            for r in range(rows):
                out_ref[r, k * chunk : (k + 1) * chunk, :] = acc[:, r * cols : (r + 1) * cols]
    if relu:
        pad = jnp.zeros((outs // chunk, width), out_ref.dtype)
        out_ref[: outs // chunk, :] = pad
        out_ref[out_ref.shape[0] - outs // chunk :, :] = pad


def banded(kernel, chunk):
    groups = kernel.shape[3]
    cols = (chunk + 2) * groups
    taps = kernel.reshape((3, 9) + kernel.shape[3:])
    col = lax.iota(jnp.int32, cols)
    spread = (col[None, :] % groups == jnp.arange(groups)[:, None]).astype(kernel.dtype)
    if kernel.ndim == 5:
        outs = kernel.shape[4]
        rows = chunk * outs
        row = lax.iota(jnp.int32, rows)
        pick = (row[:, None] % outs == jnp.arange(outs)[None, :]).astype(kernel.dtype)
        lanes = jnp.einsum("xyio,ic->xyoc", taps, spread, preferred_element_type=jnp.float32)
        tiles = jnp.einsum(
            "ro,xyoc->xyrc", pick, lanes.astype(kernel.dtype), preferred_element_type=jnp.float32
        )
        depth_of_row = row // outs
    else:
        rows = chunk
        lanes = jnp.einsum("xyi,ic->xyc", taps, spread, preferred_element_type=jnp.float32)
        tiles = lanes[:, :, None, :]
        depth_of_row = lax.iota(jnp.int32, rows)
    band = col[None, None, :] // groups == depth_of_row[None, :, None] + jnp.arange(3)[:, None, None]
    mats = jnp.sum(jnp.where(band[:, None], tiles, 0.0), axis=0)
    return mats.astype(kernel.dtype).reshape(3, 3, rows, cols)


def conv_rows(framed, mats, relu, rows, cols, chunk, ends=None):
    outs = mats.shape[2]
    groups = mats.shape[3] // (chunk + 2)
    depth = framed.shape[0] // groups - 2
    if relu:
        out_shape = jax.ShapeDtypeStruct(((depth + 2) * outs // chunk, rows * cols), jnp.bfloat16)
    else:
        out_shape = jax.ShapeDtypeStruct((rows, depth, cols), jnp.float32)
    operands = (framed, mats) if ends is None else (ends, framed, mats)
    in_specs = [pl.BlockSpec(memory_space=pltpu.VMEM), pl.BlockSpec(memory_space=pltpu.VMEM)]
    if ends is not None:
        in_specs = [pl.BlockSpec(memory_space=pltpu.SMEM)] + in_specs
    return pl.pallas_call(
        functools.partial(conv_kernel, relu=relu, rows=rows, cols=cols, groups=groups, chunk=chunk),
        out_shape=out_shape,
        in_specs=in_specs,
        out_specs=pl.BlockSpec(memory_space=pltpu.VMEM),
    )(*operands)


def halo_cols(block, cols):
    count = lax.axis_size("view")
    forward = [(i, i + 1) for i in range(count - 1)]
    backward = [(target, source) for source, target in forward]
    low = lax.ppermute(block[:, block.shape[1] - cols :], "view", forward)
    high = lax.ppermute(block[:, :cols], "view", backward)
    return jnp.concatenate([low, block, high], axis=1)


def gather_view(block):
    count = lax.axis_size("view")
    if count & (count - 1):
        return lax.all_to_all(
            jnp.broadcast_to(block, (count,) + block.shape[1:]), "view", 0, 0, tiled=True
        )
    index = lax.axis_index("view")
    gathered = block[0]
    level = 0
    stride = count // 2
    while stride >= 1:
        other = lax.ppermute(gathered, "view", [(i, i ^ stride) for i in range(count)])
        low = (index // stride) % 2 == 0
        gathered = jnp.where(
            low, jnp.stack([gathered, other], axis=level), jnp.stack([other, gathered], axis=level)
        )
        level += 1
        stride //= 2
    return gathered.reshape((count,) + block.shape[1:])


def pad_rows(volume):
    return with_halo(volume, (("view", 0),), 1)


def body(
    src_feat,
    ref_feat,
    weight_table,
    src_block,
    table_index,
    block_count,
    depth_plane,
    kern_one,
    kern_two,
):
    owners = lax.axis_size("view")
    features = src_feat[0]
    channels, spix = features.shape
    slots, block_width, tpix = weight_table.shape
    blocks = features.reshape(channels, spix // block_width, block_width).transpose(1, 0, 2)
    units = src_block.shape[1]
    cap = units // owners
    counts = block_count[0]
    nblocks = spix // block_width
    blocks = jnp.concatenate([blocks, jnp.zeros_like(blocks[:1])], axis=0)
    matches = table_index[0][:, :, None] == jnp.arange(slots)[None, None, :]
    live = (jnp.arange(slots)[None, :] < counts[:, None])[:, :, None] & matches
    picked = jnp.sum(jnp.where(matches, src_block[0][:, :, None], 0), axis=1)
    alive = jnp.any(live, axis=1)
    blk = jnp.where(alive, picked, nblocks).reshape(-1).astype(jnp.int32)
    depth_code = jnp.where(counts > 0, depth_plane[0], -1).astype(jnp.bfloat16)

    ref_all = gather_view(ref_feat)
    corr_all = correlate(
        blk, blocks, weight_table.reshape(slots * block_width, tpix), ref_all, units
    ).reshape(units, GROUPS * tpix)
    tag_lanes = jnp.broadcast_to(depth_code[:, None], (units, 128))
    payload = jnp.concatenate([corr_all, tag_lanes], axis=1)
    arriving = lax.all_to_all(
        payload.reshape(owners, cap, GROUPS * tpix + 128),
        "view",
        split_axis=0,
        concat_axis=0,
        tiled=True,
    ).reshape(owners * cap, GROUPS * tpix + 128)
    received = arriving[:, : GROUPS * tpix]
    depth_tags = arriving[:, GROUPS * tpix]
    onehot = (
        depth_tags[None, :] == jnp.arange(DEPTH).astype(jnp.bfloat16)[:, None]
    ).astype(jnp.bfloat16)
    summed = jnp.dot(onehot, received, preferred_element_type=jnp.float32)
    tallies = jnp.sum(onehot.astype(jnp.float32), axis=1)
    cost_volume = (summed / jnp.maximum(tallies, 1.0)[:, None]).astype(jnp.bfloat16)
    columns = tpix // TROWS
    volume = cost_volume.reshape(DEPTH * GROUPS, TROWS * columns)
    volume = jnp.pad(volume, ((GROUPS, GROUPS), (0, 0)))
    count = lax.axis_size("view")
    place = lax.axis_index("view")
    ends = jnp.stack([place == 0, place == count - 1]).astype(jnp.int32)
    hidden = conv_rows(
        halo_cols(volume, 2 * columns),
        banded(kern_one, DEPTH // 4),
        True,
        TROWS + 2,
        columns,
        DEPTH // 4,
        ends,
    )
    scores = conv_rows(hidden, banded(kern_two, DEPTH), False, TROWS, columns, DEPTH)
    return scores


def solution(mesh):
    in_specs = (
        P(("scene", "view"), None, None),
        P(("scene", "view"), None, None),
        P(),
        P(("scene", "view"), None, None),
        P(("scene", "view"), None, None),
        P(("scene", "view"), None),
        P(("scene", "view"), None),
        P(),
        P(),
    )
    out_specs = P(("scene", "view"), None, None)
    return jax.shard_map(body, mesh=mesh, in_specs=in_specs, out_specs=out_specs, check_vma=False)
```

```python
import functools

import jax
import jax.numpy as jnp
from jax import lax
from jax.experimental import pallas as pl
from jax.experimental.pallas import tpu as pltpu
from jax.sharding import PartitionSpec as P

GROUPS = 8
DEPTH = 64
TROWS = 4


def with_halo(block, sides, width):
    for axis, dim in sides:
        count = lax.axis_size(axis)
        forward = [(i, i + 1) for i in range(count - 1)]
        backward = [(target, source) for source, target in forward]
        low = lax.ppermute(
            lax.slice_in_dim(block, block.shape[dim] - width, None, axis=dim), axis, forward
        )
        high = lax.ppermute(lax.slice_in_dim(block, 0, width, axis=dim), axis, backward)
        block = jnp.concatenate([low, block, high], axis=dim)
    return block


def convolve_full(padded, kernel):
    rows_out = padded.shape[0] - 2
    depth_len = padded.shape[2]
    columns = padded.shape[3]
    framed = jnp.pad(padded, ((0, 0), (0, 0), (1, 1), (1, 1)))
    carried = jnp.zeros((rows_out, kernel.shape[-1], depth_len, columns), jnp.float32)
    for depth_off in range(3):
        for row_off in range(3):
            for col_off in range(3):
                window = framed[
                    row_off : row_off + rows_out,
                    :,
                    depth_off : depth_off + depth_len,
                    col_off : col_off + columns,
                ]
                carried = carried + jnp.einsum(
                    "rcdw,ce->redw",
                    window,
                    kernel[depth_off, row_off, col_off],
                    preferred_element_type=jnp.float32,
                )
    return carried


def convolve_final(padded, kernel):
    rows_out = padded.shape[0] - 2
    depth_len = padded.shape[2]
    columns = padded.shape[3]
    framed = jnp.pad(padded, ((0, 0), (0, 0), (1, 1), (1, 1)))
    carried = jnp.zeros((rows_out, depth_len, columns), jnp.float32)
    for depth_off in range(3):
        for row_off in range(3):
            for col_off in range(3):
                window = framed[
                    row_off : row_off + rows_out,
                    :,
                    depth_off : depth_off + depth_len,
                    col_off : col_off + columns,
                ]
                carried = carried + jnp.einsum(
                    "rcdw,c->rdw",
                    window,
                    kernel[depth_off, row_off, col_off],
                    preferred_element_type=jnp.float32,
                )
    return carried


def correlate_kernel(blk_ref, blocks_ref, table_ref, ref_ref, out_ref, arranged, products):
    chunk = 16
    slots = table_ref.shape[0] // blocks_ref.shape[2]
    width = blocks_ref.shape[2]
    channels = blocks_ref.shape[1]
    units = out_ref.shape[0] // GROUPS
    cap = units // ref_ref.shape[0]
    group_size = channels // GROUPS
    rows = chunk * channels

    def step(c, carry):
        for u in range(chunk):
            unit = c * chunk + u
            for w in range(slots):
                arranged[u * channels : (u + 1) * channels, w * width : (w + 1) * width] = blocks_ref[
                    blk_ref[unit * slots + w]
                ]
        warped = jnp.dot(arranged[...], table_ref[...], preferred_element_type=jnp.float32)
        warped = warped.astype(jnp.bfloat16).astype(jnp.float32)
        lanes = products.shape[0]
        for u in range(chunk):
            unit = c * chunk + u
            tile = ref_ref[unit // cap].astype(jnp.float32)
            for j in range(lanes):
                products[j, u * channels : (u + 1) * channels, :] = (
                    warped[u * channels : (u + 1) * channels, j * 128 : (j + 1) * 128]
                    * tile[:, j * 128 : (j + 1) * 128]
                )
        start = pl.multiple_of(c * (chunk * GROUPS), chunk * GROUPS)
        for j in range(lanes):
            total = products[j, pl.ds(0, rows // group_size, stride=group_size), :]
            for k in range(1, group_size):
                total = total + products[j, pl.ds(k, rows // group_size, stride=group_size), :]
            out_ref[pl.ds(start, chunk * GROUPS), j * 128 : (j + 1) * 128] = (
                total * (GROUPS / channels)
            ).astype(out_ref.dtype)
        return carry

    lax.fori_loop(0, units // chunk, step, 0, unroll=2)


def correlate(blk, blocks, table, refs, units):
    channels, width = blocks.shape[1], blocks.shape[2]
    tpix = table.shape[1]
    chunk = 16
    return pl.pallas_call(
        correlate_kernel,
        out_shape=jax.ShapeDtypeStruct((units * GROUPS, tpix), jnp.bfloat16),
        in_specs=[
            pl.BlockSpec(memory_space=pltpu.SMEM),
            pl.BlockSpec(memory_space=pltpu.VMEM),
            pl.BlockSpec(memory_space=pltpu.VMEM),
            pl.BlockSpec(memory_space=pltpu.VMEM),
        ],
        out_specs=pl.BlockSpec(memory_space=pltpu.VMEM),
        scratch_shapes=[
            pltpu.VMEM((chunk * channels, table.shape[0]), jnp.bfloat16),
            pltpu.VMEM((tpix // 128, chunk * channels, 128), jnp.float32),
        ],
    )(blk, blocks, table, refs)


def conv_kernel(*refs, relu, rows, cols, groups, chunk):
    if relu:
        ends_ref, x_ref, m_ref, out_ref = refs
    else:
        x_ref, m_ref, out_ref = refs
    width = rows * cols
    outs = m_ref.shape[2]
    depth = x_ref.shape[0] // groups - 2
    lane = lax.broadcasted_iota(jnp.int32, (outs, width), 1) % cols
    for k in range(depth // chunk):
        acc = None
        for e in range(3):
            y = None
            for b in range(3):
                window = x_ref[k * chunk * groups : (k * chunk + chunk + 2) * groups, b * cols : b * cols + width]
                part = jnp.dot(m_ref[b, e], window, preferred_element_type=jnp.float32)
                y = part if y is None else y + part
            if e == 0:
                y = jnp.where(lane >= 1, pltpu.roll(y, 1, 1), 0.0)
            elif e == 2:
                y = jnp.where(lane <= cols - 2, pltpu.roll(y, width - 1, 1), 0.0)
            acc = y if acc is None else acc + y
        if relu:
            block = lax.broadcasted_iota(jnp.int32, (outs, width), 1) // cols
            outside = ((block == 0) & (ends_ref[0] > 0)) | ((block == rows - 1) & (ends_ref[1] > 0))
            acc = jnp.where(outside, 0.0, acc)
            out_ref[(k * chunk + 1) * outs // chunk : (k * chunk + chunk + 1) * outs // chunk, :] = (
                jnp.maximum(acc, 0.0).astype(out_ref.dtype)
            )
        else:
            for r in range(rows):
                out_ref[r, k * chunk : (k + 1) * chunk, :] = acc[:, r * cols : (r + 1) * cols]
    if relu:
        pad = jnp.zeros((outs // chunk, width), out_ref.dtype)
        out_ref[: outs // chunk, :] = pad
        out_ref[out_ref.shape[0] - outs // chunk :, :] = pad


def banded(kernel, chunk):
    groups = kernel.shape[3]
    cols = (chunk + 2) * groups
    taps = kernel.reshape((3, 9) + kernel.shape[3:])
    col = lax.iota(jnp.int32, cols)
    spread = (col[None, :] % groups == jnp.arange(groups)[:, None]).astype(kernel.dtype)
    if kernel.ndim == 5:
        outs = kernel.shape[4]
        rows = chunk * outs
        row = lax.iota(jnp.int32, rows)
        pick = (row[:, None] % outs == jnp.arange(outs)[None, :]).astype(kernel.dtype)
        lanes = jnp.einsum("xyio,ic->xyoc", taps, spread, preferred_element_type=jnp.float32)
        tiles = jnp.einsum(
            "ro,xyoc->xyrc", pick, lanes.astype(kernel.dtype), preferred_element_type=jnp.float32
        )
        depth_of_row = row // outs
    else:
        rows = chunk
        lanes = jnp.einsum("xyi,ic->xyc", taps, spread, preferred_element_type=jnp.float32)
        tiles = lanes[:, :, None, :]
        depth_of_row = lax.iota(jnp.int32, rows)
    band = col[None, None, :] // groups == depth_of_row[None, :, None] + jnp.arange(3)[:, None, None]
    mats = jnp.sum(jnp.where(band[:, None], tiles, 0.0), axis=0)
    return mats.astype(kernel.dtype).reshape(3, 3, rows, cols)


def conv_rows(framed, mats, relu, rows, cols, chunk, ends=None):
    outs = mats.shape[2]
    groups = mats.shape[3] // (chunk + 2)
    depth = framed.shape[0] // groups - 2
    if relu:
        out_shape = jax.ShapeDtypeStruct(((depth + 2) * outs // chunk, rows * cols), jnp.bfloat16)
    else:
        out_shape = jax.ShapeDtypeStruct((rows, depth, cols), jnp.float32)
    operands = (framed, mats) if ends is None else (ends, framed, mats)
    in_specs = [pl.BlockSpec(memory_space=pltpu.VMEM), pl.BlockSpec(memory_space=pltpu.VMEM)]
    if ends is not None:
        in_specs = [pl.BlockSpec(memory_space=pltpu.SMEM)] + in_specs
    return pl.pallas_call(
        functools.partial(conv_kernel, relu=relu, rows=rows, cols=cols, groups=groups, chunk=chunk),
        out_shape=out_shape,
        in_specs=in_specs,
        out_specs=pl.BlockSpec(memory_space=pltpu.VMEM),
    )(*operands)


def halo_cols(block, cols):
    count = lax.axis_size("view")
    forward = [(i, i + 1) for i in range(count - 1)]
    backward = [(target, source) for source, target in forward]
    low = lax.ppermute(block[:, block.shape[1] - cols :], "view", forward)
    high = lax.ppermute(block[:, :cols], "view", backward)
    return jnp.concatenate([low, block, high], axis=1)


def gather_view(block):
    count = lax.axis_size("view")
    if count & (count - 1):
        return lax.all_to_all(
            jnp.broadcast_to(block, (count,) + block.shape[1:]), "view", 0, 0, tiled=True
        )
    index = lax.axis_index("view")
    gathered = block[0]
    level = 0
    stride = count // 2
    if count >= 4:
        top = count // 4
        parts = [gathered] + [
            lax.ppermute(gathered, "view", [(i, i ^ (m * top)) for i in range(count)])
            for m in (1, 2, 3)
        ]
        order = jnp.arange(4) ^ ((index // top) % 4)
        gathered = jnp.take(jnp.stack(parts), order, axis=0).reshape((2, 2) + gathered.shape)
        level = 2
        stride = top // 2
    while stride >= 1:
        other = lax.ppermute(gathered, "view", [(i, i ^ stride) for i in range(count)])
        low = (index // stride) % 2 == 0
        gathered = jnp.where(
            low, jnp.stack([gathered, other], axis=level), jnp.stack([other, gathered], axis=level)
        )
        level += 1
        stride //= 2
    return gathered.reshape((count,) + block.shape[1:])


def pad_rows(volume):
    return with_halo(volume, (("view", 0),), 1)


def body(
    src_feat,
    ref_feat,
    weight_table,
    src_block,
    table_index,
    block_count,
    depth_plane,
    kern_one,
    kern_two,
):
    owners = lax.axis_size("view")
    features = src_feat[0]
    channels, spix = features.shape
    slots, block_width, tpix = weight_table.shape
    blocks = features.reshape(channels, spix // block_width, block_width).transpose(1, 0, 2)
    units = src_block.shape[1]
    cap = units // owners
    counts = block_count[0]
    nblocks = spix // block_width
    blocks = jnp.concatenate([blocks, jnp.zeros_like(blocks[:1])], axis=0)
    matches = table_index[0][:, :, None] == jnp.arange(slots)[None, None, :]
    live = (jnp.arange(slots)[None, :] < counts[:, None])[:, :, None] & matches
    picked = jnp.sum(jnp.where(matches, src_block[0][:, :, None], 0), axis=1)
    alive = jnp.any(live, axis=1)
    blk = jnp.where(alive, picked, nblocks).reshape(-1).astype(jnp.int32)
    depth_code = jnp.where(counts > 0, depth_plane[0], -1).astype(jnp.bfloat16)

    ref_all = gather_view(ref_feat)
    corr_all = correlate(
        blk, blocks, weight_table.reshape(slots * block_width, tpix), ref_all, units
    ).reshape(units, GROUPS * tpix)
    tag_lanes = jnp.broadcast_to(depth_code[:, None], (units, 128))
    payload = jnp.concatenate([corr_all, tag_lanes], axis=1)
    arriving = lax.all_to_all(
        payload.reshape(owners, cap, GROUPS * tpix + 128),
        "view",
        split_axis=0,
        concat_axis=0,
        tiled=True,
    ).reshape(owners * cap, GROUPS * tpix + 128)
    received = arriving[:, : GROUPS * tpix]
    depth_tags = arriving[:, GROUPS * tpix]
    onehot = (
        depth_tags[None, :] == jnp.arange(DEPTH).astype(jnp.bfloat16)[:, None]
    ).astype(jnp.bfloat16)
    summed = jnp.dot(onehot, received, preferred_element_type=jnp.float32)
    tallies = jnp.sum(onehot.astype(jnp.float32), axis=1)
    cost_volume = (summed / jnp.maximum(tallies, 1.0)[:, None]).astype(jnp.bfloat16)
    columns = tpix // TROWS
    volume = cost_volume.reshape(DEPTH * GROUPS, TROWS * columns)
    volume = jnp.pad(volume, ((GROUPS, GROUPS), (0, 0)))
    count = lax.axis_size("view")
    place = lax.axis_index("view")
    ends = jnp.stack([place == 0, place == count - 1]).astype(jnp.int32)
    hidden = conv_rows(
        halo_cols(volume, 2 * columns),
        banded(kern_one, DEPTH // 4),
        True,
        TROWS + 2,
        columns,
        DEPTH // 4,
        ends,
    )
    scores = conv_rows(hidden, banded(kern_two, DEPTH), False, TROWS, columns, DEPTH)
    return scores


def solution(mesh):
    in_specs = (
        P(("scene", "view"), None, None),
        P(("scene", "view"), None, None),
        P(),
        P(("scene", "view"), None, None),
        P(("scene", "view"), None, None),
        P(("scene", "view"), None),
        P(("scene", "view"), None),
        P(),
        P(),
    )
    out_specs = P(("scene", "view"), None, None)
    return jax.shard_map(body, mesh=mesh, in_specs=in_specs, out_specs=out_specs, check_vma=False)
```

```python
import functools

import jax
import jax.numpy as jnp
from jax import lax
from jax.experimental import pallas as pl
from jax.experimental.pallas import tpu as pltpu
from jax.sharding import PartitionSpec as P

GROUPS = 8
DEPTH = 64
TROWS = 4


def with_halo(block, sides, width):
    for axis, dim in sides:
        count = lax.axis_size(axis)
        forward = [(i, i + 1) for i in range(count - 1)]
        backward = [(target, source) for source, target in forward]
        low = lax.ppermute(
            lax.slice_in_dim(block, block.shape[dim] - width, None, axis=dim), axis, forward
        )
        high = lax.ppermute(lax.slice_in_dim(block, 0, width, axis=dim), axis, backward)
        block = jnp.concatenate([low, block, high], axis=dim)
    return block


def convolve_full(padded, kernel):
    rows_out = padded.shape[0] - 2
    depth_len = padded.shape[2]
    columns = padded.shape[3]
    framed = jnp.pad(padded, ((0, 0), (0, 0), (1, 1), (1, 1)))
    carried = jnp.zeros((rows_out, kernel.shape[-1], depth_len, columns), jnp.float32)
    for depth_off in range(3):
        for row_off in range(3):
            for col_off in range(3):
                window = framed[
                    row_off : row_off + rows_out,
                    :,
                    depth_off : depth_off + depth_len,
                    col_off : col_off + columns,
                ]
                carried = carried + jnp.einsum(
                    "rcdw,ce->redw",
                    window,
                    kernel[depth_off, row_off, col_off],
                    preferred_element_type=jnp.float32,
                )
    return carried


def convolve_final(padded, kernel):
    rows_out = padded.shape[0] - 2
    depth_len = padded.shape[2]
    columns = padded.shape[3]
    framed = jnp.pad(padded, ((0, 0), (0, 0), (1, 1), (1, 1)))
    carried = jnp.zeros((rows_out, depth_len, columns), jnp.float32)
    for depth_off in range(3):
        for row_off in range(3):
            for col_off in range(3):
                window = framed[
                    row_off : row_off + rows_out,
                    :,
                    depth_off : depth_off + depth_len,
                    col_off : col_off + columns,
                ]
                carried = carried + jnp.einsum(
                    "rcdw,c->rdw",
                    window,
                    kernel[depth_off, row_off, col_off],
                    preferred_element_type=jnp.float32,
                )
    return carried


def correlate_kernel(blk_ref, blocks_ref, table_ref, ref_ref, out_ref, arranged, products):
    chunk = 16
    slots = table_ref.shape[0] // blocks_ref.shape[2]
    width = blocks_ref.shape[2]
    channels = blocks_ref.shape[1]
    units = out_ref.shape[0] // GROUPS
    cap = units // ref_ref.shape[0]
    group_size = channels // GROUPS
    rows = chunk * channels

    def step(c, carry):
        for u in range(chunk):
            unit = c * chunk + u
            for w in range(slots):
                arranged[u * channels : (u + 1) * channels, w * width : (w + 1) * width] = blocks_ref[
                    blk_ref[unit * slots + w]
                ]
        warped = jnp.dot(arranged[...], table_ref[...], preferred_element_type=jnp.float32)
        warped = warped.astype(jnp.bfloat16).astype(jnp.float32)
        lanes = products.shape[0]
        for u in range(chunk):
            unit = c * chunk + u
            tile = ref_ref[unit // cap].astype(jnp.float32)
            for j in range(lanes):
                products[j, u * channels : (u + 1) * channels, :] = (
                    warped[u * channels : (u + 1) * channels, j * 128 : (j + 1) * 128]
                    * tile[:, j * 128 : (j + 1) * 128]
                )
        start = pl.multiple_of(c * (chunk * GROUPS), chunk * GROUPS)
        for j in range(lanes):
            total = products[j, pl.ds(0, rows // group_size, stride=group_size), :]
            for k in range(1, group_size):
                total = total + products[j, pl.ds(k, rows // group_size, stride=group_size), :]
            out_ref[pl.ds(start, chunk * GROUPS), j * 128 : (j + 1) * 128] = (
                total * (GROUPS / channels)
            ).astype(out_ref.dtype)
        return carry

    lax.fori_loop(0, units // chunk, step, 0, unroll=2)


def correlate(blk, blocks, table, refs, units):
    channels, width = blocks.shape[1], blocks.shape[2]
    tpix = table.shape[1]
    chunk = 16
    return pl.pallas_call(
        correlate_kernel,
        out_shape=jax.ShapeDtypeStruct((units * GROUPS, tpix), jnp.bfloat16),
        in_specs=[
            pl.BlockSpec(memory_space=pltpu.SMEM),
            pl.BlockSpec(memory_space=pltpu.VMEM),
            pl.BlockSpec(memory_space=pltpu.VMEM),
            pl.BlockSpec(memory_space=pltpu.VMEM),
        ],
        out_specs=pl.BlockSpec(memory_space=pltpu.VMEM),
        scratch_shapes=[
            pltpu.VMEM((chunk * channels, table.shape[0]), jnp.bfloat16),
            pltpu.VMEM((tpix // 128, chunk * channels, 128), jnp.float32),
        ],
    )(blk, blocks, table, refs)


def conv_kernel(*refs, relu, rows, cols, groups, chunk):
    if relu:
        ends_ref, x_ref, m_ref, out_ref = refs
    else:
        x_ref, m_ref, out_ref = refs
    width = rows * cols
    outs = m_ref.shape[2]
    depth = x_ref.shape[0] // groups - 2
    lane = lax.broadcasted_iota(jnp.int32, (outs, width), 1) % cols
    for k in range(depth // chunk):
        acc = None
        for e in range(3):
            y = None
            for b in range(3):
                window = x_ref[k * chunk * groups : (k * chunk + chunk + 2) * groups, b * cols : b * cols + width]
                part = jnp.dot(m_ref[b, e], window, preferred_element_type=jnp.float32)
                y = part if y is None else y + part
            if e == 0:
                y = jnp.where(lane >= 1, pltpu.roll(y, 1, 1), 0.0)
            elif e == 2:
                y = jnp.where(lane <= cols - 2, pltpu.roll(y, width - 1, 1), 0.0)
            acc = y if acc is None else acc + y
        if relu:
            block = lax.broadcasted_iota(jnp.int32, (outs, width), 1) // cols
            outside = ((block == 0) & (ends_ref[0] > 0)) | ((block == rows - 1) & (ends_ref[1] > 0))
            acc = jnp.where(outside, 0.0, acc)
            out_ref[(k * chunk + 1) * outs // chunk : (k * chunk + chunk + 1) * outs // chunk, :] = (
                jnp.maximum(acc, 0.0).astype(out_ref.dtype)
            )
        else:
            for r in range(rows):
                out_ref[r, k * chunk : (k + 1) * chunk, :] = acc[:, r * cols : (r + 1) * cols]
    if relu:
        pad = jnp.zeros((outs // chunk, width), out_ref.dtype)
        out_ref[: outs // chunk, :] = pad
        out_ref[out_ref.shape[0] - outs // chunk :, :] = pad


def banded(kernel, chunk):
    groups = kernel.shape[3]
    cols = (chunk + 2) * groups
    taps = kernel.reshape((3, 9) + kernel.shape[3:])
    col = lax.iota(jnp.int32, cols)
    spread = (col[None, :] % groups == jnp.arange(groups)[:, None]).astype(kernel.dtype)
    if kernel.ndim == 5:
        outs = kernel.shape[4]
        rows = chunk * outs
        row = lax.iota(jnp.int32, rows)
        pick = (row[:, None] % outs == jnp.arange(outs)[None, :]).astype(kernel.dtype)
        lanes = jnp.einsum("xyio,ic->xyoc", taps, spread, preferred_element_type=jnp.float32)
        tiles = jnp.einsum(
            "ro,xyoc->xyrc", pick, lanes.astype(kernel.dtype), preferred_element_type=jnp.float32
        )
        depth_of_row = row // outs
    else:
        rows = chunk
        lanes = jnp.einsum("xyi,ic->xyc", taps, spread, preferred_element_type=jnp.float32)
        tiles = lanes[:, :, None, :]
        depth_of_row = lax.iota(jnp.int32, rows)
    band = col[None, None, :] // groups == depth_of_row[None, :, None] + jnp.arange(3)[:, None, None]
    mats = jnp.sum(jnp.where(band[:, None], tiles, 0.0), axis=0)
    return mats.astype(kernel.dtype).reshape(3, 3, rows, cols)


def conv_rows(framed, mats, relu, rows, cols, chunk, ends=None):
    outs = mats.shape[2]
    groups = mats.shape[3] // (chunk + 2)
    depth = framed.shape[0] // groups - 2
    if relu:
        out_shape = jax.ShapeDtypeStruct(((depth + 2) * outs // chunk, rows * cols), jnp.bfloat16)
    else:
        out_shape = jax.ShapeDtypeStruct((rows, depth, cols), jnp.float32)
    operands = (framed, mats) if ends is None else (ends, framed, mats)
    in_specs = [pl.BlockSpec(memory_space=pltpu.VMEM), pl.BlockSpec(memory_space=pltpu.VMEM)]
    if ends is not None:
        in_specs = [pl.BlockSpec(memory_space=pltpu.SMEM)] + in_specs
    return pl.pallas_call(
        functools.partial(conv_kernel, relu=relu, rows=rows, cols=cols, groups=groups, chunk=chunk),
        out_shape=out_shape,
        in_specs=in_specs,
        out_specs=pl.BlockSpec(memory_space=pltpu.VMEM),
    )(*operands)


def halo_cols(block, cols):
    count = lax.axis_size("view")
    forward = [(i, i + 1) for i in range(count - 1)]
    backward = [(target, source) for source, target in forward]
    low = lax.ppermute(block[:, block.shape[1] - cols :], "view", forward)
    high = lax.ppermute(block[:, :cols], "view", backward)
    return jnp.concatenate([low, block, high], axis=1)


def gather_view(block):
    count = lax.axis_size("view")
    if count & (count - 1):
        return lax.all_to_all(
            jnp.broadcast_to(block, (count,) + block.shape[1:]), "view", 0, 0, tiled=True
        )
    index = lax.axis_index("view")
    gathered = block[0]
    level = 0
    stride = count // 2
    if count >= 4:
        top = count // 4
        parts = [gathered] + [
            lax.ppermute(gathered, "view", [(i, i ^ (m * top)) for i in range(count)])
            for m in (1, 2, 3)
        ]
        order = jnp.arange(4) ^ ((index // top) % 4)
        gathered = jnp.take(jnp.stack(parts), order, axis=0).reshape((2, 2) + gathered.shape)
        level = 2
        stride = top // 2
    while stride >= 1:
        other = lax.ppermute(gathered, "view", [(i, i ^ stride) for i in range(count)])
        low = (index // stride) % 2 == 0
        gathered = jnp.where(
            low, jnp.stack([gathered, other], axis=level), jnp.stack([other, gathered], axis=level)
        )
        level += 1
        stride //= 2
    return gathered.reshape((count,) + block.shape[1:])


def pad_rows(volume):
    return with_halo(volume, (("view", 0),), 1)


def body(
    src_feat,
    ref_feat,
    weight_table,
    src_block,
    table_index,
    block_count,
    depth_plane,
    kern_one,
    kern_two,
):
    owners = lax.axis_size("view")
    features = src_feat[0]
    channels, spix = features.shape
    slots, block_width, tpix = weight_table.shape
    blocks = features.reshape(channels, spix // block_width, block_width).transpose(1, 0, 2)
    units = src_block.shape[1]
    cap = units // owners
    counts = block_count[0]
    nblocks = spix // block_width
    blocks = jnp.concatenate([blocks, jnp.zeros_like(blocks[:1])], axis=0)
    matches = table_index[0][:, :, None] == jnp.arange(slots)[None, None, :]
    live = (jnp.arange(slots)[None, :] < counts[:, None])[:, :, None] & matches
    picked = jnp.sum(jnp.where(matches, src_block[0][:, :, None], 0), axis=1)
    alive = jnp.any(live, axis=1)
    blk = jnp.where(alive, picked, nblocks).reshape(-1).astype(jnp.int32)
    depth_code = jnp.where(counts > 0, depth_plane[0], -1).astype(jnp.bfloat16)

    tag_block = jnp.pad(depth_code, (0, channels * 128 - units)).reshape(channels, 128)
    ref_all = gather_view(jnp.concatenate([ref_feat[0], tag_block], axis=1)[None])
    corr_all = correlate(
        blk, blocks, weight_table.reshape(slots * block_width, tpix), ref_all, units
    )
    arriving = lax.all_to_all(
        corr_all.reshape(owners, cap * GROUPS, tpix),
        "view",
        split_axis=0,
        concat_axis=0,
        tiled=True,
    ).reshape(owners * cap, GROUPS, tpix)
    depth_tags = lax.dynamic_slice_in_dim(
        ref_all[:, :, tpix:].reshape(owners, channels * 128), lax.axis_index("view") * cap, cap, axis=1
    ).reshape(owners * cap)
    onehot = (
        depth_tags[None, :] == jnp.arange(DEPTH).astype(jnp.bfloat16)[:, None]
    ).astype(jnp.bfloat16)
    summed = jnp.einsum("dn,ngp->dgp", onehot, arriving, preferred_element_type=jnp.float32)
    tallies = jnp.sum(onehot.astype(jnp.float32), axis=1)
    cost_volume = (summed / jnp.maximum(tallies, 1.0)[:, None, None]).astype(jnp.bfloat16)
    columns = tpix // TROWS
    volume = cost_volume.reshape(DEPTH * GROUPS, TROWS * columns)
    volume = jnp.pad(volume, ((GROUPS, GROUPS), (0, 0)))
    count = lax.axis_size("view")
    place = lax.axis_index("view")
    ends = jnp.stack([place == 0, place == count - 1]).astype(jnp.int32)
    hidden = conv_rows(
        halo_cols(volume, 2 * columns),
        banded(kern_one, DEPTH // 4),
        True,
        TROWS + 2,
        columns,
        DEPTH // 4,
        ends,
    )
    scores = conv_rows(hidden, banded(kern_two, DEPTH), False, TROWS, columns, DEPTH)
    return scores


def solution(mesh):
    in_specs = (
        P(("scene", "view"), None, None),
        P(("scene", "view"), None, None),
        P(),
        P(("scene", "view"), None, None),
        P(("scene", "view"), None, None),
        P(("scene", "view"), None),
        P(("scene", "view"), None),
        P(),
        P(),
    )
    out_specs = P(("scene", "view"), None, None)
    return jax.shard_map(body, mesh=mesh, in_specs=in_specs, out_specs=out_specs, check_vma=False)
```

```python
import functools

import jax
import jax.numpy as jnp
from jax import lax
from jax.experimental import pallas as pl
from jax.experimental.pallas import tpu as pltpu
from jax.sharding import PartitionSpec as P

GROUPS = 8
DEPTH = 64
TROWS = 4


def with_halo(block, sides, width):
    for axis, dim in sides:
        count = lax.axis_size(axis)
        forward = [(i, i + 1) for i in range(count - 1)]
        backward = [(target, source) for source, target in forward]
        low = lax.ppermute(
            lax.slice_in_dim(block, block.shape[dim] - width, None, axis=dim), axis, forward
        )
        high = lax.ppermute(lax.slice_in_dim(block, 0, width, axis=dim), axis, backward)
        block = jnp.concatenate([low, block, high], axis=dim)
    return block


def convolve_full(padded, kernel):
    rows_out = padded.shape[0] - 2
    depth_len = padded.shape[2]
    columns = padded.shape[3]
    framed = jnp.pad(padded, ((0, 0), (0, 0), (1, 1), (1, 1)))
    carried = jnp.zeros((rows_out, kernel.shape[-1], depth_len, columns), jnp.float32)
    for depth_off in range(3):
        for row_off in range(3):
            for col_off in range(3):
                window = framed[
                    row_off : row_off + rows_out,
                    :,
                    depth_off : depth_off + depth_len,
                    col_off : col_off + columns,
                ]
                carried = carried + jnp.einsum(
                    "rcdw,ce->redw",
                    window,
                    kernel[depth_off, row_off, col_off],
                    preferred_element_type=jnp.float32,
                )
    return carried


def convolve_final(padded, kernel):
    rows_out = padded.shape[0] - 2
    depth_len = padded.shape[2]
    columns = padded.shape[3]
    framed = jnp.pad(padded, ((0, 0), (0, 0), (1, 1), (1, 1)))
    carried = jnp.zeros((rows_out, depth_len, columns), jnp.float32)
    for depth_off in range(3):
        for row_off in range(3):
            for col_off in range(3):
                window = framed[
                    row_off : row_off + rows_out,
                    :,
                    depth_off : depth_off + depth_len,
                    col_off : col_off + columns,
                ]
                carried = carried + jnp.einsum(
                    "rcdw,c->rdw",
                    window,
                    kernel[depth_off, row_off, col_off],
                    preferred_element_type=jnp.float32,
                )
    return carried


def correlate_kernel(blk_ref, blocks_ref, table_ref, ref_ref, out_ref, arranged, products):
    chunk = 16
    slots = table_ref.shape[0] // blocks_ref.shape[2]
    width = blocks_ref.shape[2]
    channels = blocks_ref.shape[1]
    units = out_ref.shape[0] // GROUPS
    cap = units // ref_ref.shape[0]
    group_size = channels // GROUPS
    rows = chunk * channels

    def step(c, carry):
        for u in range(chunk):
            unit = c * chunk + u
            for w in range(slots):
                arranged[u * channels : (u + 1) * channels, w * width : (w + 1) * width] = blocks_ref[
                    blk_ref[unit * slots + w]
                ]
        warped = jnp.dot(arranged[...], table_ref[...], preferred_element_type=jnp.float32)
        warped = warped.astype(jnp.bfloat16).astype(jnp.float32)
        lanes = products.shape[0]
        for u in range(chunk):
            unit = c * chunk + u
            tile = ref_ref[unit // cap].astype(jnp.float32)
            for j in range(lanes):
                products[j, u * channels : (u + 1) * channels, :] = (
                    warped[u * channels : (u + 1) * channels, j * 128 : (j + 1) * 128]
                    * tile[:, j * 128 : (j + 1) * 128]
                )
        start = pl.multiple_of(c * (chunk * GROUPS), chunk * GROUPS)
        for j in range(lanes):
            total = products[j, pl.ds(0, rows // group_size, stride=group_size), :]
            for k in range(1, group_size):
                total = total + products[j, pl.ds(k, rows // group_size, stride=group_size), :]
            out_ref[pl.ds(start, chunk * GROUPS), j * 128 : (j + 1) * 128] = (
                total * (GROUPS / channels)
            ).astype(out_ref.dtype)
        return carry

    lax.fori_loop(0, units // chunk, step, 0, unroll=2)


def correlate(blk, blocks, table, refs, units):
    channels, width = blocks.shape[1], blocks.shape[2]
    tpix = table.shape[1]
    chunk = 16
    return pl.pallas_call(
        correlate_kernel,
        out_shape=jax.ShapeDtypeStruct((units * GROUPS, tpix), jnp.bfloat16),
        in_specs=[
            pl.BlockSpec(memory_space=pltpu.SMEM),
            pl.BlockSpec(memory_space=pltpu.VMEM),
            pl.BlockSpec(memory_space=pltpu.VMEM),
            pl.BlockSpec(memory_space=pltpu.VMEM),
        ],
        out_specs=pl.BlockSpec(memory_space=pltpu.VMEM),
        scratch_shapes=[
            pltpu.VMEM((chunk * channels, table.shape[0]), jnp.bfloat16),
            pltpu.VMEM((tpix // 128, chunk * channels, 128), jnp.float32),
        ],
    )(blk, blocks, table, refs)


def conv_body(x_ref, m_ref, out_ref, ends_ref, *, relu, rows, cols, groups, chunk):
    width = rows * cols
    outs = m_ref.shape[2]
    depth = x_ref.shape[0] // groups - 2
    lane = lax.broadcasted_iota(jnp.int32, (outs, width), 1) % cols
    for k in range(depth // chunk):
        acc = None
        for e in range(3):
            y = None
            for b in range(3):
                window = x_ref[k * chunk * groups : (k * chunk + chunk + 2) * groups, b * cols : b * cols + width]
                part = jnp.dot(m_ref[b, e], window, preferred_element_type=jnp.float32)
                y = part if y is None else y + part
            if e == 0:
                y = jnp.where(lane >= 1, pltpu.roll(y, 1, 1), 0.0)
            elif e == 2:
                y = jnp.where(lane <= cols - 2, pltpu.roll(y, width - 1, 1), 0.0)
            acc = y if acc is None else acc + y
        if relu:
            block = lax.broadcasted_iota(jnp.int32, (outs, width), 1) // cols
            outside = ((block == 0) & (ends_ref[0] > 0)) | ((block == rows - 1) & (ends_ref[1] > 0))
            acc = jnp.where(outside, 0.0, acc)
            out_ref[(k * chunk + 1) * outs // chunk : (k * chunk + chunk + 1) * outs // chunk, :] = (
                jnp.maximum(acc, 0.0).astype(out_ref.dtype)
            )
        else:
            for r in range(rows):
                out_ref[r, k * chunk : (k + 1) * chunk, :] = acc[:, r * cols : (r + 1) * cols]
    if relu:
        pad = jnp.zeros((outs // chunk, width), out_ref.dtype)
        out_ref[: outs // chunk, :] = pad
        out_ref[out_ref.shape[0] - outs // chunk :, :] = pad


def banded(kernel, chunk):
    groups = kernel.shape[3]
    cols = (chunk + 2) * groups
    taps = kernel.reshape((3, 9) + kernel.shape[3:])
    col = lax.iota(jnp.int32, cols)
    spread = (col[None, :] % groups == jnp.arange(groups)[:, None]).astype(kernel.dtype)
    if kernel.ndim == 5:
        outs = kernel.shape[4]
        rows = chunk * outs
        row = lax.iota(jnp.int32, rows)
        pick = (row[:, None] % outs == jnp.arange(outs)[None, :]).astype(kernel.dtype)
        lanes = jnp.einsum("xyio,ic->xyoc", taps, spread, preferred_element_type=jnp.float32)
        tiles = jnp.einsum(
            "ro,xyoc->xyrc", pick, lanes.astype(kernel.dtype), preferred_element_type=jnp.float32
        )
        depth_of_row = row // outs
    else:
        rows = chunk
        lanes = jnp.einsum("xyi,ic->xyc", taps, spread, preferred_element_type=jnp.float32)
        tiles = lanes[:, :, None, :]
        depth_of_row = lax.iota(jnp.int32, rows)
    band = col[None, None, :] // groups == depth_of_row[None, :, None] + jnp.arange(3)[:, None, None]
    mats = jnp.sum(jnp.where(band[:, None], tiles, 0.0), axis=0)
    return mats.astype(kernel.dtype).reshape(3, 3, rows, cols)


def conv_pair_kernel(
    ends_ref, low_ref, vol_ref, high_ref, m1_ref, m2_ref, out_ref, framed, hidden, *, rows, cols, groups
):
    halo = low_ref.shape[1]
    middle = vol_ref.shape[1]
    framed[:, :halo] = low_ref[...]
    framed[:, halo : halo + middle] = vol_ref[...]
    framed[:, halo + middle :] = high_ref[...]
    depth = framed.shape[0] // groups - 2
    first = m1_ref.shape[3] // groups - 2
    conv_body(
        framed, m1_ref, hidden, ends_ref, relu=True, rows=rows + 2, cols=cols, groups=groups, chunk=first
    )
    conv_body(
        hidden, m2_ref, out_ref, None, relu=False, rows=rows, cols=cols, groups=groups, chunk=depth
    )


def conv_pair(ends, low, volume, high, first, second, rows, cols):
    groups = second.shape[3] // (second.shape[2] + 2)
    depth = volume.shape[0] // groups - 2
    outs = first.shape[2] * depth // (first.shape[3] // groups - 2)
    vmem = pl.BlockSpec(memory_space=pltpu.VMEM)
    return pl.pallas_call(
        functools.partial(conv_pair_kernel, rows=rows, cols=cols, groups=groups),
        out_shape=jax.ShapeDtypeStruct((rows, depth, cols), jnp.float32),
        in_specs=[pl.BlockSpec(memory_space=pltpu.SMEM)] + [vmem] * 5,
        out_specs=vmem,
        scratch_shapes=[
            pltpu.VMEM((volume.shape[0], volume.shape[1] + low.shape[1] + high.shape[1]), volume.dtype),
            pltpu.VMEM(((depth + 2) * outs // depth, (rows + 2) * cols), jnp.bfloat16),
        ],
    )(ends, low, volume, high, first, second)


def halo_cols(block, cols):
    count = lax.axis_size("view")
    forward = [(i, i + 1) for i in range(count - 1)]
    backward = [(target, source) for source, target in forward]
    low = lax.ppermute(block[:, block.shape[1] - cols :], "view", forward)
    high = lax.ppermute(block[:, :cols], "view", backward)
    return jnp.concatenate([low, block, high], axis=1)


def gather_view(block):
    count = lax.axis_size("view")
    if count & (count - 1):
        return lax.all_to_all(
            jnp.broadcast_to(block, (count,) + block.shape[1:]), "view", 0, 0, tiled=True
        )
    index = lax.axis_index("view")
    gathered = block[0]
    level = 0
    stride = count // 2
    if count >= 4:
        top = count // 4
        parts = [gathered] + [
            lax.ppermute(gathered, "view", [(i, i ^ (m * top)) for i in range(count)])
            for m in (1, 2, 3)
        ]
        order = jnp.arange(4) ^ ((index // top) % 4)
        gathered = jnp.take(jnp.stack(parts), order, axis=0).reshape((2, 2) + gathered.shape)
        level = 2
        stride = top // 2
    while stride >= 1:
        other = lax.ppermute(gathered, "view", [(i, i ^ stride) for i in range(count)])
        low = (index // stride) % 2 == 0
        gathered = jnp.where(
            low, jnp.stack([gathered, other], axis=level), jnp.stack([other, gathered], axis=level)
        )
        level += 1
        stride //= 2
    return gathered.reshape((count,) + block.shape[1:])


def pad_rows(volume):
    return with_halo(volume, (("view", 0),), 1)


def body(
    src_feat,
    ref_feat,
    weight_table,
    src_block,
    table_index,
    block_count,
    depth_plane,
    kern_one,
    kern_two,
):
    owners = lax.axis_size("view")
    features = src_feat[0]
    channels, spix = features.shape
    slots, block_width, tpix = weight_table.shape
    blocks = features.reshape(channels, spix // block_width, block_width).transpose(1, 0, 2)
    units = src_block.shape[1]
    cap = units // owners
    counts = block_count[0]
    nblocks = spix // block_width
    blocks = jnp.concatenate([blocks, jnp.zeros_like(blocks[:1])], axis=0)
    matches = table_index[0][:, :, None] == jnp.arange(slots)[None, None, :]
    live = (jnp.arange(slots)[None, :] < counts[:, None])[:, :, None] & matches
    picked = jnp.sum(jnp.where(matches, src_block[0][:, :, None], 0), axis=1)
    alive = jnp.any(live, axis=1)
    blk = jnp.where(alive, picked, nblocks).reshape(-1).astype(jnp.int32)
    depth_code = jnp.where(counts > 0, depth_plane[0], -1).astype(jnp.bfloat16)

    tag_block = jnp.pad(depth_code, (0, channels * 128 - units)).reshape(channels, 128)
    ref_all = gather_view(jnp.concatenate([ref_feat[0], tag_block], axis=1)[None])
    corr_all = correlate(
        blk, blocks, weight_table.reshape(slots * block_width, tpix), ref_all, units
    )
    arriving = lax.all_to_all(
        corr_all.reshape(owners, cap * GROUPS, tpix),
        "view",
        split_axis=0,
        concat_axis=0,
        tiled=True,
    ).reshape(owners * cap, GROUPS, tpix)
    depth_tags = lax.dynamic_slice_in_dim(
        ref_all[:, :, tpix:].reshape(owners, channels * 128), lax.axis_index("view") * cap, cap, axis=1
    ).reshape(owners * cap)
    onehot = (
        depth_tags[None, :] == jnp.arange(DEPTH).astype(jnp.bfloat16)[:, None]
    ).astype(jnp.bfloat16)
    summed = jnp.einsum("dn,ngp->dgp", onehot, arriving, preferred_element_type=jnp.float32)
    tallies = jnp.sum(onehot.astype(jnp.float32), axis=1)
    cost_volume = (summed / jnp.maximum(tallies, 1.0)[:, None, None]).astype(jnp.bfloat16)
    columns = tpix // TROWS
    volume = cost_volume.reshape(DEPTH * GROUPS, TROWS * columns)
    volume = jnp.pad(volume, ((GROUPS, GROUPS), (0, 0)))
    count = lax.axis_size("view")
    place = lax.axis_index("view")
    ends = jnp.stack([place == 0, place == count - 1]).astype(jnp.int32)
    count = lax.axis_size("view")
    forward = [(i, i + 1) for i in range(count - 1)]
    backward = [(target, source) for source, target in forward]
    low = lax.ppermute(volume[:, volume.shape[1] - 2 * columns :], "view", forward)
    high = lax.ppermute(volume[:, : 2 * columns], "view", backward)
    scores = conv_pair(
        ends,
        low,
        volume,
        high,
        banded(kern_one, DEPTH // 4),
        banded(kern_two, DEPTH),
        TROWS,
        columns,
    )
    return scores


def solution(mesh):
    in_specs = (
        P(("scene", "view"), None, None),
        P(("scene", "view"), None, None),
        P(),
        P(("scene", "view"), None, None),
        P(("scene", "view"), None, None),
        P(("scene", "view"), None),
        P(("scene", "view"), None),
        P(),
        P(),
    )
    out_specs = P(("scene", "view"), None, None)
    return jax.shard_map(body, mesh=mesh, in_specs=in_specs, out_specs=out_specs, check_vma=False)
```

```python
import functools

import jax
import jax.numpy as jnp
from jax import lax
from jax.experimental import pallas as pl
from jax.experimental.pallas import tpu as pltpu
from jax.sharding import PartitionSpec as P

GROUPS = 8
DEPTH = 64
TROWS = 4


def with_halo(block, sides, width):
    for axis, dim in sides:
        count = lax.axis_size(axis)
        forward = [(i, i + 1) for i in range(count - 1)]
        backward = [(target, source) for source, target in forward]
        low = lax.ppermute(
            lax.slice_in_dim(block, block.shape[dim] - width, None, axis=dim), axis, forward
        )
        high = lax.ppermute(lax.slice_in_dim(block, 0, width, axis=dim), axis, backward)
        block = jnp.concatenate([low, block, high], axis=dim)
    return block


def convolve_full(padded, kernel):
    rows_out = padded.shape[0] - 2
    depth_len = padded.shape[2]
    columns = padded.shape[3]
    framed = jnp.pad(padded, ((0, 0), (0, 0), (1, 1), (1, 1)))
    carried = jnp.zeros((rows_out, kernel.shape[-1], depth_len, columns), jnp.float32)
    for depth_off in range(3):
        for row_off in range(3):
            for col_off in range(3):
                window = framed[
                    row_off : row_off + rows_out,
                    :,
                    depth_off : depth_off + depth_len,
                    col_off : col_off + columns,
                ]
                carried = carried + jnp.einsum(
                    "rcdw,ce->redw",
                    window,
                    kernel[depth_off, row_off, col_off],
                    preferred_element_type=jnp.float32,
                )
    return carried


def convolve_final(padded, kernel):
    rows_out = padded.shape[0] - 2
    depth_len = padded.shape[2]
    columns = padded.shape[3]
    framed = jnp.pad(padded, ((0, 0), (0, 0), (1, 1), (1, 1)))
    carried = jnp.zeros((rows_out, depth_len, columns), jnp.float32)
    for depth_off in range(3):
        for row_off in range(3):
            for col_off in range(3):
                window = framed[
                    row_off : row_off + rows_out,
                    :,
                    depth_off : depth_off + depth_len,
                    col_off : col_off + columns,
                ]
                carried = carried + jnp.einsum(
                    "rcdw,c->rdw",
                    window,
                    kernel[depth_off, row_off, col_off],
                    preferred_element_type=jnp.float32,
                )
    return carried


def correlate_kernel(blk_ref, blocks_ref, table_ref, ref_ref, out_ref, arranged, products):
    chunk = 16
    slots = table_ref.shape[0] // blocks_ref.shape[2]
    width = blocks_ref.shape[2]
    channels = blocks_ref.shape[1]
    units = out_ref.shape[0] // GROUPS
    cap = units // ref_ref.shape[0]
    group_size = channels // GROUPS
    rows = chunk * channels

    def step(c, carry):
        for u in range(chunk):
            unit = c * chunk + u
            for w in range(slots):
                arranged[u * channels : (u + 1) * channels, w * width : (w + 1) * width] = blocks_ref[
                    blk_ref[unit * slots + w]
                ]
        warped = jnp.dot(arranged[...], table_ref[...], preferred_element_type=jnp.float32)
        warped = warped.astype(jnp.bfloat16).astype(jnp.float32)
        lanes = products.shape[0]
        for u in range(chunk):
            unit = c * chunk + u
            tile = ref_ref[unit // cap].astype(jnp.float32)
            for j in range(lanes):
                products[j, u * channels : (u + 1) * channels, :] = (
                    warped[u * channels : (u + 1) * channels, j * 128 : (j + 1) * 128]
                    * tile[:, j * 128 : (j + 1) * 128]
                )
        start = pl.multiple_of(c * (chunk * GROUPS), chunk * GROUPS)
        for j in range(lanes):
            total = products[j, pl.ds(0, rows // group_size, stride=group_size), :]
            for k in range(1, group_size):
                total = total + products[j, pl.ds(k, rows // group_size, stride=group_size), :]
            out_ref[pl.ds(start, chunk * GROUPS), j * 128 : (j + 1) * 128] = (
                total * (GROUPS / channels)
            ).astype(out_ref.dtype)
        return carry

    lax.fori_loop(0, units // chunk, step, 0, unroll=2)


def correlate(blk, blocks, table, refs, units):
    channels, width = blocks.shape[1], blocks.shape[2]
    tpix = table.shape[1]
    chunk = 16
    return pl.pallas_call(
        correlate_kernel,
        out_shape=jax.ShapeDtypeStruct((units * GROUPS, tpix), jnp.bfloat16),
        in_specs=[
            pl.BlockSpec(memory_space=pltpu.SMEM),
            pl.BlockSpec(memory_space=pltpu.VMEM),
            pl.BlockSpec(memory_space=pltpu.VMEM),
            pl.BlockSpec(memory_space=pltpu.VMEM),
        ],
        out_specs=pl.BlockSpec(memory_space=pltpu.VMEM),
        scratch_shapes=[
            pltpu.VMEM((chunk * channels, table.shape[0]), jnp.bfloat16),
            pltpu.VMEM((tpix // 128, chunk * channels, 128), jnp.float32),
        ],
    )(blk, blocks, table, refs)


def conv_body(x_ref, m_ref, out_ref, ends_ref, *, relu, rows, cols, groups, chunk):
    width = rows * cols
    outs = m_ref.shape[2]
    depth = x_ref.shape[0] // groups - 2
    lane = lax.broadcasted_iota(jnp.int32, (outs, width), 1) % cols
    for k in range(depth // chunk):
        acc = None
        for e in range(3):
            y = None
            for b in range(3):
                window = x_ref[k * chunk * groups : (k * chunk + chunk + 2) * groups, b * cols : b * cols + width]
                part = jnp.dot(m_ref[b, e], window, preferred_element_type=jnp.float32)
                y = part if y is None else y + part
            if e == 0:
                y = jnp.where(lane >= 1, pltpu.roll(y, 1, 1), 0.0)
            elif e == 2:
                y = jnp.where(lane <= cols - 2, pltpu.roll(y, width - 1, 1), 0.0)
            acc = y if acc is None else acc + y
        if relu:
            block = lax.broadcasted_iota(jnp.int32, (outs, width), 1) // cols
            outside = ((block == 0) & (ends_ref[0] > 0)) | ((block == rows - 1) & (ends_ref[1] > 0))
            acc = jnp.where(outside, 0.0, acc)
            out_ref[(k * chunk + 1) * outs // chunk : (k * chunk + chunk + 1) * outs // chunk, :] = (
                jnp.maximum(acc, 0.0).astype(out_ref.dtype)
            )
        else:
            for r in range(rows):
                out_ref[r, k * chunk : (k + 1) * chunk, :] = acc[:, r * cols : (r + 1) * cols]
    if relu:
        pad = jnp.zeros((outs // chunk, width), out_ref.dtype)
        out_ref[: outs // chunk, :] = pad
        out_ref[out_ref.shape[0] - outs // chunk :, :] = pad


def banded(kernel, chunk):
    groups = kernel.shape[3]
    cols = (chunk + 2) * groups
    taps = kernel.reshape((3, 9) + kernel.shape[3:])
    col = lax.iota(jnp.int32, cols)
    spread = (col[None, :] % groups == jnp.arange(groups)[:, None]).astype(kernel.dtype)
    if kernel.ndim == 5:
        outs = kernel.shape[4]
        rows = chunk * outs
        row = lax.iota(jnp.int32, rows)
        pick = (row[:, None] % outs == jnp.arange(outs)[None, :]).astype(kernel.dtype)
        lanes = jnp.einsum("xyio,ic->xyoc", taps, spread, preferred_element_type=jnp.float32)
        tiles = jnp.einsum(
            "ro,xyoc->xyrc", pick, lanes.astype(kernel.dtype), preferred_element_type=jnp.float32
        )
        depth_of_row = row // outs
    else:
        rows = chunk
        lanes = jnp.einsum("xyi,ic->xyc", taps, spread, preferred_element_type=jnp.float32)
        tiles = lanes[:, :, None, :]
        depth_of_row = lax.iota(jnp.int32, rows)
    band = col[None, None, :] // groups == depth_of_row[None, :, None] + jnp.arange(3)[:, None, None]
    mats = jnp.sum(jnp.where(band[:, None], tiles, 0.0), axis=0)
    return mats.astype(kernel.dtype).reshape(3, 3, rows, cols)


def conv_pair_kernel(
    ends_ref, low_ref, vol_ref, high_ref, m1_ref, m2_ref, out_ref, framed, hidden, *, rows, cols, groups
):
    halo = low_ref.shape[1]
    middle = vol_ref.shape[1]
    framed[:, :halo] = low_ref[...]
    framed[:, halo : halo + middle] = vol_ref[...]
    framed[:, halo + middle :] = high_ref[...]
    depth = framed.shape[0] // groups - 2
    first = m1_ref.shape[3] // groups - 2
    conv_body(
        framed, m1_ref, hidden, ends_ref, relu=True, rows=rows + 2, cols=cols, groups=groups, chunk=first
    )
    conv_body(
        hidden,
        m2_ref,
        out_ref,
        None,
        relu=False,
        rows=rows,
        cols=cols,
        groups=groups,
        chunk=m2_ref.shape[2],
    )


def conv_pair(ends, low, volume, high, first, second, rows, cols):
    groups = second.shape[3] // (second.shape[2] + 2)
    depth = volume.shape[0] // groups - 2
    outs = first.shape[2] * depth // (first.shape[3] // groups - 2)
    vmem = pl.BlockSpec(memory_space=pltpu.VMEM)
    return pl.pallas_call(
        functools.partial(conv_pair_kernel, rows=rows, cols=cols, groups=groups),
        out_shape=jax.ShapeDtypeStruct((rows, depth, cols), jnp.float32),
        in_specs=[pl.BlockSpec(memory_space=pltpu.SMEM)] + [vmem] * 5,
        out_specs=vmem,
        scratch_shapes=[
            pltpu.VMEM((volume.shape[0], volume.shape[1] + low.shape[1] + high.shape[1]), volume.dtype),
            pltpu.VMEM(((depth + 2) * outs // depth, (rows + 2) * cols), jnp.bfloat16),
        ],
    )(ends, low, volume, high, first, second)


def halo_cols(block, cols):
    count = lax.axis_size("view")
    forward = [(i, i + 1) for i in range(count - 1)]
    backward = [(target, source) for source, target in forward]
    low = lax.ppermute(block[:, block.shape[1] - cols :], "view", forward)
    high = lax.ppermute(block[:, :cols], "view", backward)
    return jnp.concatenate([low, block, high], axis=1)


def gather_view(block):
    count = lax.axis_size("view")
    if count & (count - 1):
        return lax.all_to_all(
            jnp.broadcast_to(block, (count,) + block.shape[1:]), "view", 0, 0, tiled=True
        )
    index = lax.axis_index("view")
    gathered = block[0]
    level = 0
    stride = count // 2
    if count >= 4:
        top = count // 4
        parts = [gathered] + [
            lax.ppermute(gathered, "view", [(i, i ^ (m * top)) for i in range(count)])
            for m in (1, 2, 3)
        ]
        order = jnp.arange(4) ^ ((index // top) % 4)
        gathered = jnp.take(jnp.stack(parts), order, axis=0).reshape((2, 2) + gathered.shape)
        level = 2
        stride = top // 2
    while stride >= 1:
        other = lax.ppermute(gathered, "view", [(i, i ^ stride) for i in range(count)])
        low = (index // stride) % 2 == 0
        gathered = jnp.where(
            low, jnp.stack([gathered, other], axis=level), jnp.stack([other, gathered], axis=level)
        )
        level += 1
        stride //= 2
    return gathered.reshape((count,) + block.shape[1:])


def pad_rows(volume):
    return with_halo(volume, (("view", 0),), 1)


def body(
    src_feat,
    ref_feat,
    weight_table,
    src_block,
    table_index,
    block_count,
    depth_plane,
    kern_one,
    kern_two,
):
    owners = lax.axis_size("view")
    features = src_feat[0]
    channels, spix = features.shape
    slots, block_width, tpix = weight_table.shape
    blocks = features.reshape(channels, spix // block_width, block_width).transpose(1, 0, 2)
    units = src_block.shape[1]
    cap = units // owners
    counts = block_count[0]
    nblocks = spix // block_width
    blocks = jnp.concatenate([blocks, jnp.zeros_like(blocks[:1])], axis=0)
    matches = table_index[0][:, :, None] == jnp.arange(slots)[None, None, :]
    live = (jnp.arange(slots)[None, :] < counts[:, None])[:, :, None] & matches
    picked = jnp.sum(jnp.where(matches, src_block[0][:, :, None], 0), axis=1)
    alive = jnp.any(live, axis=1)
    blk = jnp.where(alive, picked, nblocks).reshape(-1).astype(jnp.int32)
    depth_code = jnp.where(counts > 0, depth_plane[0], -1).astype(jnp.bfloat16)

    tag_block = jnp.pad(depth_code, (0, channels * 128 - units)).reshape(channels, 128)
    ref_all = gather_view(jnp.concatenate([ref_feat[0], tag_block], axis=1)[None])
    corr_all = correlate(
        blk, blocks, weight_table.reshape(slots * block_width, tpix), ref_all, units
    )
    arriving = lax.all_to_all(
        corr_all.reshape(owners, cap * GROUPS, tpix),
        "view",
        split_axis=0,
        concat_axis=0,
        tiled=True,
    ).reshape(owners * cap, GROUPS, tpix)
    depth_tags = lax.dynamic_slice_in_dim(
        ref_all[:, :, tpix:].reshape(owners, channels * 128), lax.axis_index("view") * cap, cap, axis=1
    ).reshape(owners * cap)
    onehot = (
        depth_tags[None, :] == jnp.arange(DEPTH).astype(jnp.bfloat16)[:, None]
    ).astype(jnp.bfloat16)
    summed = jnp.einsum("dn,ngp->dgp", onehot, arriving, preferred_element_type=jnp.float32)
    tallies = jnp.sum(onehot.astype(jnp.float32), axis=1)
    cost_volume = (summed / jnp.maximum(tallies, 1.0)[:, None, None]).astype(jnp.bfloat16)
    columns = tpix // TROWS
    volume = cost_volume.reshape(DEPTH * GROUPS, TROWS * columns)
    volume = jnp.pad(volume, ((GROUPS, GROUPS), (0, 0)))
    count = lax.axis_size("view")
    place = lax.axis_index("view")
    ends = jnp.stack([place == 0, place == count - 1]).astype(jnp.int32)
    count = lax.axis_size("view")
    forward = [(i, i + 1) for i in range(count - 1)]
    backward = [(target, source) for source, target in forward]
    low = lax.ppermute(volume[:, volume.shape[1] - 2 * columns :], "view", forward)
    high = lax.ppermute(volume[:, : 2 * columns], "view", backward)
    scores = conv_pair(
        ends,
        low,
        volume,
        high,
        banded(kern_one, DEPTH // 4),
        banded(kern_two, DEPTH // 4),
        TROWS,
        columns,
    )
    return scores


def solution(mesh):
    in_specs = (
        P(("scene", "view"), None, None),
        P(("scene", "view"), None, None),
        P(),
        P(("scene", "view"), None, None),
        P(("scene", "view"), None, None),
        P(("scene", "view"), None),
        P(("scene", "view"), None),
        P(),
        P(),
    )
    out_specs = P(("scene", "view"), None, None)
    return jax.shard_map(body, mesh=mesh, in_specs=in_specs, out_specs=out_specs, check_vma=False)
```

```python
import functools

import jax
import jax.numpy as jnp
from jax import lax
from jax.experimental import pallas as pl
from jax.experimental.pallas import tpu as pltpu
from jax.sharding import PartitionSpec as P

GROUPS = 8
DEPTH = 64
TROWS = 4


def with_halo(block, sides, width):
    for axis, dim in sides:
        count = lax.axis_size(axis)
        forward = [(i, i + 1) for i in range(count - 1)]
        backward = [(target, source) for source, target in forward]
        low = lax.ppermute(
            lax.slice_in_dim(block, block.shape[dim] - width, None, axis=dim), axis, forward
        )
        high = lax.ppermute(lax.slice_in_dim(block, 0, width, axis=dim), axis, backward)
        block = jnp.concatenate([low, block, high], axis=dim)
    return block


def convolve_full(padded, kernel):
    rows_out = padded.shape[0] - 2
    depth_len = padded.shape[2]
    columns = padded.shape[3]
    framed = jnp.pad(padded, ((0, 0), (0, 0), (1, 1), (1, 1)))
    carried = jnp.zeros((rows_out, kernel.shape[-1], depth_len, columns), jnp.float32)
    for depth_off in range(3):
        for row_off in range(3):
            for col_off in range(3):
                window = framed[
                    row_off : row_off + rows_out,
                    :,
                    depth_off : depth_off + depth_len,
                    col_off : col_off + columns,
                ]
                carried = carried + jnp.einsum(
                    "rcdw,ce->redw",
                    window,
                    kernel[depth_off, row_off, col_off],
                    preferred_element_type=jnp.float32,
                )
    return carried


def convolve_final(padded, kernel):
    rows_out = padded.shape[0] - 2
    depth_len = padded.shape[2]
    columns = padded.shape[3]
    framed = jnp.pad(padded, ((0, 0), (0, 0), (1, 1), (1, 1)))
    carried = jnp.zeros((rows_out, depth_len, columns), jnp.float32)
    for depth_off in range(3):
        for row_off in range(3):
            for col_off in range(3):
                window = framed[
                    row_off : row_off + rows_out,
                    :,
                    depth_off : depth_off + depth_len,
                    col_off : col_off + columns,
                ]
                carried = carried + jnp.einsum(
                    "rcdw,c->rdw",
                    window,
                    kernel[depth_off, row_off, col_off],
                    preferred_element_type=jnp.float32,
                )
    return carried


def correlate_kernel(blk_ref, blocks_ref, table_ref, ref_ref, out_ref, arranged, products):
    chunk = 16
    slots = table_ref.shape[0] // blocks_ref.shape[2]
    width = blocks_ref.shape[2]
    channels = blocks_ref.shape[1]
    units = out_ref.shape[0] // GROUPS
    cap = units // ref_ref.shape[0]
    group_size = channels // GROUPS
    rows = chunk * channels

    def step(c, carry):
        for u in range(chunk):
            unit = c * chunk + u
            for w in range(slots):
                arranged[u * channels : (u + 1) * channels, w * width : (w + 1) * width] = blocks_ref[
                    blk_ref[unit * slots + w]
                ]
        warped = jnp.dot(arranged[...], table_ref[...], preferred_element_type=jnp.float32)
        warped = warped.astype(jnp.bfloat16).astype(jnp.float32)
        lanes = products.shape[0]
        for u in range(chunk):
            unit = c * chunk + u
            tile = ref_ref[unit // cap].astype(jnp.float32)
            for j in range(lanes):
                products[j, u * channels : (u + 1) * channels, :] = (
                    warped[u * channels : (u + 1) * channels, j * 128 : (j + 1) * 128]
                    * tile[:, j * 128 : (j + 1) * 128]
                )
        start = pl.multiple_of(c * (chunk * GROUPS), chunk * GROUPS)
        for j in range(lanes):
            total = products[j, pl.ds(0, rows // group_size, stride=group_size), :]
            for k in range(1, group_size):
                total = total + products[j, pl.ds(k, rows // group_size, stride=group_size), :]
            out_ref[pl.ds(start, chunk * GROUPS), j * 128 : (j + 1) * 128] = (
                total * (GROUPS / channels)
            ).astype(out_ref.dtype)
        return carry

    lax.fori_loop(0, units // chunk, step, 0, unroll=2)


def correlate(blk, blocks, table, refs, units):
    channels, width = blocks.shape[1], blocks.shape[2]
    tpix = table.shape[1]
    chunk = 16
    return pl.pallas_call(
        correlate_kernel,
        out_shape=jax.ShapeDtypeStruct((units * GROUPS, tpix), jnp.bfloat16),
        in_specs=[
            pl.BlockSpec(memory_space=pltpu.SMEM),
            pl.BlockSpec(memory_space=pltpu.VMEM),
            pl.BlockSpec(memory_space=pltpu.VMEM),
            pl.BlockSpec(memory_space=pltpu.VMEM),
        ],
        out_specs=pl.BlockSpec(memory_space=pltpu.VMEM),
        scratch_shapes=[
            pltpu.VMEM((chunk * channels, table.shape[0]), jnp.bfloat16),
            pltpu.VMEM((tpix // 128, chunk * channels, 128), jnp.float32),
        ],
    )(blk, blocks, table, refs)


def conv_body(x_ref, m_ref, out_ref, ends_ref, *, relu, rows, cols, groups, chunk):
    width = rows * cols
    outs = m_ref.shape[2]
    depth = x_ref.shape[0] // groups - 2
    lane = lax.broadcasted_iota(jnp.int32, (outs, width), 1) % cols
    for k in range(depth // chunk):
        acc = None
        for e in range(3):
            y = None
            for b in range(3):
                window = x_ref[k * chunk * groups : (k * chunk + chunk + 2) * groups, b * cols : b * cols + width]
                part = jnp.dot(m_ref[b, e], window, preferred_element_type=jnp.float32)
                y = part if y is None else y + part
            if e == 0:
                y = jnp.where(lane >= 1, pltpu.roll(y, 1, 1), 0.0)
            elif e == 2:
                y = jnp.where(lane <= cols - 2, pltpu.roll(y, width - 1, 1), 0.0)
            acc = y if acc is None else acc + y
        if relu:
            block = lax.broadcasted_iota(jnp.int32, (outs, width), 1) // cols
            outside = ((block == 0) & (ends_ref[0] > 0)) | ((block == rows - 1) & (ends_ref[1] > 0))
            acc = jnp.where(outside, 0.0, acc)
            out_ref[(k * chunk + 1) * outs // chunk : (k * chunk + chunk + 1) * outs // chunk, :] = (
                jnp.maximum(acc, 0.0).astype(out_ref.dtype)
            )
        else:
            for r in range(rows):
                out_ref[r, k * chunk : (k + 1) * chunk, :] = acc[:, r * cols : (r + 1) * cols]
    if relu:
        pad = jnp.zeros((outs // chunk, width), out_ref.dtype)
        out_ref[: outs // chunk, :] = pad
        out_ref[out_ref.shape[0] - outs // chunk :, :] = pad


def banded(kernel, chunk):
    groups = kernel.shape[3]
    cols = (chunk + 2) * groups
    taps = kernel.reshape((3, 9) + kernel.shape[3:])
    col = lax.iota(jnp.int32, cols)
    spread = (col[None, :] % groups == jnp.arange(groups)[:, None]).astype(kernel.dtype)
    if kernel.ndim == 5:
        outs = kernel.shape[4]
        rows = chunk * outs
        row = lax.iota(jnp.int32, rows)
        pick = (row[:, None] % outs == jnp.arange(outs)[None, :]).astype(kernel.dtype)
        lanes = jnp.einsum("xyio,ic->xyoc", taps, spread, preferred_element_type=jnp.float32)
        tiles = jnp.einsum(
            "ro,xyoc->xyrc", pick, lanes.astype(kernel.dtype), preferred_element_type=jnp.float32
        )
        depth_of_row = row // outs
    else:
        rows = chunk
        lanes = jnp.einsum("xyi,ic->xyc", taps, spread, preferred_element_type=jnp.float32)
        tiles = lanes[:, :, None, :]
        depth_of_row = lax.iota(jnp.int32, rows)
    band = col[None, None, :] // groups == depth_of_row[None, :, None] + jnp.arange(3)[:, None, None]
    mats = jnp.sum(jnp.where(band[:, None], tiles, 0.0), axis=0)
    return mats.astype(kernel.dtype).reshape(3, 3, rows, cols)


def conv_pair_kernel(
    ends_ref, low_ref, vol_ref, high_ref, m1_ref, m2_ref, out_ref, framed, hidden, *, rows, cols, groups
):
    halo = low_ref.shape[1]
    middle = vol_ref.shape[1]
    framed[:, :halo] = low_ref[...]
    framed[:, halo : halo + middle] = vol_ref[...]
    framed[:, halo + middle :] = high_ref[...]
    depth = framed.shape[0] // groups - 2
    first = m1_ref.shape[3] // groups - 2
    conv_body(
        framed, m1_ref, hidden, ends_ref, relu=True, rows=rows + 2, cols=cols, groups=groups, chunk=first
    )
    conv_body(
        hidden,
        m2_ref,
        out_ref,
        None,
        relu=False,
        rows=rows,
        cols=cols,
        groups=groups,
        chunk=m2_ref.shape[2],
    )


def conv_pair(ends, low, volume, high, first, second, rows, cols):
    groups = second.shape[3] // (second.shape[2] + 2)
    depth = volume.shape[0] // groups - 2
    outs = first.shape[2] * depth // (first.shape[3] // groups - 2)
    vmem = pl.BlockSpec(memory_space=pltpu.VMEM)
    return pl.pallas_call(
        functools.partial(conv_pair_kernel, rows=rows, cols=cols, groups=groups),
        out_shape=jax.ShapeDtypeStruct((rows, depth, cols), jnp.float32),
        in_specs=[pl.BlockSpec(memory_space=pltpu.SMEM)] + [vmem] * 5,
        out_specs=vmem,
        scratch_shapes=[
            pltpu.VMEM((volume.shape[0], volume.shape[1] + low.shape[1] + high.shape[1]), volume.dtype),
            pltpu.VMEM(((depth + 2) * outs // depth, (rows + 2) * cols), jnp.bfloat16),
        ],
    )(ends, low, volume, high, first, second)


def halo_cols(block, cols):
    count = lax.axis_size("view")
    forward = [(i, i + 1) for i in range(count - 1)]
    backward = [(target, source) for source, target in forward]
    low = lax.ppermute(block[:, block.shape[1] - cols :], "view", forward)
    high = lax.ppermute(block[:, :cols], "view", backward)
    return jnp.concatenate([low, block, high], axis=1)


def gather_view(block):
    count = lax.axis_size("view")
    if count & (count - 1):
        return lax.all_to_all(
            jnp.broadcast_to(block, (count,) + block.shape[1:]), "view", 0, 0, tiled=True
        )
    index = lax.axis_index("view")
    gathered = block[0]
    level = 0
    stride = count // 2
    if count >= 4:
        top = count // 4
        parts = [gathered] + [
            lax.ppermute(gathered, "view", [(i, i ^ (m * top)) for i in range(count)])
            for m in (1, 2, 3)
        ]
        order = jnp.arange(4) ^ ((index // top) % 4)
        gathered = jnp.take(jnp.stack(parts), order, axis=0).reshape((2, 2) + gathered.shape)
        level = 2
        stride = top // 2
    while stride >= 1:
        other = lax.ppermute(gathered, "view", [(i, i ^ stride) for i in range(count)])
        low = (index // stride) % 2 == 0
        gathered = jnp.where(
            low, jnp.stack([gathered, other], axis=level), jnp.stack([other, gathered], axis=level)
        )
        level += 1
        stride //= 2
    return gathered.reshape((count,) + block.shape[1:])


def pad_rows(volume):
    return with_halo(volume, (("view", 0),), 1)


def body(
    src_feat,
    ref_feat,
    weight_table,
    src_block,
    table_index,
    block_count,
    depth_plane,
    kern_one,
    kern_two,
):
    owners = lax.axis_size("view")
    features = src_feat[0]
    channels, spix = features.shape
    slots, block_width, tpix = weight_table.shape
    blocks = features.reshape(channels, spix // block_width, block_width).transpose(1, 0, 2)
    units = src_block.shape[1]
    cap = units // owners
    counts = block_count[0]
    nblocks = spix // block_width
    blocks = jnp.concatenate([blocks, jnp.zeros_like(blocks[:1])], axis=0)
    matches = table_index[0][:, :, None] == jnp.arange(slots)[None, None, :]
    live = (jnp.arange(slots)[None, :] < counts[:, None])[:, :, None] & matches
    picked = jnp.sum(jnp.where(matches, src_block[0][:, :, None], 0), axis=1)
    alive = jnp.any(live, axis=1)
    blk = jnp.where(alive, picked, nblocks).reshape(-1).astype(jnp.int32)
    depth_code = jnp.where(counts > 0, depth_plane[0], -1).astype(jnp.bfloat16)

    tag_block = jnp.pad(depth_code, (0, channels * 128 - units)).reshape(channels, 128)
    ref_all = gather_view(jnp.concatenate([ref_feat[0], tag_block], axis=1)[None])
    ref_all, first, second = lax.optimization_barrier(
        (ref_all, banded(kern_one, DEPTH // 4), banded(kern_two, DEPTH // 4))
    )
    corr_all = correlate(
        blk, blocks, weight_table.reshape(slots * block_width, tpix), ref_all, units
    )
    arriving = lax.all_to_all(
        corr_all.reshape(owners, cap * GROUPS, tpix),
        "view",
        split_axis=0,
        concat_axis=0,
        tiled=True,
    ).reshape(owners * cap, GROUPS, tpix)
    depth_tags = lax.dynamic_slice_in_dim(
        ref_all[:, :, tpix:].reshape(owners, channels * 128), lax.axis_index("view") * cap, cap, axis=1
    ).reshape(owners * cap)
    labels = jnp.arange(-1, DEPTH + 1).at[0].set(-2)
    onehot = (
        depth_tags[None, :] == labels.astype(jnp.bfloat16)[:, None]
    ).astype(jnp.bfloat16)
    summed = jnp.einsum("dn,ngp->dgp", onehot, arriving, preferred_element_type=jnp.float32)
    tallies = jnp.sum(onehot.astype(jnp.float32), axis=1)
    cost_volume = (summed / jnp.maximum(tallies, 1.0)[:, None, None]).astype(jnp.bfloat16)
    columns = tpix // TROWS
    volume = cost_volume.reshape((DEPTH + 2) * GROUPS, TROWS * columns)
    count = lax.axis_size("view")
    place = lax.axis_index("view")
    ends = jnp.stack([place == 0, place == count - 1]).astype(jnp.int32)
    count = lax.axis_size("view")
    forward = [(i, i + 1) for i in range(count - 1)]
    backward = [(target, source) for source, target in forward]
    low = lax.ppermute(volume[:, volume.shape[1] - 2 * columns :], "view", forward)
    high = lax.ppermute(volume[:, : 2 * columns], "view", backward)
    scores = conv_pair(
        ends,
        low,
        volume,
        high,
        first,
        second,
        TROWS,
        columns,
    )
    return scores


def solution(mesh):
    in_specs = (
        P(("scene", "view"), None, None),
        P(("scene", "view"), None, None),
        P(),
        P(("scene", "view"), None, None),
        P(("scene", "view"), None, None),
        P(("scene", "view"), None),
        P(("scene", "view"), None),
        P(),
        P(),
    )
    out_specs = P(("scene", "view"), None, None)
    return jax.shard_map(body, mesh=mesh, in_specs=in_specs, out_specs=out_specs, check_vma=False)
```

```python
import functools

import jax
import jax.numpy as jnp
from jax import lax
from jax.experimental import pallas as pl
from jax.experimental.pallas import tpu as pltpu
from jax.sharding import PartitionSpec as P

GROUPS = 8
DEPTH = 64
TROWS = 4


def with_halo(block, sides, width):
    for axis, dim in sides:
        count = lax.axis_size(axis)
        forward = [(i, i + 1) for i in range(count - 1)]
        backward = [(target, source) for source, target in forward]
        low = lax.ppermute(
            lax.slice_in_dim(block, block.shape[dim] - width, None, axis=dim), axis, forward
        )
        high = lax.ppermute(lax.slice_in_dim(block, 0, width, axis=dim), axis, backward)
        block = jnp.concatenate([low, block, high], axis=dim)
    return block


def convolve_full(padded, kernel):
    rows_out = padded.shape[0] - 2
    depth_len = padded.shape[2]
    columns = padded.shape[3]
    framed = jnp.pad(padded, ((0, 0), (0, 0), (1, 1), (1, 1)))
    carried = jnp.zeros((rows_out, kernel.shape[-1], depth_len, columns), jnp.float32)
    for depth_off in range(3):
        for row_off in range(3):
            for col_off in range(3):
                window = framed[
                    row_off : row_off + rows_out,
                    :,
                    depth_off : depth_off + depth_len,
                    col_off : col_off + columns,
                ]
                carried = carried + jnp.einsum(
                    "rcdw,ce->redw",
                    window,
                    kernel[depth_off, row_off, col_off],
                    preferred_element_type=jnp.float32,
                )
    return carried


def convolve_final(padded, kernel):
    rows_out = padded.shape[0] - 2
    depth_len = padded.shape[2]
    columns = padded.shape[3]
    framed = jnp.pad(padded, ((0, 0), (0, 0), (1, 1), (1, 1)))
    carried = jnp.zeros((rows_out, depth_len, columns), jnp.float32)
    for depth_off in range(3):
        for row_off in range(3):
            for col_off in range(3):
                window = framed[
                    row_off : row_off + rows_out,
                    :,
                    depth_off : depth_off + depth_len,
                    col_off : col_off + columns,
                ]
                carried = carried + jnp.einsum(
                    "rcdw,c->rdw",
                    window,
                    kernel[depth_off, row_off, col_off],
                    preferred_element_type=jnp.float32,
                )
    return carried


def correlate_kernel(blk_ref, blocks_ref, table_ref, ref_ref, out_ref, arranged, products):
    chunk = 16
    slots = table_ref.shape[0] // blocks_ref.shape[2]
    width = blocks_ref.shape[2]
    channels = blocks_ref.shape[1]
    units = out_ref.shape[0] // GROUPS
    cap = units // ref_ref.shape[0]
    group_size = channels // GROUPS
    rows = chunk * channels

    def step(c, carry):
        for u in range(chunk):
            unit = c * chunk + u
            for w in range(slots):
                arranged[u * channels : (u + 1) * channels, w * width : (w + 1) * width] = blocks_ref[
                    blk_ref[unit * slots + w]
                ]
        warped = jnp.dot(arranged[...], table_ref[...], preferred_element_type=jnp.float32)
        warped = warped.astype(jnp.bfloat16).astype(jnp.float32)
        lanes = products.shape[0]
        for u in range(chunk):
            unit = c * chunk + u
            tile = ref_ref[unit // cap].astype(jnp.float32)
            for j in range(lanes):
                products[j, u * channels : (u + 1) * channels, :] = (
                    warped[u * channels : (u + 1) * channels, j * 128 : (j + 1) * 128]
                    * tile[:, j * 128 : (j + 1) * 128]
                )
        start = pl.multiple_of(c * (chunk * GROUPS), chunk * GROUPS)
        for j in range(lanes):
            total = products[j, pl.ds(0, rows // group_size, stride=group_size), :]
            for k in range(1, group_size):
                total = total + products[j, pl.ds(k, rows // group_size, stride=group_size), :]
            out_ref[pl.ds(start, chunk * GROUPS), j * 128 : (j + 1) * 128] = (
                total * (GROUPS / channels)
            ).astype(out_ref.dtype)
        return carry

    lax.fori_loop(0, units // chunk, step, 0, unroll=2)


def correlate(blk, blocks, table, refs, units):
    channels, width = blocks.shape[1], blocks.shape[2]
    tpix = table.shape[1]
    chunk = 16
    return pl.pallas_call(
        correlate_kernel,
        out_shape=jax.ShapeDtypeStruct((units * GROUPS, tpix), jnp.bfloat16),
        in_specs=[
            pl.BlockSpec(memory_space=pltpu.SMEM),
            pl.BlockSpec(memory_space=pltpu.VMEM),
            pl.BlockSpec(memory_space=pltpu.VMEM),
            pl.BlockSpec(memory_space=pltpu.VMEM),
        ],
        out_specs=pl.BlockSpec(memory_space=pltpu.VMEM),
        scratch_shapes=[
            pltpu.VMEM((chunk * channels, table.shape[0]), jnp.bfloat16),
            pltpu.VMEM((tpix // 128, chunk * channels, 128), jnp.float32),
        ],
    )(blk, blocks, table, refs)


def conv_body(x_ref, m_ref, out_ref, ends_ref, *, relu, rows, cols, groups, chunk):
    width = rows * cols
    outs = m_ref.shape[2]
    depth = x_ref.shape[0] // groups - 2
    lane = lax.broadcasted_iota(jnp.int32, (outs, width), 1) % cols
    for k in range(depth // chunk):
        acc = None
        for e in range(3):
            y = None
            for b in range(3):
                window = x_ref[k * chunk * groups : (k * chunk + chunk + 2) * groups, b * cols : b * cols + width]
                part = jnp.dot(m_ref[b, e], window, preferred_element_type=jnp.float32)
                y = part if y is None else y + part
            if e == 0:
                y = jnp.where(lane >= 1, pltpu.roll(y, 1, 1), 0.0)
            elif e == 2:
                y = jnp.where(lane <= cols - 2, pltpu.roll(y, width - 1, 1), 0.0)
            acc = y if acc is None else acc + y
        if relu:
            block = lax.broadcasted_iota(jnp.int32, (outs, width), 1) // cols
            outside = ((block == 0) & (ends_ref[0] > 0)) | ((block == rows - 1) & (ends_ref[1] > 0))
            acc = jnp.where(outside, 0.0, acc)
            out_ref[(k * chunk + 1) * outs // chunk : (k * chunk + chunk + 1) * outs // chunk, :] = (
                jnp.maximum(acc, 0.0).astype(out_ref.dtype)
            )
        else:
            for r in range(rows):
                out_ref[r, k * chunk : (k + 1) * chunk, :] = acc[:, r * cols : (r + 1) * cols]
    if relu:
        pad = jnp.zeros((outs // chunk, width), out_ref.dtype)
        out_ref[: outs // chunk, :] = pad
        out_ref[out_ref.shape[0] - outs // chunk :, :] = pad


def banded(kernel, chunk):
    groups = kernel.shape[3]
    cols = (chunk + 2) * groups
    taps = kernel.reshape((3, 9) + kernel.shape[3:])
    col = lax.iota(jnp.int32, cols)
    spread = (col[None, :] % groups == jnp.arange(groups)[:, None]).astype(kernel.dtype)
    if kernel.ndim == 5:
        outs = kernel.shape[4]
        rows = chunk * outs
        row = lax.iota(jnp.int32, rows)
        pick = (row[:, None] % outs == jnp.arange(outs)[None, :]).astype(kernel.dtype)
        lanes = jnp.einsum("xyio,ic->xyoc", taps, spread, preferred_element_type=jnp.float32)
        tiles = jnp.einsum(
            "ro,xyoc->xyrc", pick, lanes.astype(kernel.dtype), preferred_element_type=jnp.float32
        )
        depth_of_row = row // outs
    else:
        rows = chunk
        lanes = jnp.einsum("xyi,ic->xyc", taps, spread, preferred_element_type=jnp.float32)
        tiles = lanes[:, :, None, :]
        depth_of_row = lax.iota(jnp.int32, rows)
    band = col[None, None, :] // groups == depth_of_row[None, :, None] + jnp.arange(3)[:, None, None]
    mats = jnp.sum(jnp.where(band[:, None], tiles, 0.0), axis=0)
    return mats.astype(kernel.dtype).reshape(3, 3, rows, cols)


def conv_pair_kernel(
    ends_ref, low_ref, vol_ref, high_ref, m1_ref, m2_ref, out_ref, framed, hidden, *, rows, cols, groups
):
    halo = low_ref.shape[1]
    middle = vol_ref.shape[1]
    framed[:, :halo] = low_ref[...]
    framed[:, halo : halo + middle] = vol_ref[...]
    framed[:, halo + middle :] = high_ref[...]
    depth = framed.shape[0] // groups - 2
    first = m1_ref.shape[3] // groups - 2
    conv_body(
        framed, m1_ref, hidden, ends_ref, relu=True, rows=rows + 2, cols=cols, groups=groups, chunk=first
    )
    conv_body(
        hidden,
        m2_ref,
        out_ref,
        None,
        relu=False,
        rows=rows,
        cols=cols,
        groups=groups,
        chunk=m2_ref.shape[2],
    )


def conv_pair(ends, low, volume, high, first, second, rows, cols):
    groups = second.shape[3] // (second.shape[2] + 2)
    depth = volume.shape[0] // groups - 2
    outs = first.shape[2] * depth // (first.shape[3] // groups - 2)
    vmem = pl.BlockSpec(memory_space=pltpu.VMEM)
    return pl.pallas_call(
        functools.partial(conv_pair_kernel, rows=rows, cols=cols, groups=groups),
        out_shape=jax.ShapeDtypeStruct((rows, depth, cols), jnp.float32),
        in_specs=[pl.BlockSpec(memory_space=pltpu.SMEM)] + [vmem] * 5,
        out_specs=vmem,
        scratch_shapes=[
            pltpu.VMEM((volume.shape[0], volume.shape[1] + low.shape[1] + high.shape[1]), volume.dtype),
            pltpu.VMEM(((depth + 2) * outs // depth, (rows + 2) * cols), jnp.bfloat16),
        ],
    )(ends, low, volume, high, first, second)


def halo_cols(block, cols):
    count = lax.axis_size("view")
    forward = [(i, i + 1) for i in range(count - 1)]
    backward = [(target, source) for source, target in forward]
    low = lax.ppermute(block[:, block.shape[1] - cols :], "view", forward)
    high = lax.ppermute(block[:, :cols], "view", backward)
    return jnp.concatenate([low, block, high], axis=1)


def gather_view(block):
    count = lax.axis_size("view")
    if count & (count - 1):
        return lax.all_to_all(
            jnp.broadcast_to(block, (count,) + block.shape[1:]), "view", 0, 0, tiled=True
        )
    index = lax.axis_index("view")
    gathered = block[0]
    level = 0
    stride = count // 2
    if count >= 4:
        top = count // 4
        parts = [gathered] + [
            lax.ppermute(gathered, "view", [(i, i ^ (m * top)) for i in range(count)])
            for m in (1, 2, 3)
        ]
        order = jnp.arange(4) ^ ((index // top) % 4)
        gathered = jnp.take(jnp.stack(parts), order, axis=0).reshape((2, 2) + gathered.shape)
        level = 2
        stride = top // 2
    while stride >= 1:
        other = lax.ppermute(gathered, "view", [(i, i ^ stride) for i in range(count)])
        low = (index // stride) % 2 == 0
        gathered = jnp.where(
            low, jnp.stack([gathered, other], axis=level), jnp.stack([other, gathered], axis=level)
        )
        level += 1
        stride //= 2
    return gathered.reshape((count,) + block.shape[1:])


def pad_rows(volume):
    return with_halo(volume, (("view", 0),), 1)


def body(
    src_feat,
    ref_feat,
    weight_table,
    src_block,
    table_index,
    block_count,
    depth_plane,
    kern_one,
    kern_two,
):
    owners = lax.axis_size("view")
    features = src_feat[0]
    channels, spix = features.shape
    slots, block_width, tpix = weight_table.shape
    blocks = features.reshape(channels, spix // block_width, block_width).transpose(1, 0, 2)
    units = src_block.shape[1]
    cap = units // owners
    counts = block_count[0]
    nblocks = spix // block_width
    blocks = jnp.concatenate([blocks, jnp.zeros_like(blocks[:1])], axis=0)
    matches = table_index[0][:, :, None] == jnp.arange(slots)[None, None, :]
    live = (jnp.arange(slots)[None, :] < counts[:, None])[:, :, None] & matches
    picked = jnp.sum(jnp.where(matches, src_block[0][:, :, None], 0), axis=1)
    alive = jnp.any(live, axis=1)
    blk = jnp.where(alive, picked, nblocks).reshape(-1).astype(jnp.int32)
    depth_code = jnp.where(counts > 0, depth_plane[0], -1).astype(jnp.bfloat16)

    tag_block = jnp.pad(depth_code, (0, channels * 128 - units)).reshape(channels, 128)
    ref_all = gather_view(jnp.concatenate([ref_feat[0], tag_block], axis=1)[None])
    corr_all = correlate(
        blk, blocks, weight_table.reshape(slots * block_width, tpix), ref_all, units
    )
    arriving = lax.all_to_all(
        corr_all.reshape(owners, cap * GROUPS, tpix),
        "view",
        split_axis=0,
        concat_axis=0,
        tiled=True,
    ).reshape(owners * cap, GROUPS, tpix)
    depth_tags = lax.dynamic_slice_in_dim(
        ref_all[:, :, tpix:].reshape(owners, channels * 128), lax.axis_index("view") * cap, cap, axis=1
    ).reshape(owners * cap)
    labels = jnp.arange(-1, DEPTH + 1).at[0].set(-2)
    onehot = (
        depth_tags[None, :] == labels.astype(jnp.bfloat16)[:, None]
    ).astype(jnp.bfloat16)
    summed = jnp.einsum("dn,ngp->dgp", onehot, arriving, preferred_element_type=jnp.float32)
    tallies = jnp.sum(onehot.astype(jnp.float32), axis=1)
    cost_volume = (summed / jnp.maximum(tallies, 1.0)[:, None, None]).astype(jnp.bfloat16)
    columns = tpix // TROWS
    volume = cost_volume.reshape((DEPTH + 2) * GROUPS, TROWS * columns)
    count = lax.axis_size("view")
    place = lax.axis_index("view")
    ends = jnp.stack([place == 0, place == count - 1]).astype(jnp.int32)
    count = lax.axis_size("view")
    forward = [(i, i + 1) for i in range(count - 1)]
    backward = [(target, source) for source, target in forward]
    low = lax.ppermute(volume[:, volume.shape[1] - 2 * columns :], "view", forward)
    high = lax.ppermute(volume[:, : 2 * columns], "view", backward)
    scores = conv_pair(
        ends,
        low,
        volume,
        high,
        banded(kern_one, DEPTH // 4),
        banded(kern_two, DEPTH // 4),
        TROWS,
        columns,
    )
    return scores


def solution(mesh):
    in_specs = (
        P(("scene", "view"), None, None),
        P(("scene", "view"), None, None),
        P(),
        P(("scene", "view"), None, None),
        P(("scene", "view"), None, None),
        P(("scene", "view"), None),
        P(("scene", "view"), None),
        P(),
        P(),
    )
    out_specs = P(("scene", "view"), None, None)
    return jax.shard_map(body, mesh=mesh, in_specs=in_specs, out_specs=out_specs, check_vma=False)
```

```python
import functools

import jax
import jax.numpy as jnp
from jax import lax
from jax.experimental import pallas as pl
from jax.experimental.pallas import tpu as pltpu
from jax.sharding import PartitionSpec as P

GROUPS = 8
DEPTH = 64
TROWS = 4


def with_halo(block, sides, width):
    for axis, dim in sides:
        count = lax.axis_size(axis)
        forward = [(i, i + 1) for i in range(count - 1)]
        backward = [(target, source) for source, target in forward]
        low = lax.ppermute(
            lax.slice_in_dim(block, block.shape[dim] - width, None, axis=dim), axis, forward
        )
        high = lax.ppermute(lax.slice_in_dim(block, 0, width, axis=dim), axis, backward)
        block = jnp.concatenate([low, block, high], axis=dim)
    return block


def convolve_full(padded, kernel):
    rows_out = padded.shape[0] - 2
    depth_len = padded.shape[2]
    columns = padded.shape[3]
    framed = jnp.pad(padded, ((0, 0), (0, 0), (1, 1), (1, 1)))
    carried = jnp.zeros((rows_out, kernel.shape[-1], depth_len, columns), jnp.float32)
    for depth_off in range(3):
        for row_off in range(3):
            for col_off in range(3):
                window = framed[
                    row_off : row_off + rows_out,
                    :,
                    depth_off : depth_off + depth_len,
                    col_off : col_off + columns,
                ]
                carried = carried + jnp.einsum(
                    "rcdw,ce->redw",
                    window,
                    kernel[depth_off, row_off, col_off],
                    preferred_element_type=jnp.float32,
                )
    return carried


def convolve_final(padded, kernel):
    rows_out = padded.shape[0] - 2
    depth_len = padded.shape[2]
    columns = padded.shape[3]
    framed = jnp.pad(padded, ((0, 0), (0, 0), (1, 1), (1, 1)))
    carried = jnp.zeros((rows_out, depth_len, columns), jnp.float32)
    for depth_off in range(3):
        for row_off in range(3):
            for col_off in range(3):
                window = framed[
                    row_off : row_off + rows_out,
                    :,
                    depth_off : depth_off + depth_len,
                    col_off : col_off + columns,
                ]
                carried = carried + jnp.einsum(
                    "rcdw,c->rdw",
                    window,
                    kernel[depth_off, row_off, col_off],
                    preferred_element_type=jnp.float32,
                )
    return carried


def correlate_kernel(blk_ref, blocks_ref, table_ref, ref_ref, out_ref, arranged, products):
    chunk = 16
    slots = table_ref.shape[0] // blocks_ref.shape[2]
    width = blocks_ref.shape[2]
    channels = blocks_ref.shape[1]
    units = out_ref.shape[0] // GROUPS
    cap = units // ref_ref.shape[0]
    group_size = channels // GROUPS
    rows = chunk * channels

    def step(c, carry):
        for u in range(chunk):
            unit = c * chunk + u
            for w in range(slots):
                arranged[u * channels : (u + 1) * channels, w * width : (w + 1) * width] = blocks_ref[
                    blk_ref[unit * slots + w]
                ]
        warped = jnp.dot(arranged[...], table_ref[...], preferred_element_type=jnp.float32)
        warped = warped.astype(jnp.bfloat16).astype(jnp.float32)
        lanes = products.shape[0]
        for u in range(chunk):
            unit = c * chunk + u
            tile = ref_ref[unit // cap].astype(jnp.float32)
            for j in range(lanes):
                products[j, u * channels : (u + 1) * channels, :] = (
                    warped[u * channels : (u + 1) * channels, j * 128 : (j + 1) * 128]
                    * tile[:, j * 128 : (j + 1) * 128]
                )
        start = pl.multiple_of(c * (chunk * GROUPS), chunk * GROUPS)
        for j in range(lanes):
            total = products[j, pl.ds(0, rows // group_size, stride=group_size), :]
            for k in range(1, group_size):
                total = total + products[j, pl.ds(k, rows // group_size, stride=group_size), :]
            out_ref[pl.ds(start, chunk * GROUPS), j * 128 : (j + 1) * 128] = (
                total * (GROUPS / channels)
            ).astype(out_ref.dtype)
        return carry

    lax.fori_loop(0, units // chunk, step, 0, unroll=2)


def correlate(blk, blocks, table, refs, units):
    channels, width = blocks.shape[1], blocks.shape[2]
    tpix = table.shape[1]
    chunk = 16
    return pl.pallas_call(
        correlate_kernel,
        out_shape=jax.ShapeDtypeStruct((units * GROUPS, tpix), jnp.bfloat16),
        in_specs=[
            pl.BlockSpec(memory_space=pltpu.SMEM),
            pl.BlockSpec(memory_space=pltpu.VMEM),
            pl.BlockSpec(memory_space=pltpu.VMEM),
            pl.BlockSpec(memory_space=pltpu.VMEM),
        ],
        out_specs=pl.BlockSpec(memory_space=pltpu.VMEM),
        scratch_shapes=[
            pltpu.VMEM((chunk * channels, table.shape[0]), jnp.bfloat16),
            pltpu.VMEM((tpix // 128, chunk * channels, 128), jnp.float32),
        ],
    )(blk, blocks, table, refs)


def conv_body(x_ref, m_ref, out_ref, ends_ref, *, relu, rows, cols, groups, chunk):
    width = rows * cols
    outs = m_ref.shape[2]
    depth = x_ref.shape[0] // groups - 2
    lane = lax.broadcasted_iota(jnp.int32, (outs, width), 1) % cols
    for k in range(depth // chunk):
        acc = None
        for e in range(3):
            y = None
            for b in range(3):
                window = x_ref[k * chunk * groups : (k * chunk + chunk + 2) * groups, b * cols : b * cols + width]
                part = jnp.dot(m_ref[b, e], window, preferred_element_type=jnp.float32)
                y = part if y is None else y + part
            if e == 0:
                y = jnp.where(lane >= 1, pltpu.roll(y, 1, 1), 0.0)
            elif e == 2:
                y = jnp.where(lane <= cols - 2, pltpu.roll(y, width - 1, 1), 0.0)
            acc = y if acc is None else acc + y
        if relu:
            block = lax.broadcasted_iota(jnp.int32, (outs, width), 1) // cols
            outside = ((block == 0) & (ends_ref[0] > 0)) | ((block == rows - 1) & (ends_ref[1] > 0))
            acc = jnp.where(outside, 0.0, acc)
            out_ref[(k * chunk + 1) * outs // chunk : (k * chunk + chunk + 1) * outs // chunk, :] = (
                jnp.maximum(acc, 0.0).astype(out_ref.dtype)
            )
        else:
            for r in range(rows):
                out_ref[r, k * chunk : (k + 1) * chunk, :] = acc[:, r * cols : (r + 1) * cols]
    if relu:
        pad = jnp.zeros((outs // chunk, width), out_ref.dtype)
        out_ref[: outs // chunk, :] = pad
        out_ref[out_ref.shape[0] - outs // chunk :, :] = pad


def banded(kernel, chunk):
    groups = kernel.shape[3]
    cols = (chunk + 2) * groups
    taps = kernel.reshape((3, 9) + kernel.shape[3:])
    col = lax.iota(jnp.int32, cols)
    spread = (col[None, :] % groups == jnp.arange(groups)[:, None]).astype(kernel.dtype)
    if kernel.ndim == 5:
        outs = kernel.shape[4]
        rows = chunk * outs
        row = lax.iota(jnp.int32, rows)
        lanes = jnp.einsum("xyio,ic->xyoc", taps, spread, preferred_element_type=jnp.float32)
        tiles = jnp.broadcast_to(lanes[:, :, None], (3, 9, chunk, outs, cols)).reshape(3, 9, rows, cols)
        depth_of_row = row // outs
    else:
        rows = chunk
        lanes = jnp.einsum("xyi,ic->xyc", taps, spread, preferred_element_type=jnp.float32)
        tiles = lanes[:, :, None, :]
        depth_of_row = lax.iota(jnp.int32, rows)
    band = col[None, None, :] // groups == depth_of_row[None, :, None] + jnp.arange(3)[:, None, None]
    mats = jnp.sum(jnp.where(band[:, None], tiles, 0.0), axis=0)
    return mats.astype(kernel.dtype).reshape(3, 3, rows, cols)


def conv_pair_kernel(
    ends_ref, low_ref, vol_ref, high_ref, m1_ref, m2_ref, out_ref, framed, hidden, *, rows, cols, groups
):
    halo = low_ref.shape[1]
    middle = vol_ref.shape[1]
    framed[:, :halo] = low_ref[...]
    framed[:, halo : halo + middle] = vol_ref[...]
    framed[:, halo + middle :] = high_ref[...]
    depth = framed.shape[0] // groups - 2
    first = m1_ref.shape[3] // groups - 2
    conv_body(
        framed, m1_ref, hidden, ends_ref, relu=True, rows=rows + 2, cols=cols, groups=groups, chunk=first
    )
    conv_body(
        hidden,
        m2_ref,
        out_ref,
        None,
        relu=False,
        rows=rows,
        cols=cols,
        groups=groups,
        chunk=m2_ref.shape[2],
    )


def conv_pair(ends, low, volume, high, first, second, rows, cols):
    groups = second.shape[3] // (second.shape[2] + 2)
    depth = volume.shape[0] // groups - 2
    outs = first.shape[2] * depth // (first.shape[3] // groups - 2)
    vmem = pl.BlockSpec(memory_space=pltpu.VMEM)
    return pl.pallas_call(
        functools.partial(conv_pair_kernel, rows=rows, cols=cols, groups=groups),
        out_shape=jax.ShapeDtypeStruct((rows, depth, cols), jnp.float32),
        in_specs=[pl.BlockSpec(memory_space=pltpu.SMEM)] + [vmem] * 5,
        out_specs=vmem,
        scratch_shapes=[
            pltpu.VMEM((volume.shape[0], volume.shape[1] + low.shape[1] + high.shape[1]), volume.dtype),
            pltpu.VMEM(((depth + 2) * outs // depth, (rows + 2) * cols), jnp.bfloat16),
        ],
    )(ends, low, volume, high, first, second)


def halo_cols(block, cols):
    count = lax.axis_size("view")
    forward = [(i, i + 1) for i in range(count - 1)]
    backward = [(target, source) for source, target in forward]
    low = lax.ppermute(block[:, block.shape[1] - cols :], "view", forward)
    high = lax.ppermute(block[:, :cols], "view", backward)
    return jnp.concatenate([low, block, high], axis=1)


def gather_view(block):
    count = lax.axis_size("view")
    if count & (count - 1):
        return lax.all_to_all(
            jnp.broadcast_to(block, (count,) + block.shape[1:]), "view", 0, 0, tiled=True
        )
    index = lax.axis_index("view")
    gathered = block[0]
    level = 0
    stride = count // 2
    if count >= 4:
        top = count // 4
        parts = [gathered] + [
            lax.ppermute(gathered, "view", [(i, i ^ (m * top)) for i in range(count)])
            for m in (1, 2, 3)
        ]
        order = jnp.arange(4) ^ ((index // top) % 4)
        gathered = jnp.take(jnp.stack(parts), order, axis=0).reshape((2, 2) + gathered.shape)
        level = 2
        stride = top // 2
    while stride >= 1:
        other = lax.ppermute(gathered, "view", [(i, i ^ stride) for i in range(count)])
        low = (index // stride) % 2 == 0
        gathered = jnp.where(
            low, jnp.stack([gathered, other], axis=level), jnp.stack([other, gathered], axis=level)
        )
        level += 1
        stride //= 2
    return gathered.reshape((count,) + block.shape[1:])


def pad_rows(volume):
    return with_halo(volume, (("view", 0),), 1)


def body(
    src_feat,
    ref_feat,
    weight_table,
    src_block,
    table_index,
    block_count,
    depth_plane,
    kern_one,
    kern_two,
):
    owners = lax.axis_size("view")
    features = src_feat[0]
    channels, spix = features.shape
    slots, block_width, tpix = weight_table.shape
    blocks = features.reshape(channels, spix // block_width, block_width).transpose(1, 0, 2)
    units = src_block.shape[1]
    cap = units // owners
    counts = block_count[0]
    nblocks = spix // block_width
    blocks = jnp.concatenate([blocks, jnp.zeros_like(blocks[:1])], axis=0)
    matches = table_index[0][:, :, None] == jnp.arange(slots)[None, None, :]
    live = (jnp.arange(slots)[None, :] < counts[:, None])[:, :, None] & matches
    picked = jnp.sum(jnp.where(matches, src_block[0][:, :, None], 0), axis=1)
    alive = jnp.any(live, axis=1)
    blk = jnp.where(alive, picked, nblocks).reshape(-1).astype(jnp.int32)
    depth_code = jnp.where(counts > 0, depth_plane[0], -1).astype(jnp.bfloat16)

    tag_block = jnp.pad(depth_code, (0, channels * 128 - units)).reshape(channels, 128)
    ref_all = gather_view(jnp.concatenate([ref_feat[0], tag_block], axis=1)[None])
    corr_all = correlate(
        blk, blocks, weight_table.reshape(slots * block_width, tpix), ref_all, units
    )
    arriving = lax.all_to_all(
        corr_all.reshape(owners, cap * GROUPS, tpix),
        "view",
        split_axis=0,
        concat_axis=0,
        tiled=True,
    ).reshape(owners * cap, GROUPS, tpix)
    depth_tags = lax.dynamic_slice_in_dim(
        ref_all[:, :, tpix:].reshape(owners, channels * 128), lax.axis_index("view") * cap, cap, axis=1
    ).reshape(owners * cap)
    labels = jnp.arange(-1, DEPTH + 1).at[0].set(-2)
    onehot = (
        depth_tags[None, :] == labels.astype(jnp.bfloat16)[:, None]
    ).astype(jnp.bfloat16)
    summed = jnp.einsum("dn,ngp->dgp", onehot, arriving, preferred_element_type=jnp.float32)
    tallies = jnp.sum(onehot.astype(jnp.float32), axis=1)
    cost_volume = (summed / jnp.maximum(tallies, 1.0)[:, None, None]).astype(jnp.bfloat16)
    columns = tpix // TROWS
    volume = cost_volume.reshape((DEPTH + 2) * GROUPS, TROWS * columns)
    count = lax.axis_size("view")
    place = lax.axis_index("view")
    ends = jnp.stack([place == 0, place == count - 1]).astype(jnp.int32)
    count = lax.axis_size("view")
    forward = [(i, i + 1) for i in range(count - 1)]
    backward = [(target, source) for source, target in forward]
    low = lax.ppermute(volume[:, volume.shape[1] - 2 * columns :], "view", forward)
    high = lax.ppermute(volume[:, : 2 * columns], "view", backward)
    scores = conv_pair(
        ends,
        low,
        volume,
        high,
        banded(kern_one, DEPTH // 4),
        banded(kern_two, DEPTH // 4),
        TROWS,
        columns,
    )
    return scores


def solution(mesh):
    in_specs = (
        P(("scene", "view"), None, None),
        P(("scene", "view"), None, None),
        P(),
        P(("scene", "view"), None, None),
        P(("scene", "view"), None, None),
        P(("scene", "view"), None),
        P(("scene", "view"), None),
        P(),
        P(),
    )
    out_specs = P(("scene", "view"), None, None)
    return jax.shard_map(body, mesh=mesh, in_specs=in_specs, out_specs=out_specs, check_vma=False)
```

```python
import functools

import jax
import jax.numpy as jnp
from jax import lax
from jax.experimental import pallas as pl
from jax.experimental.pallas import tpu as pltpu
from jax.sharding import PartitionSpec as P

GROUPS = 8
DEPTH = 64
TROWS = 4


def with_halo(block, sides, width):
    for axis, dim in sides:
        count = lax.axis_size(axis)
        forward = [(i, i + 1) for i in range(count - 1)]
        backward = [(target, source) for source, target in forward]
        low = lax.ppermute(
            lax.slice_in_dim(block, block.shape[dim] - width, None, axis=dim), axis, forward
        )
        high = lax.ppermute(lax.slice_in_dim(block, 0, width, axis=dim), axis, backward)
        block = jnp.concatenate([low, block, high], axis=dim)
    return block


def convolve_full(padded, kernel):
    rows_out = padded.shape[0] - 2
    depth_len = padded.shape[2]
    columns = padded.shape[3]
    framed = jnp.pad(padded, ((0, 0), (0, 0), (1, 1), (1, 1)))
    carried = jnp.zeros((rows_out, kernel.shape[-1], depth_len, columns), jnp.float32)
    for depth_off in range(3):
        for row_off in range(3):
            for col_off in range(3):
                window = framed[
                    row_off : row_off + rows_out,
                    :,
                    depth_off : depth_off + depth_len,
                    col_off : col_off + columns,
                ]
                carried = carried + jnp.einsum(
                    "rcdw,ce->redw",
                    window,
                    kernel[depth_off, row_off, col_off],
                    preferred_element_type=jnp.float32,
                )
    return carried


def convolve_final(padded, kernel):
    rows_out = padded.shape[0] - 2
    depth_len = padded.shape[2]
    columns = padded.shape[3]
    framed = jnp.pad(padded, ((0, 0), (0, 0), (1, 1), (1, 1)))
    carried = jnp.zeros((rows_out, depth_len, columns), jnp.float32)
    for depth_off in range(3):
        for row_off in range(3):
            for col_off in range(3):
                window = framed[
                    row_off : row_off + rows_out,
                    :,
                    depth_off : depth_off + depth_len,
                    col_off : col_off + columns,
                ]
                carried = carried + jnp.einsum(
                    "rcdw,c->rdw",
                    window,
                    kernel[depth_off, row_off, col_off],
                    preferred_element_type=jnp.float32,
                )
    return carried


def correlate_kernel(blk_ref, blocks_ref, table_ref, ref_ref, out_ref, arranged, products):
    chunk = 16
    slots = table_ref.shape[0] // blocks_ref.shape[2]
    width = blocks_ref.shape[2]
    channels = blocks_ref.shape[1]
    units = out_ref.shape[0] // GROUPS
    cap = units // ref_ref.shape[0]
    group_size = channels // GROUPS
    rows = chunk * channels

    def step(c, carry):
        for u in range(chunk):
            unit = c * chunk + u
            for w in range(slots):
                arranged[u * channels : (u + 1) * channels, w * width : (w + 1) * width] = blocks_ref[
                    blk_ref[unit * slots + w]
                ]
        warped = jnp.dot(arranged[...], table_ref[...], preferred_element_type=jnp.float32)
        warped = warped.astype(jnp.bfloat16).astype(jnp.float32)
        lanes = products.shape[0]
        for u in range(chunk):
            unit = c * chunk + u
            tile = ref_ref[unit // cap].astype(jnp.float32)
            for j in range(lanes):
                products[j, u * channels : (u + 1) * channels, :] = (
                    warped[u * channels : (u + 1) * channels, j * 128 : (j + 1) * 128]
                    * tile[:, j * 128 : (j + 1) * 128]
                )
        start = pl.multiple_of(c * (chunk * GROUPS), chunk * GROUPS)
        for j in range(lanes):
            total = products[j, pl.ds(0, rows // group_size, stride=group_size), :]
            for k in range(1, group_size):
                total = total + products[j, pl.ds(k, rows // group_size, stride=group_size), :]
            out_ref[pl.ds(start, chunk * GROUPS), j * 128 : (j + 1) * 128] = (
                total * (GROUPS / channels)
            ).astype(out_ref.dtype)
        return carry

    lax.fori_loop(0, units // chunk, step, 0, unroll=2)


def correlate(blk, blocks, table, refs, units):
    channels, width = blocks.shape[1], blocks.shape[2]
    tpix = table.shape[1]
    chunk = 16
    return pl.pallas_call(
        correlate_kernel,
        out_shape=jax.ShapeDtypeStruct((units * GROUPS, tpix), jnp.bfloat16),
        in_specs=[
            pl.BlockSpec(memory_space=pltpu.SMEM),
            pl.BlockSpec(memory_space=pltpu.VMEM),
            pl.BlockSpec(memory_space=pltpu.VMEM),
            pl.BlockSpec(memory_space=pltpu.VMEM),
        ],
        out_specs=pl.BlockSpec(memory_space=pltpu.VMEM),
        scratch_shapes=[
            pltpu.VMEM((chunk * channels, table.shape[0]), jnp.bfloat16),
            pltpu.VMEM((tpix // 128, chunk * channels, 128), jnp.float32),
        ],
    )(blk, blocks, table, refs)


def conv_body(x_ref, m_ref, out_ref, ends_ref, *, relu, rows, cols, groups, chunk):
    width = rows * cols
    outs = m_ref.shape[2]
    depth = x_ref.shape[0] // groups - 2
    lane = lax.broadcasted_iota(jnp.int32, (outs, width), 1) % cols
    for k in range(depth // chunk):
        acc = None
        for e in range(3):
            y = None
            for b in range(3):
                window = x_ref[k * chunk * groups : (k * chunk + chunk + 2) * groups, b * cols : b * cols + width]
                part = jnp.dot(m_ref[b, e], window, preferred_element_type=jnp.float32)
                y = part if y is None else y + part
            if e == 0:
                y = jnp.where(lane >= 1, pltpu.roll(y, 1, 1), 0.0)
            elif e == 2:
                y = jnp.where(lane <= cols - 2, pltpu.roll(y, width - 1, 1), 0.0)
            acc = y if acc is None else acc + y
        if relu:
            block = lax.broadcasted_iota(jnp.int32, (outs, width), 1) // cols
            outside = ((block == 0) & (ends_ref[0] > 0)) | ((block == rows - 1) & (ends_ref[1] > 0))
            acc = jnp.where(outside, 0.0, acc)
            out_ref[(k * chunk + 1) * outs // chunk : (k * chunk + chunk + 1) * outs // chunk, :] = (
                jnp.maximum(acc, 0.0).astype(out_ref.dtype)
            )
        else:
            for r in range(rows):
                out_ref[r, k * chunk : (k + 1) * chunk, :] = acc[:, r * cols : (r + 1) * cols]
    if relu:
        pad = jnp.zeros((outs // chunk, width), out_ref.dtype)
        out_ref[: outs // chunk, :] = pad
        out_ref[out_ref.shape[0] - outs // chunk :, :] = pad


def banded(kernel, chunk):
    groups = kernel.shape[3]
    cols = (chunk + 2) * groups
    taps = kernel.reshape((3, 9) + kernel.shape[3:])
    col = lax.iota(jnp.int32, cols)
    spread = (col[None, :] % groups == jnp.arange(groups)[:, None]).astype(kernel.dtype)
    if kernel.ndim == 5:
        outs = kernel.shape[4]
        rows = chunk * outs
        row = lax.iota(jnp.int32, rows)
        lanes = jnp.einsum("xyio,ic->xyoc", taps, spread, preferred_element_type=jnp.float32)
        tiles = jnp.broadcast_to(lanes[:, :, None], (3, 9, chunk, outs, cols)).reshape(3, 9, rows, cols)
        depth_of_row = row // outs
    else:
        rows = chunk
        lanes = jnp.einsum("xyi,ic->xyc", taps, spread, preferred_element_type=jnp.float32)
        tiles = lanes[:, :, None, :]
        depth_of_row = lax.iota(jnp.int32, rows)
    band = col[None, None, :] // groups == depth_of_row[None, :, None] + jnp.arange(3)[:, None, None]
    mats = jnp.sum(jnp.where(band[:, None], tiles, 0.0), axis=0)
    return mats.astype(kernel.dtype).reshape(3, 3, rows, cols)


def conv_pair_kernel(
    ends_ref, low_ref, vol_ref, high_ref, m1_ref, m2_ref, out_ref, framed, hidden, *, rows, cols, groups
):
    halo = low_ref.shape[1]
    middle = vol_ref.shape[1]
    framed[:, :halo] = low_ref[...]
    framed[:, halo : halo + middle] = vol_ref[...]
    framed[:, halo + middle :] = high_ref[...]
    depth = framed.shape[0] // groups - 2
    first = m1_ref.shape[3] // groups - 2
    conv_body(
        framed, m1_ref, hidden, ends_ref, relu=True, rows=rows + 2, cols=cols, groups=groups, chunk=first
    )
    conv_body(
        hidden,
        m2_ref,
        out_ref,
        None,
        relu=False,
        rows=rows,
        cols=cols,
        groups=groups,
        chunk=m2_ref.shape[2],
    )


def conv_pair(ends, low, volume, high, first, second, rows, cols):
    groups = second.shape[3] // (second.shape[2] + 2)
    depth = volume.shape[0] // groups - 2
    outs = first.shape[2] * depth // (first.shape[3] // groups - 2)
    vmem = pl.BlockSpec(memory_space=pltpu.VMEM)
    return pl.pallas_call(
        functools.partial(conv_pair_kernel, rows=rows, cols=cols, groups=groups),
        out_shape=jax.ShapeDtypeStruct((rows, depth, cols), jnp.float32),
        in_specs=[pl.BlockSpec(memory_space=pltpu.SMEM)] + [vmem] * 5,
        out_specs=vmem,
        scratch_shapes=[
            pltpu.VMEM((volume.shape[0], volume.shape[1] + low.shape[1] + high.shape[1]), volume.dtype),
            pltpu.VMEM(((depth + 2) * outs // depth, (rows + 2) * cols), jnp.bfloat16),
        ],
    )(ends, low, volume, high, first, second)


def halo_cols(block, cols):
    count = lax.axis_size("view")
    forward = [(i, i + 1) for i in range(count - 1)]
    backward = [(target, source) for source, target in forward]
    low = lax.ppermute(block[:, block.shape[1] - cols :], "view", forward)
    high = lax.ppermute(block[:, :cols], "view", backward)
    return jnp.concatenate([low, block, high], axis=1)


def gather_view(block):
    count = lax.axis_size("view")
    if count & (count - 1):
        return lax.all_to_all(
            jnp.broadcast_to(block, (count,) + block.shape[1:]), "view", 0, 0, tiled=True
        )
    index = lax.axis_index("view")
    gathered = block[0]
    level = 0
    stride = count // 2
    if count >= 4:
        top = count // 4
        parts = [gathered] + [
            lax.ppermute(gathered, "view", [(i, i ^ (m * top)) for i in range(count)])
            for m in (1, 2, 3)
        ]
        order = jnp.arange(4) ^ ((index // top) % 4)
        gathered = jnp.take(jnp.stack(parts), order, axis=0).reshape((2, 2) + gathered.shape)
        level = 2
        stride = top // 2
    while stride >= 1:
        other = lax.ppermute(gathered, "view", [(i, i ^ stride) for i in range(count)])
        low = (index // stride) % 2 == 0
        gathered = jnp.where(
            low, jnp.stack([gathered, other], axis=level), jnp.stack([other, gathered], axis=level)
        )
        level += 1
        stride //= 2
    return gathered.reshape((count,) + block.shape[1:])


def pad_rows(volume):
    return with_halo(volume, (("view", 0),), 1)


def body(
    src_feat,
    ref_feat,
    weight_table,
    src_block,
    table_index,
    block_count,
    depth_plane,
    kern_one,
    kern_two,
):
    owners = lax.axis_size("view")
    features = src_feat[0]
    channels, spix = features.shape
    slots, block_width, tpix = weight_table.shape
    blocks = features.reshape(channels, spix // block_width, block_width).transpose(1, 0, 2)
    units = src_block.shape[1]
    cap = units // owners
    counts = block_count[0]
    nblocks = spix // block_width
    blocks = jnp.concatenate([blocks, jnp.zeros_like(blocks[:1])], axis=0)
    matches = table_index[0][:, :, None] == jnp.arange(slots)[None, None, :]
    live = (jnp.arange(slots)[None, :] < counts[:, None])[:, :, None] & matches
    picked = jnp.sum(jnp.where(matches, src_block[0][:, :, None], 0), axis=1)
    alive = jnp.any(live, axis=1)
    blk = jnp.where(alive, picked, nblocks).reshape(-1).astype(jnp.int32)
    depth_code = jnp.where(counts > 0, depth_plane[0], -1).astype(jnp.bfloat16)

    tag_block = jnp.pad(depth_code, (0, channels * 128 - units)).reshape(channels, 128)
    ref_all = gather_view(jnp.concatenate([ref_feat[0], tag_block], axis=1)[None])
    corr_all = correlate(
        blk, blocks, weight_table.reshape(slots * block_width, tpix), ref_all, units
    )
    corr_all, kern_one, kern_two = lax.optimization_barrier((corr_all, kern_one, kern_two))
    first = banded(kern_one, DEPTH // 4)
    second = banded(kern_two, DEPTH // 4)
    arriving = lax.all_to_all(
        corr_all.reshape(owners, cap * GROUPS, tpix),
        "view",
        split_axis=0,
        concat_axis=0,
        tiled=True,
    ).reshape(owners * cap, GROUPS, tpix)
    depth_tags = lax.dynamic_slice_in_dim(
        ref_all[:, :, tpix:].reshape(owners, channels * 128), lax.axis_index("view") * cap, cap, axis=1
    ).reshape(owners * cap)
    labels = jnp.arange(-1, DEPTH + 1).at[0].set(-2)
    onehot = (
        depth_tags[None, :] == labels.astype(jnp.bfloat16)[:, None]
    ).astype(jnp.bfloat16)
    summed = jnp.einsum("dn,ngp->dgp", onehot, arriving, preferred_element_type=jnp.float32)
    tallies = jnp.sum(onehot.astype(jnp.float32), axis=1)
    cost_volume = (summed / jnp.maximum(tallies, 1.0)[:, None, None]).astype(jnp.bfloat16)
    columns = tpix // TROWS
    volume = cost_volume.reshape((DEPTH + 2) * GROUPS, TROWS * columns)
    count = lax.axis_size("view")
    place = lax.axis_index("view")
    ends = jnp.stack([place == 0, place == count - 1]).astype(jnp.int32)
    count = lax.axis_size("view")
    forward = [(i, i + 1) for i in range(count - 1)]
    backward = [(target, source) for source, target in forward]
    low = lax.ppermute(volume[:, volume.shape[1] - 2 * columns :], "view", forward)
    high = lax.ppermute(volume[:, : 2 * columns], "view", backward)
    scores = conv_pair(
        ends,
        low,
        volume,
        high,
        first,
        second,
        TROWS,
        columns,
    )
    return scores


def solution(mesh):
    in_specs = (
        P(("scene", "view"), None, None),
        P(("scene", "view"), None, None),
        P(),
        P(("scene", "view"), None, None),
        P(("scene", "view"), None, None),
        P(("scene", "view"), None),
        P(("scene", "view"), None),
        P(),
        P(),
    )
    out_specs = P(("scene", "view"), None, None)
    return jax.shard_map(body, mesh=mesh, in_specs=in_specs, out_specs=out_specs, check_vma=False)
```

```python
import functools

import jax
import jax.numpy as jnp
from jax import lax
from jax.experimental import pallas as pl
from jax.experimental.pallas import tpu as pltpu
from jax.sharding import PartitionSpec as P

GROUPS = 8
DEPTH = 64
TROWS = 4


def with_halo(block, sides, width):
    for axis, dim in sides:
        count = lax.axis_size(axis)
        forward = [(i, i + 1) for i in range(count - 1)]
        backward = [(target, source) for source, target in forward]
        low = lax.ppermute(
            lax.slice_in_dim(block, block.shape[dim] - width, None, axis=dim), axis, forward
        )
        high = lax.ppermute(lax.slice_in_dim(block, 0, width, axis=dim), axis, backward)
        block = jnp.concatenate([low, block, high], axis=dim)
    return block


def convolve_full(padded, kernel):
    rows_out = padded.shape[0] - 2
    depth_len = padded.shape[2]
    columns = padded.shape[3]
    framed = jnp.pad(padded, ((0, 0), (0, 0), (1, 1), (1, 1)))
    carried = jnp.zeros((rows_out, kernel.shape[-1], depth_len, columns), jnp.float32)
    for depth_off in range(3):
        for row_off in range(3):
            for col_off in range(3):
                window = framed[
                    row_off : row_off + rows_out,
                    :,
                    depth_off : depth_off + depth_len,
                    col_off : col_off + columns,
                ]
                carried = carried + jnp.einsum(
                    "rcdw,ce->redw",
                    window,
                    kernel[depth_off, row_off, col_off],
                    preferred_element_type=jnp.float32,
                )
    return carried


def convolve_final(padded, kernel):
    rows_out = padded.shape[0] - 2
    depth_len = padded.shape[2]
    columns = padded.shape[3]
    framed = jnp.pad(padded, ((0, 0), (0, 0), (1, 1), (1, 1)))
    carried = jnp.zeros((rows_out, depth_len, columns), jnp.float32)
    for depth_off in range(3):
        for row_off in range(3):
            for col_off in range(3):
                window = framed[
                    row_off : row_off + rows_out,
                    :,
                    depth_off : depth_off + depth_len,
                    col_off : col_off + columns,
                ]
                carried = carried + jnp.einsum(
                    "rcdw,c->rdw",
                    window,
                    kernel[depth_off, row_off, col_off],
                    preferred_element_type=jnp.float32,
                )
    return carried


def correlate_kernel(blk_ref, blocks_ref, table_ref, ref_ref, out_ref, arranged, products):
    chunk = 16
    slots = table_ref.shape[0] // blocks_ref.shape[2]
    width = blocks_ref.shape[2]
    channels = blocks_ref.shape[1]
    units = out_ref.shape[0] // GROUPS
    cap = units // ref_ref.shape[0]
    group_size = channels // GROUPS
    rows = chunk * channels

    def step(c, carry):
        for u in range(chunk):
            unit = c * chunk + u
            for w in range(slots):
                arranged[u * channels : (u + 1) * channels, w * width : (w + 1) * width] = blocks_ref[
                    blk_ref[unit * slots + w]
                ]
        warped = jnp.dot(arranged[...], table_ref[...], preferred_element_type=jnp.float32)
        warped = warped.astype(jnp.bfloat16).astype(jnp.float32)
        lanes = products.shape[0]
        for u in range(chunk):
            unit = c * chunk + u
            tile = ref_ref[unit // cap].astype(jnp.float32)
            for j in range(lanes):
                products[j, u * channels : (u + 1) * channels, :] = (
                    warped[u * channels : (u + 1) * channels, j * 128 : (j + 1) * 128]
                    * tile[:, j * 128 : (j + 1) * 128]
                )
        start = pl.multiple_of(c * (chunk * GROUPS), chunk * GROUPS)
        for j in range(lanes):
            total = products[j, pl.ds(0, rows // group_size, stride=group_size), :]
            for k in range(1, group_size):
                total = total + products[j, pl.ds(k, rows // group_size, stride=group_size), :]
            out_ref[pl.ds(start, chunk * GROUPS), j * 128 : (j + 1) * 128] = (
                total * (GROUPS / channels)
            ).astype(out_ref.dtype)
        return carry

    lax.fori_loop(0, units // chunk, step, 0, unroll=2)


def correlate(blk, blocks, table, refs, units):
    channels, width = blocks.shape[1], blocks.shape[2]
    tpix = table.shape[1]
    chunk = 16
    return pl.pallas_call(
        correlate_kernel,
        out_shape=jax.ShapeDtypeStruct((units * GROUPS, tpix), jnp.bfloat16),
        in_specs=[
            pl.BlockSpec(memory_space=pltpu.SMEM),
            pl.BlockSpec(memory_space=pltpu.VMEM),
            pl.BlockSpec(memory_space=pltpu.VMEM),
            pl.BlockSpec(memory_space=pltpu.VMEM),
        ],
        out_specs=pl.BlockSpec(memory_space=pltpu.VMEM),
        scratch_shapes=[
            pltpu.VMEM((chunk * channels, table.shape[0]), jnp.bfloat16),
            pltpu.VMEM((tpix // 128, chunk * channels, 128), jnp.float32),
        ],
    )(blk, blocks, table, refs)


def conv_body(x_ref, m_ref, out_ref, ends_ref, *, relu, rows, cols, groups, chunk):
    width = rows * cols
    outs = m_ref.shape[2]
    depth = x_ref.shape[0] // groups - 2
    lane = lax.broadcasted_iota(jnp.int32, (outs, width), 1) % cols
    for k in range(depth // chunk):
        acc = None
        for e in range(3):
            y = None
            for b in range(3):
                window = x_ref[k * chunk * groups : (k * chunk + chunk + 2) * groups, b * cols : b * cols + width]
                part = jnp.dot(m_ref[b, e], window, preferred_element_type=jnp.float32)
                y = part if y is None else y + part
            if e == 0:
                y = jnp.where(lane >= 1, pltpu.roll(y, 1, 1), 0.0)
            elif e == 2:
                y = jnp.where(lane <= cols - 2, pltpu.roll(y, width - 1, 1), 0.0)
            acc = y if acc is None else acc + y
        if relu:
            block = lax.broadcasted_iota(jnp.int32, (outs, width), 1) // cols
            outside = ((block == 0) & (ends_ref[0] > 0)) | ((block == rows - 1) & (ends_ref[1] > 0))
            acc = jnp.where(outside, 0.0, acc)
            out_ref[(k * chunk + 1) * outs // chunk : (k * chunk + chunk + 1) * outs // chunk, :] = (
                jnp.maximum(acc, 0.0).astype(out_ref.dtype)
            )
        else:
            for r in range(rows):
                out_ref[r, k * chunk : (k + 1) * chunk, :] = acc[:, r * cols : (r + 1) * cols]
    if relu:
        pad = jnp.zeros((outs // chunk, width), out_ref.dtype)
        out_ref[: outs // chunk, :] = pad
        out_ref[out_ref.shape[0] - outs // chunk :, :] = pad


def banded(kernel, chunk):
    groups = kernel.shape[3]
    cols = (chunk + 2) * groups
    taps = kernel.reshape((3, 9) + kernel.shape[3:])
    col = lax.iota(jnp.int32, cols)
    spread = (col[None, :] % groups == jnp.arange(groups)[:, None]).astype(kernel.dtype)
    if kernel.ndim == 5:
        outs = kernel.shape[4]
        rows = chunk * outs
        row = lax.iota(jnp.int32, rows)
        lanes = jnp.einsum("xyio,ic->xyoc", taps, spread, preferred_element_type=jnp.float32)
        tiles = jnp.broadcast_to(lanes[:, :, None], (3, 9, chunk, outs, cols)).reshape(3, 9, rows, cols)
        depth_of_row = row // outs
    else:
        rows = chunk
        lanes = jnp.einsum("xyi,ic->xyc", taps, spread, preferred_element_type=jnp.float32)
        tiles = lanes[:, :, None, :]
        depth_of_row = lax.iota(jnp.int32, rows)
    band = col[None, None, :] // groups == depth_of_row[None, :, None] + jnp.arange(3)[:, None, None]
    mats = jnp.sum(jnp.where(band[:, None], tiles, 0.0), axis=0)
    return mats.astype(kernel.dtype).reshape(3, 3, rows, cols)


def conv_pair_kernel(
    ends_ref, low_ref, vol_ref, high_ref, m1_ref, m2_ref, out_ref, framed, hidden, *, rows, cols, groups
):
    halo = low_ref.shape[1]
    middle = vol_ref.shape[1]
    framed[:, :halo] = low_ref[...]
    framed[:, halo : halo + middle] = vol_ref[...]
    framed[:, halo + middle :] = high_ref[...]
    depth = framed.shape[0] // groups - 2
    first = m1_ref.shape[3] // groups - 2
    conv_body(
        framed, m1_ref, hidden, ends_ref, relu=True, rows=rows + 2, cols=cols, groups=groups, chunk=first
    )
    conv_body(
        hidden,
        m2_ref,
        out_ref,
        None,
        relu=False,
        rows=rows,
        cols=cols,
        groups=groups,
        chunk=m2_ref.shape[2],
    )


def conv_pair(ends, low, volume, high, first, second, rows, cols):
    groups = second.shape[3] // (second.shape[2] + 2)
    depth = volume.shape[0] // groups - 2
    outs = first.shape[2] * depth // (first.shape[3] // groups - 2)
    vmem = pl.BlockSpec(memory_space=pltpu.VMEM)
    return pl.pallas_call(
        functools.partial(conv_pair_kernel, rows=rows, cols=cols, groups=groups),
        out_shape=jax.ShapeDtypeStruct((rows, depth, cols), jnp.float32),
        in_specs=[pl.BlockSpec(memory_space=pltpu.SMEM)] + [vmem] * 5,
        out_specs=vmem,
        scratch_shapes=[
            pltpu.VMEM((volume.shape[0], volume.shape[1] + low.shape[1] + high.shape[1]), volume.dtype),
            pltpu.VMEM(((depth + 2) * outs // depth, (rows + 2) * cols), jnp.bfloat16),
        ],
    )(ends, low, volume, high, first, second)


def halo_cols(block, cols):
    count = lax.axis_size("view")
    forward = [(i, i + 1) for i in range(count - 1)]
    backward = [(target, source) for source, target in forward]
    low = lax.ppermute(block[:, block.shape[1] - cols :], "view", forward)
    high = lax.ppermute(block[:, :cols], "view", backward)
    return jnp.concatenate([low, block, high], axis=1)


def gather_view(block):
    count = lax.axis_size("view")
    if count & (count - 1):
        return lax.all_to_all(
            jnp.broadcast_to(block, (count,) + block.shape[1:]), "view", 0, 0, tiled=True
        )
    index = lax.axis_index("view")
    gathered = block[0]
    level = 0
    stride = count // 2
    if count >= 4:
        top = count // 4
        parts = [gathered] + [
            lax.ppermute(gathered, "view", [(i, i ^ (m * top)) for i in range(count)])
            for m in (1, 2, 3)
        ]
        order = jnp.arange(4) ^ ((index // top) % 4)
        gathered = jnp.take(jnp.stack(parts), order, axis=0).reshape((2, 2) + gathered.shape)
        level = 2
        stride = top // 2
    while stride >= 1:
        other = lax.ppermute(gathered, "view", [(i, i ^ stride) for i in range(count)])
        low = (index // stride) % 2 == 0
        gathered = jnp.where(
            low, jnp.stack([gathered, other], axis=level), jnp.stack([other, gathered], axis=level)
        )
        level += 1
        stride //= 2
    return gathered.reshape((count,) + block.shape[1:])


def pad_rows(volume):
    return with_halo(volume, (("view", 0),), 1)


def body(
    src_feat,
    ref_feat,
    weight_table,
    src_block,
    table_index,
    block_count,
    depth_plane,
    kern_one,
    kern_two,
):
    owners = lax.axis_size("view")
    features = src_feat[0]
    channels, spix = features.shape
    slots, block_width, tpix = weight_table.shape
    blocks = features.reshape(channels, spix // block_width, block_width).transpose(1, 0, 2)
    units = src_block.shape[1]
    cap = units // owners
    counts = block_count[0]
    nblocks = spix // block_width
    blocks = jnp.concatenate([blocks, jnp.zeros_like(blocks[:1])], axis=0)
    matches = table_index[0][:, :, None] == jnp.arange(slots)[None, None, :]
    live = (jnp.arange(slots)[None, :] < counts[:, None])[:, :, None] & matches
    picked = jnp.sum(jnp.where(matches, src_block[0][:, :, None], 0), axis=1)
    alive = jnp.any(live, axis=1)
    blk = jnp.where(alive, picked, nblocks).reshape(-1).astype(jnp.int32)
    depth_code = jnp.where(counts > 0, depth_plane[0], -1).astype(jnp.bfloat16)

    tag_block = jnp.pad(depth_code, (0, channels * 128 - units)).reshape(channels, 128)
    ref_all = gather_view(jnp.concatenate([ref_feat[0], tag_block], axis=1)[None])
    corr_all = correlate(
        blk, blocks, weight_table.reshape(slots * block_width, tpix), ref_all, units
    )
    corr_all, kern_one, kern_two = lax.optimization_barrier((corr_all, kern_one, kern_two))
    first = banded(kern_one, DEPTH // 4)
    second = banded(kern_two, DEPTH // 4)
    arriving = lax.all_to_all(
        corr_all.reshape(owners, cap * GROUPS, tpix),
        "view",
        split_axis=0,
        concat_axis=0,
        tiled=True,
    ).reshape(owners * cap, GROUPS, tpix)
    arriving, first, second = lax.optimization_barrier((arriving, first, second))
    depth_tags = lax.dynamic_slice_in_dim(
        ref_all[:, :, tpix:].reshape(owners, channels * 128), lax.axis_index("view") * cap, cap, axis=1
    ).reshape(owners * cap)
    labels = jnp.arange(-1, DEPTH + 1).at[0].set(-2)
    onehot = (
        depth_tags[None, :] == labels.astype(jnp.bfloat16)[:, None]
    ).astype(jnp.bfloat16)
    summed = jnp.einsum("dn,ngp->dgp", onehot, arriving, preferred_element_type=jnp.float32)
    tallies = jnp.sum(onehot.astype(jnp.float32), axis=1)
    cost_volume = (summed / jnp.maximum(tallies, 1.0)[:, None, None]).astype(jnp.bfloat16)
    columns = tpix // TROWS
    volume = cost_volume.reshape((DEPTH + 2) * GROUPS, TROWS * columns)
    count = lax.axis_size("view")
    place = lax.axis_index("view")
    ends = jnp.stack([place == 0, place == count - 1]).astype(jnp.int32)
    count = lax.axis_size("view")
    forward = [(i, i + 1) for i in range(count - 1)]
    backward = [(target, source) for source, target in forward]
    low = lax.ppermute(volume[:, volume.shape[1] - 2 * columns :], "view", forward)
    high = lax.ppermute(volume[:, : 2 * columns], "view", backward)
    scores = conv_pair(
        ends,
        low,
        volume,
        high,
        first,
        second,
        TROWS,
        columns,
    )
    return scores


def solution(mesh):
    in_specs = (
        P(("scene", "view"), None, None),
        P(("scene", "view"), None, None),
        P(),
        P(("scene", "view"), None, None),
        P(("scene", "view"), None, None),
        P(("scene", "view"), None),
        P(("scene", "view"), None),
        P(),
        P(),
    )
    out_specs = P(("scene", "view"), None, None)
    return jax.shard_map(body, mesh=mesh, in_specs=in_specs, out_specs=out_specs, check_vma=False)
```

```python
import functools

import jax
import jax.numpy as jnp
from jax import lax
from jax.experimental import pallas as pl
from jax.experimental.pallas import tpu as pltpu
from jax.sharding import PartitionSpec as P

GROUPS = 8
DEPTH = 64
TROWS = 4


def with_halo(block, sides, width):
    for axis, dim in sides:
        count = lax.axis_size(axis)
        forward = [(i, i + 1) for i in range(count - 1)]
        backward = [(target, source) for source, target in forward]
        low = lax.ppermute(
            lax.slice_in_dim(block, block.shape[dim] - width, None, axis=dim), axis, forward
        )
        high = lax.ppermute(lax.slice_in_dim(block, 0, width, axis=dim), axis, backward)
        block = jnp.concatenate([low, block, high], axis=dim)
    return block


def convolve_full(padded, kernel):
    rows_out = padded.shape[0] - 2
    depth_len = padded.shape[2]
    columns = padded.shape[3]
    framed = jnp.pad(padded, ((0, 0), (0, 0), (1, 1), (1, 1)))
    carried = jnp.zeros((rows_out, kernel.shape[-1], depth_len, columns), jnp.float32)
    for depth_off in range(3):
        for row_off in range(3):
            for col_off in range(3):
                window = framed[
                    row_off : row_off + rows_out,
                    :,
                    depth_off : depth_off + depth_len,
                    col_off : col_off + columns,
                ]
                carried = carried + jnp.einsum(
                    "rcdw,ce->redw",
                    window,
                    kernel[depth_off, row_off, col_off],
                    preferred_element_type=jnp.float32,
                )
    return carried


def convolve_final(padded, kernel):
    rows_out = padded.shape[0] - 2
    depth_len = padded.shape[2]
    columns = padded.shape[3]
    framed = jnp.pad(padded, ((0, 0), (0, 0), (1, 1), (1, 1)))
    carried = jnp.zeros((rows_out, depth_len, columns), jnp.float32)
    for depth_off in range(3):
        for row_off in range(3):
            for col_off in range(3):
                window = framed[
                    row_off : row_off + rows_out,
                    :,
                    depth_off : depth_off + depth_len,
                    col_off : col_off + columns,
                ]
                carried = carried + jnp.einsum(
                    "rcdw,c->rdw",
                    window,
                    kernel[depth_off, row_off, col_off],
                    preferred_element_type=jnp.float32,
                )
    return carried


def correlate_kernel(blk_ref, bit_ref, blocks_ref, table_ref, ref_ref, partner_ref, out_ref, arranged, products, *, pairs):
    chunk = 16
    slots = table_ref.shape[0] // blocks_ref.shape[2]
    width = blocks_ref.shape[2]
    channels = blocks_ref.shape[1]
    units = out_ref.shape[0] // GROUPS
    cap = units // (ref_ref.shape[0] * (2 if pairs else 1))
    group_size = channels // GROUPS
    rows = chunk * channels

    def step(c, carry):
        for u in range(chunk):
            unit = c * chunk + u
            for w in range(slots):
                arranged[u * channels : (u + 1) * channels, w * width : (w + 1) * width] = blocks_ref[
                    blk_ref[unit * slots + w]
                ]
        warped = jnp.dot(arranged[...], table_ref[...], preferred_element_type=jnp.float32)
        warped = warped.astype(jnp.bfloat16).astype(jnp.float32)
        lanes = products.shape[0]
        for u in range(chunk):
            unit = c * chunk + u
            if pairs:
                owner = unit // cap
                tile = jnp.where(
                    owner % 2 == bit_ref[0], ref_ref[owner // 2], partner_ref[owner // 2]
                ).astype(jnp.float32)
            else:
                tile = ref_ref[unit // cap].astype(jnp.float32)
            for j in range(lanes):
                products[j, u * channels : (u + 1) * channels, :] = (
                    warped[u * channels : (u + 1) * channels, j * 128 : (j + 1) * 128]
                    * tile[:, j * 128 : (j + 1) * 128]
                )
        start = pl.multiple_of(c * (chunk * GROUPS), chunk * GROUPS)
        for j in range(lanes):
            total = products[j, pl.ds(0, rows // group_size, stride=group_size), :]
            for k in range(1, group_size):
                total = total + products[j, pl.ds(k, rows // group_size, stride=group_size), :]
            out_ref[pl.ds(start, chunk * GROUPS), j * 128 : (j + 1) * 128] = (
                total * (GROUPS / channels)
            ).astype(out_ref.dtype)
        return carry

    lax.fori_loop(0, units // chunk, step, 0, unroll=2)


def correlate(blk, blocks, table, mine, partner, bit, units):
    channels = blocks.shape[1]
    tpix = table.shape[1]
    chunk = 16
    pairs = bit is not None
    bits = jnp.reshape(bit if pairs else 0, (1,)).astype(jnp.int32)
    return pl.pallas_call(
        functools.partial(correlate_kernel, pairs=pairs),
        out_shape=jax.ShapeDtypeStruct((units * GROUPS, tpix), jnp.bfloat16),
        in_specs=[
            pl.BlockSpec(memory_space=pltpu.SMEM),
            pl.BlockSpec(memory_space=pltpu.SMEM),
            pl.BlockSpec(memory_space=pltpu.VMEM),
            pl.BlockSpec(memory_space=pltpu.VMEM),
            pl.BlockSpec(memory_space=pltpu.VMEM),
            pl.BlockSpec(memory_space=pltpu.VMEM),
        ],
        out_specs=pl.BlockSpec(memory_space=pltpu.VMEM),
        scratch_shapes=[
            pltpu.VMEM((chunk * channels, table.shape[0]), jnp.bfloat16),
            pltpu.VMEM((tpix // 128, chunk * channels, 128), jnp.float32),
        ],
    )(blk, bits, blocks, table, mine, partner)


def conv_body(x_ref, m_ref, out_ref, ends_ref, *, relu, rows, cols, groups, chunk):
    width = rows * cols
    outs = m_ref.shape[2]
    depth = x_ref.shape[0] // groups - 2
    lane = lax.broadcasted_iota(jnp.int32, (outs, width), 1) % cols
    for k in range(depth // chunk):
        acc = None
        for e in range(3):
            y = None
            for b in range(3):
                window = x_ref[k * chunk * groups : (k * chunk + chunk + 2) * groups, b * cols : b * cols + width]
                part = jnp.dot(m_ref[b, e], window, preferred_element_type=jnp.float32)
                y = part if y is None else y + part
            if e == 0:
                y = jnp.where(lane >= 1, pltpu.roll(y, 1, 1), 0.0)
            elif e == 2:
                y = jnp.where(lane <= cols - 2, pltpu.roll(y, width - 1, 1), 0.0)
            acc = y if acc is None else acc + y
        if relu:
            block = lax.broadcasted_iota(jnp.int32, (outs, width), 1) // cols
            outside = ((block == 0) & (ends_ref[0] > 0)) | ((block == rows - 1) & (ends_ref[1] > 0))
            acc = jnp.where(outside, 0.0, acc)
            out_ref[(k * chunk + 1) * outs // chunk : (k * chunk + chunk + 1) * outs // chunk, :] = (
                jnp.maximum(acc, 0.0).astype(out_ref.dtype)
            )
        else:
            for r in range(rows):
                out_ref[r, k * chunk : (k + 1) * chunk, :] = acc[:, r * cols : (r + 1) * cols]
    if relu:
        pad = jnp.zeros((outs // chunk, width), out_ref.dtype)
        out_ref[: outs // chunk, :] = pad
        out_ref[out_ref.shape[0] - outs // chunk :, :] = pad


def banded(kernel, chunk):
    groups = kernel.shape[3]
    cols = (chunk + 2) * groups
    taps = kernel.reshape((3, 9) + kernel.shape[3:])
    col = lax.iota(jnp.int32, cols)
    spread = (col[None, :] % groups == jnp.arange(groups)[:, None]).astype(kernel.dtype)
    if kernel.ndim == 5:
        outs = kernel.shape[4]
        rows = chunk * outs
        row = lax.iota(jnp.int32, rows)
        lanes = jnp.einsum("xyio,ic->xyoc", taps, spread, preferred_element_type=jnp.float32)
        tiles = jnp.broadcast_to(lanes[:, :, None], (3, 9, chunk, outs, cols)).reshape(3, 9, rows, cols)
        depth_of_row = row // outs
    else:
        rows = chunk
        lanes = jnp.einsum("xyi,ic->xyc", taps, spread, preferred_element_type=jnp.float32)
        tiles = lanes[:, :, None, :]
        depth_of_row = lax.iota(jnp.int32, rows)
    band = col[None, None, :] // groups == depth_of_row[None, :, None] + jnp.arange(3)[:, None, None]
    mats = jnp.sum(jnp.where(band[:, None], tiles, 0.0), axis=0)
    return mats.astype(kernel.dtype).reshape(3, 3, rows, cols)


def conv_pair_kernel(
    ends_ref, low_ref, vol_ref, high_ref, m1_ref, m2_ref, out_ref, framed, hidden, *, rows, cols, groups
):
    halo = low_ref.shape[1]
    middle = vol_ref.shape[1]
    framed[:, :halo] = low_ref[...]
    framed[:, halo : halo + middle] = vol_ref[...]
    framed[:, halo + middle :] = high_ref[...]
    depth = framed.shape[0] // groups - 2
    first = m1_ref.shape[3] // groups - 2
    conv_body(
        framed, m1_ref, hidden, ends_ref, relu=True, rows=rows + 2, cols=cols, groups=groups, chunk=first
    )
    conv_body(
        hidden,
        m2_ref,
        out_ref,
        None,
        relu=False,
        rows=rows,
        cols=cols,
        groups=groups,
        chunk=m2_ref.shape[2],
    )


def conv_pair(ends, low, volume, high, first, second, rows, cols):
    groups = second.shape[3] // (second.shape[2] + 2)
    depth = volume.shape[0] // groups - 2
    outs = first.shape[2] * depth // (first.shape[3] // groups - 2)
    vmem = pl.BlockSpec(memory_space=pltpu.VMEM)
    return pl.pallas_call(
        functools.partial(conv_pair_kernel, rows=rows, cols=cols, groups=groups),
        out_shape=jax.ShapeDtypeStruct((rows, depth, cols), jnp.float32),
        in_specs=[pl.BlockSpec(memory_space=pltpu.SMEM)] + [vmem] * 5,
        out_specs=vmem,
        scratch_shapes=[
            pltpu.VMEM((volume.shape[0], volume.shape[1] + low.shape[1] + high.shape[1]), volume.dtype),
            pltpu.VMEM(((depth + 2) * outs // depth, (rows + 2) * cols), jnp.bfloat16),
        ],
    )(ends, low, volume, high, first, second)


def halo_cols(block, cols):
    count = lax.axis_size("view")
    forward = [(i, i + 1) for i in range(count - 1)]
    backward = [(target, source) for source, target in forward]
    low = lax.ppermute(block[:, block.shape[1] - cols :], "view", forward)
    high = lax.ppermute(block[:, :cols], "view", backward)
    return jnp.concatenate([low, block, high], axis=1)


def gather_view(block, split=False):
    count = lax.axis_size("view")
    if count & (count - 1) or (split and count < 8):
        whole = lax.all_to_all(
            jnp.broadcast_to(block, (count,) + block.shape[1:]), "view", 0, 0, tiled=True
        )
        return (whole, whole, None) if split else whole
    index = lax.axis_index("view")
    gathered = block[0]
    level = 0
    stride = count // 2
    if count >= 4:
        top = count // 4
        parts = [gathered] + [
            lax.ppermute(gathered, "view", [(i, i ^ (m * top)) for i in range(count)])
            for m in (1, 2, 3)
        ]
        order = jnp.arange(4) ^ ((index // top) % 4)
        gathered = jnp.take(jnp.stack(parts), order, axis=0).reshape((2, 2) + gathered.shape)
        level = 2
        stride = top // 2
    while stride >= 1:
        other = lax.ppermute(gathered, "view", [(i, i ^ stride) for i in range(count)])
        if split and stride == 1:
            half = (count // 2,) + block.shape[1:]
            return gathered.reshape(half), other.reshape(half), index % 2
        low = (index // stride) % 2 == 0
        gathered = jnp.where(
            low, jnp.stack([gathered, other], axis=level), jnp.stack([other, gathered], axis=level)
        )
        level += 1
        stride //= 2
    return gathered.reshape((count,) + block.shape[1:])


def pad_rows(volume):
    return with_halo(volume, (("view", 0),), 1)


def body(
    src_feat,
    ref_feat,
    weight_table,
    src_block,
    table_index,
    block_count,
    depth_plane,
    kern_one,
    kern_two,
):
    owners = lax.axis_size("view")
    features = src_feat[0]
    channels, spix = features.shape
    slots, block_width, tpix = weight_table.shape
    blocks = features.reshape(channels, spix // block_width, block_width).transpose(1, 0, 2)
    units = src_block.shape[1]
    cap = units // owners
    counts = block_count[0]
    nblocks = spix // block_width
    blocks = jnp.concatenate([blocks, jnp.zeros_like(blocks[:1])], axis=0)
    matches = table_index[0][:, :, None] == jnp.arange(slots)[None, None, :]
    live = (jnp.arange(slots)[None, :] < counts[:, None])[:, :, None] & matches
    picked = jnp.sum(jnp.where(matches, src_block[0][:, :, None], 0), axis=1)
    alive = jnp.any(live, axis=1)
    blk = jnp.where(alive, picked, nblocks).reshape(-1).astype(jnp.int32)
    depth_code = jnp.where(counts > 0, depth_plane[0], -1).astype(jnp.bfloat16)

    tag_block = jnp.pad(depth_code, (0, channels * 128 - units)).reshape(channels, 128)
    mine, partner, bit = gather_view(
        jnp.concatenate([ref_feat[0], tag_block], axis=1)[None], split=True
    )
    corr_all = correlate(
        blk, blocks, weight_table.reshape(slots * block_width, tpix), mine, partner, bit, units
    )
    corr_all, kern_one, kern_two = lax.optimization_barrier((corr_all, kern_one, kern_two))
    first = banded(kern_one, DEPTH // 4)
    second = banded(kern_two, DEPTH // 4)
    arriving = lax.all_to_all(
        corr_all.reshape(owners, cap * GROUPS, tpix),
        "view",
        split_axis=0,
        concat_axis=0,
        tiled=True,
    ).reshape(owners * cap, GROUPS, tpix)
    arriving, first, second = lax.optimization_barrier((arriving, first, second))
    if bit is None:
        tag_rows = mine[:, :, tpix:]
    else:
        own, other = mine[:, :, tpix:], partner[:, :, tpix:]
        tag_rows = jnp.where(
            bit == 0, jnp.stack([own, other], axis=1), jnp.stack([other, own], axis=1)
        )
    depth_tags = lax.dynamic_slice_in_dim(
        tag_rows.reshape(owners, channels * 128), lax.axis_index("view") * cap, cap, axis=1
    ).reshape(owners * cap)
    labels = jnp.arange(-1, DEPTH + 1).at[0].set(-2)
    onehot = (
        depth_tags[None, :] == labels.astype(jnp.bfloat16)[:, None]
    ).astype(jnp.bfloat16)
    summed = jnp.einsum("dn,ngp->dgp", onehot, arriving, preferred_element_type=jnp.float32)
    tallies = jnp.sum(onehot.astype(jnp.float32), axis=1)
    cost_volume = (summed / jnp.maximum(tallies, 1.0)[:, None, None]).astype(jnp.bfloat16)
    columns = tpix // TROWS
    volume = cost_volume.reshape((DEPTH + 2) * GROUPS, TROWS * columns)
    count = lax.axis_size("view")
    place = lax.axis_index("view")
    ends = jnp.stack([place == 0, place == count - 1]).astype(jnp.int32)
    count = lax.axis_size("view")
    forward = [(i, i + 1) for i in range(count - 1)]
    backward = [(target, source) for source, target in forward]
    low = lax.ppermute(volume[:, volume.shape[1] - 2 * columns :], "view", forward)
    high = lax.ppermute(volume[:, : 2 * columns], "view", backward)
    scores = conv_pair(
        ends,
        low,
        volume,
        high,
        first,
        second,
        TROWS,
        columns,
    )
    return scores


def solution(mesh):
    in_specs = (
        P(("scene", "view"), None, None),
        P(("scene", "view"), None, None),
        P(),
        P(("scene", "view"), None, None),
        P(("scene", "view"), None, None),
        P(("scene", "view"), None),
        P(("scene", "view"), None),
        P(),
        P(),
    )
    out_specs = P(("scene", "view"), None, None)
    return jax.shard_map(body, mesh=mesh, in_specs=in_specs, out_specs=out_specs, check_vma=False)
```

```python
import functools

import jax
import jax.numpy as jnp
from jax import lax
from jax.experimental import pallas as pl
from jax.experimental.pallas import tpu as pltpu
from jax.sharding import PartitionSpec as P

GROUPS = 8
DEPTH = 64
TROWS = 4


def with_halo(block, sides, width):
    for axis, dim in sides:
        count = lax.axis_size(axis)
        forward = [(i, i + 1) for i in range(count - 1)]
        backward = [(target, source) for source, target in forward]
        low = lax.ppermute(
            lax.slice_in_dim(block, block.shape[dim] - width, None, axis=dim), axis, forward
        )
        high = lax.ppermute(lax.slice_in_dim(block, 0, width, axis=dim), axis, backward)
        block = jnp.concatenate([low, block, high], axis=dim)
    return block


def convolve_full(padded, kernel):
    rows_out = padded.shape[0] - 2
    depth_len = padded.shape[2]
    columns = padded.shape[3]
    framed = jnp.pad(padded, ((0, 0), (0, 0), (1, 1), (1, 1)))
    carried = jnp.zeros((rows_out, kernel.shape[-1], depth_len, columns), jnp.float32)
    for depth_off in range(3):
        for row_off in range(3):
            for col_off in range(3):
                window = framed[
                    row_off : row_off + rows_out,
                    :,
                    depth_off : depth_off + depth_len,
                    col_off : col_off + columns,
                ]
                carried = carried + jnp.einsum(
                    "rcdw,ce->redw",
                    window,
                    kernel[depth_off, row_off, col_off],
                    preferred_element_type=jnp.float32,
                )
    return carried


def convolve_final(padded, kernel):
    rows_out = padded.shape[0] - 2
    depth_len = padded.shape[2]
    columns = padded.shape[3]
    framed = jnp.pad(padded, ((0, 0), (0, 0), (1, 1), (1, 1)))
    carried = jnp.zeros((rows_out, depth_len, columns), jnp.float32)
    for depth_off in range(3):
        for row_off in range(3):
            for col_off in range(3):
                window = framed[
                    row_off : row_off + rows_out,
                    :,
                    depth_off : depth_off + depth_len,
                    col_off : col_off + columns,
                ]
                carried = carried + jnp.einsum(
                    "rcdw,c->rdw",
                    window,
                    kernel[depth_off, row_off, col_off],
                    preferred_element_type=jnp.float32,
                )
    return carried


def correlate_kernel(blk_ref, blocks_ref, table_ref, ref_ref, out_ref, arranged, products):
    chunk = 32
    slots = table_ref.shape[0] // blocks_ref.shape[2]
    width = blocks_ref.shape[2]
    channels = blocks_ref.shape[1]
    units = out_ref.shape[0] // GROUPS
    cap = units // ref_ref.shape[0]
    group_size = channels // GROUPS
    rows = chunk * channels

    def step(c, carry):
        for u in range(chunk):
            unit = c * chunk + u
            for w in range(slots):
                arranged[u * channels : (u + 1) * channels, w * width : (w + 1) * width] = blocks_ref[
                    blk_ref[unit * slots + w]
                ]
        warped = jnp.dot(arranged[...], table_ref[...], preferred_element_type=jnp.float32)
        warped = warped.astype(jnp.bfloat16).astype(jnp.float32)
        lanes = products.shape[0]
        for u in range(chunk):
            unit = c * chunk + u
            tile = ref_ref[unit // cap].astype(jnp.float32)
            for j in range(lanes):
                products[j, u * channels : (u + 1) * channels, :] = (
                    warped[u * channels : (u + 1) * channels, j * 128 : (j + 1) * 128]
                    * tile[:, j * 128 : (j + 1) * 128]
                )
        start = pl.multiple_of(c * (chunk * GROUPS), chunk * GROUPS)
        for j in range(lanes):
            total = products[j, pl.ds(0, rows // group_size, stride=group_size), :]
            for k in range(1, group_size):
                total = total + products[j, pl.ds(k, rows // group_size, stride=group_size), :]
            out_ref[pl.ds(start, chunk * GROUPS), j * 128 : (j + 1) * 128] = (
                total * (GROUPS / channels)
            ).astype(out_ref.dtype)
        return carry

    lax.fori_loop(0, units // chunk, step, 0, unroll=True)


def correlate(blk, blocks, table, refs, units):
    channels, width = blocks.shape[1], blocks.shape[2]
    tpix = table.shape[1]
    chunk = 32
    return pl.pallas_call(
        correlate_kernel,
        out_shape=jax.ShapeDtypeStruct((units * GROUPS, tpix), jnp.bfloat16),
        in_specs=[
            pl.BlockSpec(memory_space=pltpu.SMEM),
            pl.BlockSpec(memory_space=pltpu.VMEM),
            pl.BlockSpec(memory_space=pltpu.VMEM),
            pl.BlockSpec(memory_space=pltpu.VMEM),
        ],
        out_specs=pl.BlockSpec(memory_space=pltpu.VMEM),
        scratch_shapes=[
            pltpu.VMEM((chunk * channels, table.shape[0]), jnp.bfloat16),
            pltpu.VMEM((tpix // 128, chunk * channels, 128), jnp.float32),
        ],
    )(blk, blocks, table, refs)


def conv_body(x_ref, m_ref, out_ref, ends_ref, *, relu, rows, cols, groups, chunk):
    width = rows * cols
    outs = m_ref.shape[2]
    depth = x_ref.shape[0] // groups - 2
    lane = lax.broadcasted_iota(jnp.int32, (outs, width), 1) % cols
    for k in range(depth // chunk):
        acc = None
        for e in range(3):
            y = None
            for b in range(3):
                window = x_ref[k * chunk * groups : (k * chunk + chunk + 2) * groups, b * cols : b * cols + width]
                part = jnp.dot(m_ref[b, e], window, preferred_element_type=jnp.float32)
                y = part if y is None else y + part
            if e == 0:
                y = jnp.where(lane >= 1, pltpu.roll(y, 1, 1), 0.0)
            elif e == 2:
                y = jnp.where(lane <= cols - 2, pltpu.roll(y, width - 1, 1), 0.0)
            acc = y if acc is None else acc + y
        if relu:
            block = lax.broadcasted_iota(jnp.int32, (outs, width), 1) // cols
            outside = ((block == 0) & (ends_ref[0] > 0)) | ((block == rows - 1) & (ends_ref[1] > 0))
            acc = jnp.where(outside, 0.0, acc)
            out_ref[(k * chunk + 1) * outs // chunk : (k * chunk + chunk + 1) * outs // chunk, :] = (
                jnp.maximum(acc, 0.0).astype(out_ref.dtype)
            )
        else:
            for r in range(rows):
                out_ref[r, k * chunk : (k + 1) * chunk, :] = acc[:, r * cols : (r + 1) * cols]
    if relu:
        pad = jnp.zeros((outs // chunk, width), out_ref.dtype)
        out_ref[: outs // chunk, :] = pad
        out_ref[out_ref.shape[0] - outs // chunk :, :] = pad


def banded(kernel, chunk):
    groups = kernel.shape[3]
    cols = (chunk + 2) * groups
    taps = kernel.reshape((3, 9) + kernel.shape[3:])
    col = lax.iota(jnp.int32, cols)
    spread = (col[None, :] % groups == jnp.arange(groups)[:, None]).astype(kernel.dtype)
    if kernel.ndim == 5:
        outs = kernel.shape[4]
        rows = chunk * outs
        row = lax.iota(jnp.int32, rows)
        lanes = jnp.einsum("xyio,ic->xyoc", taps, spread, preferred_element_type=jnp.float32)
        tiles = jnp.broadcast_to(lanes[:, :, None], (3, 9, chunk, outs, cols)).reshape(3, 9, rows, cols)
        depth_of_row = row // outs
    else:
        rows = chunk
        lanes = jnp.einsum("xyi,ic->xyc", taps, spread, preferred_element_type=jnp.float32)
        tiles = lanes[:, :, None, :]
        depth_of_row = lax.iota(jnp.int32, rows)
    band = col[None, None, :] // groups == depth_of_row[None, :, None] + jnp.arange(3)[:, None, None]
    mats = jnp.sum(jnp.where(band[:, None], tiles, 0.0), axis=0)
    return mats.astype(kernel.dtype).reshape(3, 3, rows, cols)


def conv_pair_kernel(
    ends_ref, low_ref, vol_ref, high_ref, m1_ref, m2_ref, out_ref, framed, hidden, *, rows, cols, groups
):
    halo = low_ref.shape[1]
    middle = vol_ref.shape[1]
    framed[:, :halo] = low_ref[...]
    framed[:, halo : halo + middle] = vol_ref[...]
    framed[:, halo + middle :] = high_ref[...]
    depth = framed.shape[0] // groups - 2
    first = m1_ref.shape[3] // groups - 2
    conv_body(
        framed, m1_ref, hidden, ends_ref, relu=True, rows=rows + 2, cols=cols, groups=groups, chunk=first
    )
    conv_body(
        hidden,
        m2_ref,
        out_ref,
        None,
        relu=False,
        rows=rows,
        cols=cols,
        groups=groups,
        chunk=m2_ref.shape[2],
    )


def conv_pair(ends, low, volume, high, first, second, rows, cols):
    groups = second.shape[3] // (second.shape[2] + 2)
    depth = volume.shape[0] // groups - 2
    outs = first.shape[2] * depth // (first.shape[3] // groups - 2)
    vmem = pl.BlockSpec(memory_space=pltpu.VMEM)
    return pl.pallas_call(
        functools.partial(conv_pair_kernel, rows=rows, cols=cols, groups=groups),
        out_shape=jax.ShapeDtypeStruct((rows, depth, cols), jnp.float32),
        in_specs=[pl.BlockSpec(memory_space=pltpu.SMEM)] + [vmem] * 5,
        out_specs=vmem,
        scratch_shapes=[
            pltpu.VMEM((volume.shape[0], volume.shape[1] + low.shape[1] + high.shape[1]), volume.dtype),
            pltpu.VMEM(((depth + 2) * outs // depth, (rows + 2) * cols), jnp.bfloat16),
        ],
    )(ends, low, volume, high, first, second)


def halo_cols(block, cols):
    count = lax.axis_size("view")
    forward = [(i, i + 1) for i in range(count - 1)]
    backward = [(target, source) for source, target in forward]
    low = lax.ppermute(block[:, block.shape[1] - cols :], "view", forward)
    high = lax.ppermute(block[:, :cols], "view", backward)
    return jnp.concatenate([low, block, high], axis=1)


def gather_view(block):
    count = lax.axis_size("view")
    if count & (count - 1):
        return lax.all_to_all(
            jnp.broadcast_to(block, (count,) + block.shape[1:]), "view", 0, 0, tiled=True
        )
    index = lax.axis_index("view")
    gathered = block[0]
    level = 0
    stride = count // 2
    if count >= 4:
        top = count // 4
        parts = [gathered] + [
            lax.ppermute(gathered, "view", [(i, i ^ (m * top)) for i in range(count)])
            for m in (1, 2, 3)
        ]
        order = jnp.arange(4) ^ ((index // top) % 4)
        gathered = jnp.take(jnp.stack(parts), order, axis=0).reshape((2, 2) + gathered.shape)
        level = 2
        stride = top // 2
    while stride >= 1:
        other = lax.ppermute(gathered, "view", [(i, i ^ stride) for i in range(count)])
        low = (index // stride) % 2 == 0
        gathered = jnp.where(
            low, jnp.stack([gathered, other], axis=level), jnp.stack([other, gathered], axis=level)
        )
        level += 1
        stride //= 2
    return gathered.reshape((count,) + block.shape[1:])


def pad_rows(volume):
    return with_halo(volume, (("view", 0),), 1)


def body(
    src_feat,
    ref_feat,
    weight_table,
    src_block,
    table_index,
    block_count,
    depth_plane,
    kern_one,
    kern_two,
):
    owners = lax.axis_size("view")
    features = src_feat[0]
    channels, spix = features.shape
    slots, block_width, tpix = weight_table.shape
    blocks = features.reshape(channels, spix // block_width, block_width).transpose(1, 0, 2)
    units = src_block.shape[1]
    cap = units // owners
    counts = block_count[0]
    nblocks = spix // block_width
    blocks = jnp.concatenate([blocks, jnp.zeros_like(blocks[:1])], axis=0)
    matches = table_index[0][:, :, None] == jnp.arange(slots)[None, None, :]
    live = (jnp.arange(slots)[None, :] < counts[:, None])[:, :, None] & matches
    picked = jnp.sum(jnp.where(matches, src_block[0][:, :, None], 0), axis=1)
    alive = jnp.any(live, axis=1)
    blk = jnp.where(alive, picked, nblocks).reshape(-1).astype(jnp.int32)
    depth_code = jnp.where(counts > 0, depth_plane[0], -1).astype(jnp.bfloat16)

    tag_block = jnp.pad(depth_code, (0, channels * 128 - units)).reshape(channels, 128)
    ref_all = gather_view(jnp.concatenate([ref_feat[0], tag_block], axis=1)[None])
    corr_all = correlate(
        blk, blocks, weight_table.reshape(slots * block_width, tpix), ref_all, units
    )
    corr_all, kern_one, kern_two = lax.optimization_barrier((corr_all, kern_one, kern_two))
    first = banded(kern_one, DEPTH // 4)
    second = banded(kern_two, DEPTH // 4)
    arriving = lax.all_to_all(
        corr_all.reshape(owners, cap * GROUPS, tpix),
        "view",
        split_axis=0,
        concat_axis=0,
        tiled=True,
    ).reshape(owners * cap, GROUPS, tpix)
    arriving, first, second = lax.optimization_barrier((arriving, first, second))
    depth_tags = lax.dynamic_slice_in_dim(
        ref_all[:, :, tpix:].reshape(owners, channels * 128), lax.axis_index("view") * cap, cap, axis=1
    ).reshape(owners * cap)
    labels = jnp.arange(-1, DEPTH + 1).at[0].set(-2)
    onehot = (
        depth_tags[None, :] == labels.astype(jnp.bfloat16)[:, None]
    ).astype(jnp.bfloat16)
    summed = jnp.einsum("dn,ngp->dgp", onehot, arriving, preferred_element_type=jnp.float32)
    tallies = jnp.sum(onehot.astype(jnp.float32), axis=1)
    cost_volume = (summed / jnp.maximum(tallies, 1.0)[:, None, None]).astype(jnp.bfloat16)
    columns = tpix // TROWS
    volume = cost_volume.reshape((DEPTH + 2) * GROUPS, TROWS * columns)
    count = lax.axis_size("view")
    place = lax.axis_index("view")
    ends = jnp.stack([place == 0, place == count - 1]).astype(jnp.int32)
    count = lax.axis_size("view")
    forward = [(i, i + 1) for i in range(count - 1)]
    backward = [(target, source) for source, target in forward]
    low = lax.ppermute(volume[:, volume.shape[1] - 2 * columns :], "view", forward)
    high = lax.ppermute(volume[:, : 2 * columns], "view", backward)
    scores = conv_pair(
        ends,
        low,
        volume,
        high,
        first,
        second,
        TROWS,
        columns,
    )
    return scores


def solution(mesh):
    in_specs = (
        P(("scene", "view"), None, None),
        P(("scene", "view"), None, None),
        P(),
        P(("scene", "view"), None, None),
        P(("scene", "view"), None, None),
        P(("scene", "view"), None),
        P(("scene", "view"), None),
        P(),
        P(),
    )
    out_specs = P(("scene", "view"), None, None)
    return jax.shard_map(body, mesh=mesh, in_specs=in_specs, out_specs=out_specs, check_vma=False)
```

```python
import functools

import jax
import jax.numpy as jnp
from jax import lax
from jax.experimental import pallas as pl
from jax.experimental.pallas import tpu as pltpu
from jax.sharding import PartitionSpec as P

GROUPS = 8
DEPTH = 64
TROWS = 4


def with_halo(block, sides, width):
    for axis, dim in sides:
        count = lax.axis_size(axis)
        forward = [(i, i + 1) for i in range(count - 1)]
        backward = [(target, source) for source, target in forward]
        low = lax.ppermute(
            lax.slice_in_dim(block, block.shape[dim] - width, None, axis=dim), axis, forward
        )
        high = lax.ppermute(lax.slice_in_dim(block, 0, width, axis=dim), axis, backward)
        block = jnp.concatenate([low, block, high], axis=dim)
    return block


def convolve_full(padded, kernel):
    rows_out = padded.shape[0] - 2
    depth_len = padded.shape[2]
    columns = padded.shape[3]
    framed = jnp.pad(padded, ((0, 0), (0, 0), (1, 1), (1, 1)))
    carried = jnp.zeros((rows_out, kernel.shape[-1], depth_len, columns), jnp.float32)
    for depth_off in range(3):
        for row_off in range(3):
            for col_off in range(3):
                window = framed[
                    row_off : row_off + rows_out,
                    :,
                    depth_off : depth_off + depth_len,
                    col_off : col_off + columns,
                ]
                carried = carried + jnp.einsum(
                    "rcdw,ce->redw",
                    window,
                    kernel[depth_off, row_off, col_off],
                    preferred_element_type=jnp.float32,
                )
    return carried


def convolve_final(padded, kernel):
    rows_out = padded.shape[0] - 2
    depth_len = padded.shape[2]
    columns = padded.shape[3]
    framed = jnp.pad(padded, ((0, 0), (0, 0), (1, 1), (1, 1)))
    carried = jnp.zeros((rows_out, depth_len, columns), jnp.float32)
    for depth_off in range(3):
        for row_off in range(3):
            for col_off in range(3):
                window = framed[
                    row_off : row_off + rows_out,
                    :,
                    depth_off : depth_off + depth_len,
                    col_off : col_off + columns,
                ]
                carried = carried + jnp.einsum(
                    "rcdw,c->rdw",
                    window,
                    kernel[depth_off, row_off, col_off],
                    preferred_element_type=jnp.float32,
                )
    return carried


def correlate_kernel(blk_ref, blocks_ref, table_ref, ref_ref, out_ref, arranged, products):
    chunk = 32
    slots = table_ref.shape[0] // blocks_ref.shape[2]
    width = blocks_ref.shape[2]
    channels = blocks_ref.shape[1]
    units = out_ref.shape[0] // GROUPS
    cap = units // ref_ref.shape[0]
    group_size = channels // GROUPS
    rows = chunk * channels

    def step(c, carry):
        for u in range(chunk):
            unit = c * chunk + u
            for w in range(slots):
                arranged[u * channels : (u + 1) * channels, w * width : (w + 1) * width] = blocks_ref[
                    blk_ref[unit * slots + w]
                ]
        warped = jnp.dot(arranged[...], table_ref[...], preferred_element_type=jnp.float32)
        warped = warped.astype(jnp.bfloat16).astype(jnp.float32)
        lanes = products.shape[0]
        for u in range(chunk):
            unit = c * chunk + u
            tile = ref_ref[unit // cap].astype(jnp.float32)
            for j in range(lanes):
                products[j, u * channels : (u + 1) * channels, :] = (
                    warped[u * channels : (u + 1) * channels, j * 128 : (j + 1) * 128]
                    * tile[:, j * 128 : (j + 1) * 128]
                )
        start = pl.multiple_of(c * (chunk * GROUPS), chunk * GROUPS)
        for j in range(lanes):
            total = products[j, pl.ds(0, rows // group_size, stride=group_size), :]
            for k in range(1, group_size):
                total = total + products[j, pl.ds(k, rows // group_size, stride=group_size), :]
            out_ref[pl.ds(start, chunk * GROUPS), j * 128 : (j + 1) * 128] = (
                total * (GROUPS / channels)
            ).astype(out_ref.dtype)
        return carry

    lax.fori_loop(0, units // chunk, step, 0, unroll=True)


def correlate(blk, blocks, table, refs, units):
    channels, width = blocks.shape[1], blocks.shape[2]
    tpix = table.shape[1]
    chunk = 32
    return pl.pallas_call(
        correlate_kernel,
        out_shape=jax.ShapeDtypeStruct((units * GROUPS, tpix), jnp.bfloat16),
        in_specs=[
            pl.BlockSpec(memory_space=pltpu.SMEM),
            pl.BlockSpec(memory_space=pltpu.VMEM),
            pl.BlockSpec(memory_space=pltpu.VMEM),
            pl.BlockSpec(memory_space=pltpu.VMEM),
        ],
        out_specs=pl.BlockSpec(memory_space=pltpu.VMEM),
        scratch_shapes=[
            pltpu.VMEM((chunk * channels, table.shape[0]), jnp.bfloat16),
            pltpu.VMEM((tpix // 128, chunk * channels, 128), jnp.float32),
        ],
    )(blk, blocks, table, refs)


def conv_body(x_ref, m_ref, out_ref, ends_ref, *, relu, rows, cols, groups, chunk):
    width = rows * cols
    outs = m_ref.shape[2]
    depth = x_ref.shape[0] // groups - 2
    lane = lax.broadcasted_iota(jnp.int32, (outs, width), 1) % cols
    for k in range(depth // chunk):
        acc = None
        for e in range(3):
            y = None
            for b in range(3):
                window = x_ref[k * chunk * groups : (k * chunk + chunk + 2) * groups, b * cols : b * cols + width]
                part = jnp.dot(m_ref[b, e], window, preferred_element_type=jnp.float32)
                y = part if y is None else y + part
            if e == 0:
                y = jnp.where(lane >= 1, pltpu.roll(y, 1, 1), 0.0)
            elif e == 2:
                y = jnp.where(lane <= cols - 2, pltpu.roll(y, width - 1, 1), 0.0)
            acc = y if acc is None else acc + y
        if relu:
            block = lax.broadcasted_iota(jnp.int32, (outs, width), 1) // cols
            outside = ((block == 0) & (ends_ref[0] > 0)) | ((block == rows - 1) & (ends_ref[1] > 0))
            acc = jnp.where(outside, 0.0, acc)
            out_ref[(k * chunk + 1) * outs // chunk : (k * chunk + chunk + 1) * outs // chunk, :] = (
                jnp.maximum(acc, 0.0).astype(out_ref.dtype)
            )
        else:
            for r in range(rows):
                out_ref[r, k * chunk : (k + 1) * chunk, :] = acc[:, r * cols : (r + 1) * cols]
    if relu:
        pad = jnp.zeros((outs // chunk, width), out_ref.dtype)
        out_ref[: outs // chunk, :] = pad
        out_ref[out_ref.shape[0] - outs // chunk :, :] = pad


def banded(kernel, chunk):
    groups = kernel.shape[3]
    cols = (chunk + 2) * groups
    taps = kernel.reshape((3, 9) + kernel.shape[3:])
    col = lax.iota(jnp.int32, cols)
    spread = (col[None, :] % groups == jnp.arange(groups)[:, None]).astype(kernel.dtype)
    if kernel.ndim == 5:
        outs = kernel.shape[4]
        rows = chunk * outs
        row = lax.iota(jnp.int32, rows)
        lanes = jnp.einsum("xyio,ic->xyoc", taps, spread, preferred_element_type=jnp.float32)
        tiles = jnp.broadcast_to(lanes[:, :, None], (3, 9, chunk, outs, cols)).reshape(3, 9, rows, cols)
        depth_of_row = row // outs
    else:
        rows = chunk
        lanes = jnp.einsum("xyi,ic->xyc", taps, spread, preferred_element_type=jnp.float32)
        tiles = lanes[:, :, None, :]
        depth_of_row = lax.iota(jnp.int32, rows)
    band = col[None, None, :] // groups == depth_of_row[None, :, None] + jnp.arange(3)[:, None, None]
    mats = jnp.sum(jnp.where(band[:, None], tiles, 0.0), axis=0)
    return mats.astype(kernel.dtype).reshape(3, 3, rows, cols)


def conv_pair_kernel(
    ends_ref, low_ref, vol_ref, high_ref, m1_ref, m2_ref, out_ref, framed, hidden, *, rows, cols, groups
):
    halo = low_ref.shape[1]
    middle = vol_ref.shape[1]
    framed[:, :halo] = low_ref[...]
    framed[:, halo : halo + middle] = vol_ref[...]
    framed[:, halo + middle :] = high_ref[...]
    depth = framed.shape[0] // groups - 2
    first = m1_ref.shape[3] // groups - 2
    conv_body(
        framed, m1_ref, hidden, ends_ref, relu=True, rows=rows + 2, cols=cols, groups=groups, chunk=first
    )
    conv_body(
        hidden,
        m2_ref,
        out_ref,
        None,
        relu=False,
        rows=rows,
        cols=cols,
        groups=groups,
        chunk=m2_ref.shape[2],
    )


def conv_pair(ends, low, volume, high, first, second, rows, cols):
    groups = second.shape[3] // (second.shape[2] + 2)
    depth = volume.shape[0] // groups - 2
    outs = first.shape[2] * depth // (first.shape[3] // groups - 2)
    vmem = pl.BlockSpec(memory_space=pltpu.VMEM)
    return pl.pallas_call(
        functools.partial(conv_pair_kernel, rows=rows, cols=cols, groups=groups),
        out_shape=jax.ShapeDtypeStruct((rows, depth, cols), jnp.float32),
        in_specs=[pl.BlockSpec(memory_space=pltpu.SMEM)] + [vmem] * 5,
        out_specs=vmem,
        scratch_shapes=[
            pltpu.VMEM((volume.shape[0], volume.shape[1] + low.shape[1] + high.shape[1]), volume.dtype),
            pltpu.VMEM(((depth + 2) * outs // depth, (rows + 2) * cols), jnp.bfloat16),
        ],
    )(ends, low, volume, high, first, second)


def halo_cols(block, cols):
    count = lax.axis_size("view")
    forward = [(i, i + 1) for i in range(count - 1)]
    backward = [(target, source) for source, target in forward]
    low = lax.ppermute(block[:, block.shape[1] - cols :], "view", forward)
    high = lax.ppermute(block[:, :cols], "view", backward)
    return jnp.concatenate([low, block, high], axis=1)


def gather_view(block):
    count = lax.axis_size("view")
    if count & (count - 1):
        return lax.all_to_all(
            jnp.broadcast_to(block, (count,) + block.shape[1:]), "view", 0, 0, tiled=True
        )
    index = lax.axis_index("view")
    gathered = block[0]
    level = 0
    stride = count // 2
    if count >= 4:
        top = count // 4
        parts = [gathered] + [
            lax.ppermute(gathered, "view", [(i, i ^ (m * top)) for i in range(count)])
            for m in (1, 2, 3)
        ]
        order = jnp.arange(4) ^ ((index // top) % 4)
        gathered = jnp.take(jnp.stack(parts), order, axis=0).reshape((2, 2) + gathered.shape)
        level = 2
        stride = top // 2
    while stride >= 1:
        other = lax.ppermute(gathered, "view", [(i, i ^ stride) for i in range(count)])
        low = (index // stride) % 2 == 0
        gathered = jnp.where(
            low, jnp.stack([gathered, other], axis=level), jnp.stack([other, gathered], axis=level)
        )
        level += 1
        stride //= 2
    return gathered.reshape((count,) + block.shape[1:])


def pad_rows(volume):
    return with_halo(volume, (("view", 0),), 1)


def body(
    src_feat,
    ref_feat,
    weight_table,
    src_block,
    table_index,
    block_count,
    depth_plane,
    kern_one,
    kern_two,
):
    owners = lax.axis_size("view")
    features = src_feat[0]
    channels, spix = features.shape
    slots, block_width, tpix = weight_table.shape
    blocks = features.reshape(channels, spix // block_width, block_width).transpose(1, 0, 2)
    units = src_block.shape[1]
    cap = units // owners
    counts = block_count[0]
    nblocks = spix // block_width
    blocks = jnp.concatenate([blocks, jnp.zeros_like(blocks[:1])], axis=0)
    matches = table_index[0][:, :, None] == jnp.arange(slots)[None, None, :]
    live = (jnp.arange(slots)[None, :] < counts[:, None])[:, :, None] & matches
    picked = jnp.sum(jnp.where(matches, src_block[0][:, :, None], 0), axis=1)
    alive = jnp.any(live, axis=1)
    blk = jnp.where(alive, picked, nblocks).reshape(-1).astype(jnp.int32)
    depth_code = jnp.where(counts > 0, depth_plane[0], -1).astype(jnp.bfloat16)

    tag_block = jnp.pad(depth_code, (0, channels * 128 - units)).reshape(channels, 128)
    ref_all = gather_view(jnp.concatenate([ref_feat[0], tag_block], axis=1)[None])
    corr_all = correlate(
        blk, blocks, weight_table.reshape(slots * block_width, tpix), ref_all, units
    )
    corr_all, kern_one, kern_two = lax.optimization_barrier((corr_all, kern_one, kern_two))
    first = banded(kern_one, DEPTH // 8)
    second = banded(kern_two, DEPTH // 4)
    arriving = lax.all_to_all(
        corr_all.reshape(owners, cap * GROUPS, tpix),
        "view",
        split_axis=0,
        concat_axis=0,
        tiled=True,
    ).reshape(owners * cap, GROUPS, tpix)
    arriving, first, second = lax.optimization_barrier((arriving, first, second))
    depth_tags = lax.dynamic_slice_in_dim(
        ref_all[:, :, tpix:].reshape(owners, channels * 128), lax.axis_index("view") * cap, cap, axis=1
    ).reshape(owners * cap)
    labels = jnp.arange(-1, DEPTH + 1).at[0].set(-2)
    onehot = (
        depth_tags[None, :] == labels.astype(jnp.bfloat16)[:, None]
    ).astype(jnp.bfloat16)
    summed = jnp.einsum("dn,ngp->dgp", onehot, arriving, preferred_element_type=jnp.float32)
    tallies = jnp.sum(onehot.astype(jnp.float32), axis=1)
    cost_volume = (summed / jnp.maximum(tallies, 1.0)[:, None, None]).astype(jnp.bfloat16)
    columns = tpix // TROWS
    volume = cost_volume.reshape((DEPTH + 2) * GROUPS, TROWS * columns)
    count = lax.axis_size("view")
    place = lax.axis_index("view")
    ends = jnp.stack([place == 0, place == count - 1]).astype(jnp.int32)
    count = lax.axis_size("view")
    forward = [(i, i + 1) for i in range(count - 1)]
    backward = [(target, source) for source, target in forward]
    low = lax.ppermute(volume[:, volume.shape[1] - 2 * columns :], "view", forward)
    high = lax.ppermute(volume[:, : 2 * columns], "view", backward)
    scores = conv_pair(
        ends,
        low,
        volume,
        high,
        first,
        second,
        TROWS,
        columns,
    )
    return scores


def solution(mesh):
    in_specs = (
        P(("scene", "view"), None, None),
        P(("scene", "view"), None, None),
        P(),
        P(("scene", "view"), None, None),
        P(("scene", "view"), None, None),
        P(("scene", "view"), None),
        P(("scene", "view"), None),
        P(),
        P(),
    )
    out_specs = P(("scene", "view"), None, None)
    return jax.shard_map(body, mesh=mesh, in_specs=in_specs, out_specs=out_specs, check_vma=False)
```

```python
import functools

import jax
import jax.numpy as jnp
from jax import lax
from jax.experimental import pallas as pl
from jax.experimental.pallas import tpu as pltpu
from jax.sharding import PartitionSpec as P

GROUPS = 8
DEPTH = 64
TROWS = 4


def with_halo(block, sides, width):
    for axis, dim in sides:
        count = lax.axis_size(axis)
        forward = [(i, i + 1) for i in range(count - 1)]
        backward = [(target, source) for source, target in forward]
        low = lax.ppermute(
            lax.slice_in_dim(block, block.shape[dim] - width, None, axis=dim), axis, forward
        )
        high = lax.ppermute(lax.slice_in_dim(block, 0, width, axis=dim), axis, backward)
        block = jnp.concatenate([low, block, high], axis=dim)
    return block


def convolve_full(padded, kernel):
    rows_out = padded.shape[0] - 2
    depth_len = padded.shape[2]
    columns = padded.shape[3]
    framed = jnp.pad(padded, ((0, 0), (0, 0), (1, 1), (1, 1)))
    carried = jnp.zeros((rows_out, kernel.shape[-1], depth_len, columns), jnp.float32)
    for depth_off in range(3):
        for row_off in range(3):
            for col_off in range(3):
                window = framed[
                    row_off : row_off + rows_out,
                    :,
                    depth_off : depth_off + depth_len,
                    col_off : col_off + columns,
                ]
                carried = carried + jnp.einsum(
                    "rcdw,ce->redw",
                    window,
                    kernel[depth_off, row_off, col_off],
                    preferred_element_type=jnp.float32,
                )
    return carried


def convolve_final(padded, kernel):
    rows_out = padded.shape[0] - 2
    depth_len = padded.shape[2]
    columns = padded.shape[3]
    framed = jnp.pad(padded, ((0, 0), (0, 0), (1, 1), (1, 1)))
    carried = jnp.zeros((rows_out, depth_len, columns), jnp.float32)
    for depth_off in range(3):
        for row_off in range(3):
            for col_off in range(3):
                window = framed[
                    row_off : row_off + rows_out,
                    :,
                    depth_off : depth_off + depth_len,
                    col_off : col_off + columns,
                ]
                carried = carried + jnp.einsum(
                    "rcdw,c->rdw",
                    window,
                    kernel[depth_off, row_off, col_off],
                    preferred_element_type=jnp.float32,
                )
    return carried


def correlate_kernel(blk_ref, blocks_ref, table_ref, ref_ref, out_ref, arranged, products):
    chunk = 32
    slots = table_ref.shape[0] // blocks_ref.shape[2]
    width = blocks_ref.shape[2]
    channels = blocks_ref.shape[1]
    units = out_ref.shape[0] // GROUPS
    cap = units // ref_ref.shape[0]
    group_size = channels // GROUPS
    rows = chunk * channels

    def step(c, carry):
        for u in range(chunk):
            unit = c * chunk + u
            for w in range(slots):
                arranged[u * channels : (u + 1) * channels, w * width : (w + 1) * width] = blocks_ref[
                    blk_ref[unit * slots + w]
                ]
        warped = jnp.dot(arranged[...], table_ref[...], preferred_element_type=jnp.float32)
        warped = warped.astype(jnp.bfloat16).astype(jnp.float32)
        lanes = products.shape[0]
        for u in range(chunk):
            unit = c * chunk + u
            tile = ref_ref[unit // cap].astype(jnp.float32)
            for j in range(lanes):
                products[j, u * channels : (u + 1) * channels, :] = (
                    warped[u * channels : (u + 1) * channels, j * 128 : (j + 1) * 128]
                    * tile[:, j * 128 : (j + 1) * 128]
                )
        start = pl.multiple_of(c * (chunk * GROUPS), chunk * GROUPS)
        for j in range(lanes):
            total = products[j, pl.ds(0, rows // group_size, stride=group_size), :]
            for k in range(1, group_size):
                total = total + products[j, pl.ds(k, rows // group_size, stride=group_size), :]
            out_ref[pl.ds(start, chunk * GROUPS), j * 128 : (j + 1) * 128] = (
                total * (GROUPS / channels)
            ).astype(out_ref.dtype)
        return carry

    lax.fori_loop(0, units // chunk, step, 0, unroll=True)


def correlate(blk, blocks, table, refs, units):
    channels, width = blocks.shape[1], blocks.shape[2]
    tpix = table.shape[1]
    chunk = 32
    return pl.pallas_call(
        correlate_kernel,
        out_shape=jax.ShapeDtypeStruct((units * GROUPS, tpix), jnp.bfloat16),
        in_specs=[
            pl.BlockSpec(memory_space=pltpu.SMEM),
            pl.BlockSpec(memory_space=pltpu.VMEM),
            pl.BlockSpec(memory_space=pltpu.VMEM),
            pl.BlockSpec(memory_space=pltpu.VMEM),
        ],
        out_specs=pl.BlockSpec(memory_space=pltpu.VMEM),
        scratch_shapes=[
            pltpu.VMEM((chunk * channels, table.shape[0]), jnp.bfloat16),
            pltpu.VMEM((tpix // 128, chunk * channels, 128), jnp.float32),
        ],
    )(blk, blocks, table, refs)


def conv_body(x_ref, m_ref, out_ref, ends_ref, *, relu, rows, cols, groups, chunk):
    width = rows * cols
    outs = m_ref.shape[2]
    depth = x_ref.shape[0] // groups - 2
    lane = lax.broadcasted_iota(jnp.int32, (outs, width), 1) % cols
    for k in range(depth // chunk):
        acc = None
        for e in range(3):
            y = None
            for b in range(3):
                window = x_ref[k * chunk * groups : (k * chunk + chunk + 2) * groups, b * cols : b * cols + width]
                part = jnp.dot(m_ref[b, e], window, preferred_element_type=jnp.float32)
                y = part if y is None else y + part
            if e == 0:
                y = jnp.where(lane >= 1, pltpu.roll(y, 1, 1), 0.0)
            elif e == 2:
                y = jnp.where(lane <= cols - 2, pltpu.roll(y, width - 1, 1), 0.0)
            acc = y if acc is None else acc + y
        if relu:
            block = lax.broadcasted_iota(jnp.int32, (outs, width), 1) // cols
            outside = ((block == 0) & (ends_ref[0] > 0)) | ((block == rows - 1) & (ends_ref[1] > 0))
            acc = jnp.where(outside, 0.0, acc)
            out_ref[(k * chunk + 1) * outs // chunk : (k * chunk + chunk + 1) * outs // chunk, :] = (
                jnp.maximum(acc, 0.0).astype(out_ref.dtype)
            )
        else:
            for r in range(rows):
                out_ref[r, k * chunk : (k + 1) * chunk, :] = acc[:, r * cols : (r + 1) * cols]
    if relu:
        pad = jnp.zeros((outs // chunk, width), out_ref.dtype)
        out_ref[: outs // chunk, :] = pad
        out_ref[out_ref.shape[0] - outs // chunk :, :] = pad


def banded(kernel, chunk):
    groups = kernel.shape[3]
    cols = (chunk + 2) * groups
    taps = kernel.reshape((3, 9) + kernel.shape[3:])
    col = lax.iota(jnp.int32, cols)
    spread = (col[None, :] % groups == jnp.arange(groups)[:, None]).astype(kernel.dtype)
    if kernel.ndim == 5:
        outs = kernel.shape[4]
        rows = chunk * outs
        row = lax.iota(jnp.int32, rows)
        lanes = jnp.einsum("xyio,ic->xyoc", taps, spread, preferred_element_type=jnp.float32)
        tiles = jnp.broadcast_to(lanes[:, :, None], (3, 9, chunk, outs, cols)).reshape(3, 9, rows, cols)
        depth_of_row = row // outs
    else:
        rows = chunk
        lanes = jnp.einsum("xyi,ic->xyc", taps, spread, preferred_element_type=jnp.float32)
        tiles = lanes[:, :, None, :]
        depth_of_row = lax.iota(jnp.int32, rows)
    band = col[None, None, :] // groups == depth_of_row[None, :, None] + jnp.arange(3)[:, None, None]
    mats = jnp.sum(jnp.where(band[:, None], tiles, 0.0), axis=0)
    return mats.astype(kernel.dtype).reshape(3, 3, rows, cols)


def conv_pair_kernel(
    ends_ref, low_ref, vol_ref, high_ref, m1_ref, m2_ref, out_ref, framed, hidden, *, rows, cols, groups
):
    halo = low_ref.shape[1]
    middle = vol_ref.shape[1]
    framed[:, :halo] = low_ref[...]
    framed[:, halo : halo + middle] = vol_ref[...]
    framed[:, halo + middle :] = high_ref[...]
    depth = framed.shape[0] // groups - 2
    first = m1_ref.shape[3] // groups - 2
    conv_body(
        framed, m1_ref, hidden, ends_ref, relu=True, rows=rows + 2, cols=cols, groups=groups, chunk=first
    )
    conv_body(
        hidden,
        m2_ref,
        out_ref,
        None,
        relu=False,
        rows=rows,
        cols=cols,
        groups=groups,
        chunk=m2_ref.shape[2],
    )


def conv_pair(ends, low, volume, high, first, second, rows, cols):
    groups = second.shape[3] // (second.shape[2] + 2)
    depth = volume.shape[0] // groups - 2
    outs = first.shape[2] * depth // (first.shape[3] // groups - 2)
    vmem = pl.BlockSpec(memory_space=pltpu.VMEM)
    return pl.pallas_call(
        functools.partial(conv_pair_kernel, rows=rows, cols=cols, groups=groups),
        out_shape=jax.ShapeDtypeStruct((rows, depth, cols), jnp.float32),
        in_specs=[pl.BlockSpec(memory_space=pltpu.SMEM)] + [vmem] * 5,
        out_specs=vmem,
        scratch_shapes=[
            pltpu.VMEM((volume.shape[0], volume.shape[1] + low.shape[1] + high.shape[1]), volume.dtype),
            pltpu.VMEM(((depth + 2) * outs // depth, (rows + 2) * cols), jnp.bfloat16),
        ],
    )(ends, low, volume, high, first, second)


def halo_cols(block, cols):
    count = lax.axis_size("view")
    forward = [(i, i + 1) for i in range(count - 1)]
    backward = [(target, source) for source, target in forward]
    low = lax.ppermute(block[:, block.shape[1] - cols :], "view", forward)
    high = lax.ppermute(block[:, :cols], "view", backward)
    return jnp.concatenate([low, block, high], axis=1)


def gather_view(block):
    count = lax.axis_size("view")
    if count & (count - 1):
        return lax.all_to_all(
            jnp.broadcast_to(block, (count,) + block.shape[1:]), "view", 0, 0, tiled=True
        )
    index = lax.axis_index("view")
    gathered = block[0]
    level = 0
    stride = count // 2
    if count >= 4:
        top = count // 4
        parts = [gathered] + [
            lax.ppermute(gathered, "view", [(i, i ^ (m * top)) for i in range(count)])
            for m in (1, 2, 3)
        ]
        order = jnp.arange(4) ^ ((index // top) % 4)
        gathered = jnp.take(jnp.stack(parts), order, axis=0).reshape((2, 2) + gathered.shape)
        level = 2
        stride = top // 2
    while stride >= 1:
        other = lax.ppermute(gathered, "view", [(i, i ^ stride) for i in range(count)])
        low = (index // stride) % 2 == 0
        gathered = jnp.where(
            low, jnp.stack([gathered, other], axis=level), jnp.stack([other, gathered], axis=level)
        )
        level += 1
        stride //= 2
    return gathered.reshape((count,) + block.shape[1:])


def pad_rows(volume):
    return with_halo(volume, (("view", 0),), 1)


def body(
    src_feat,
    ref_feat,
    weight_table,
    src_block,
    table_index,
    block_count,
    depth_plane,
    kern_one,
    kern_two,
):
    owners = lax.axis_size("view")
    features = src_feat[0]
    channels, spix = features.shape
    slots, block_width, tpix = weight_table.shape
    blocks = features.reshape(channels, spix // block_width, block_width).transpose(1, 0, 2)
    units = src_block.shape[1]
    cap = units // owners
    counts = block_count[0]
    nblocks = spix // block_width
    blocks = jnp.concatenate([blocks, jnp.zeros_like(blocks[:1])], axis=0)
    matches = table_index[0][:, :, None] == jnp.arange(slots)[None, None, :]
    live = (jnp.arange(slots)[None, :] < counts[:, None])[:, :, None] & matches
    picked = jnp.sum(jnp.where(matches, src_block[0][:, :, None], 0), axis=1)
    alive = jnp.any(live, axis=1)
    blk = jnp.where(alive, picked, nblocks).reshape(-1).astype(jnp.int32)
    depth_code = jnp.where(counts > 0, depth_plane[0], -1).astype(jnp.bfloat16)

    tag_block = jnp.pad(depth_code, (0, channels * 128 - units)).reshape(channels, 128)
    ref_all = gather_view(jnp.concatenate([ref_feat[0], tag_block], axis=1)[None])
    corr_all = correlate(
        blk, blocks, weight_table.reshape(slots * block_width, tpix), ref_all, units
    )
    corr_all, kern_one, kern_two = lax.optimization_barrier((corr_all, kern_one, kern_two))
    first = banded(kern_one, DEPTH // 2)
    second = banded(kern_two, DEPTH // 4)
    arriving = lax.all_to_all(
        corr_all.reshape(owners, cap * GROUPS, tpix),
        "view",
        split_axis=0,
        concat_axis=0,
        tiled=True,
    ).reshape(owners * cap, GROUPS, tpix)
    arriving, first, second = lax.optimization_barrier((arriving, first, second))
    depth_tags = lax.dynamic_slice_in_dim(
        ref_all[:, :, tpix:].reshape(owners, channels * 128), lax.axis_index("view") * cap, cap, axis=1
    ).reshape(owners * cap)
    labels = jnp.arange(-1, DEPTH + 1).at[0].set(-2)
    onehot = (
        depth_tags[None, :] == labels.astype(jnp.bfloat16)[:, None]
    ).astype(jnp.bfloat16)
    summed = jnp.einsum("dn,ngp->dgp", onehot, arriving, preferred_element_type=jnp.float32)
    tallies = jnp.sum(onehot.astype(jnp.float32), axis=1)
    cost_volume = (summed / jnp.maximum(tallies, 1.0)[:, None, None]).astype(jnp.bfloat16)
    columns = tpix // TROWS
    volume = cost_volume.reshape((DEPTH + 2) * GROUPS, TROWS * columns)
    count = lax.axis_size("view")
    place = lax.axis_index("view")
    ends = jnp.stack([place == 0, place == count - 1]).astype(jnp.int32)
    count = lax.axis_size("view")
    forward = [(i, i + 1) for i in range(count - 1)]
    backward = [(target, source) for source, target in forward]
    low = lax.ppermute(volume[:, volume.shape[1] - 2 * columns :], "view", forward)
    high = lax.ppermute(volume[:, : 2 * columns], "view", backward)
    scores = conv_pair(
        ends,
        low,
        volume,
        high,
        first,
        second,
        TROWS,
        columns,
    )
    return scores


def solution(mesh):
    in_specs = (
        P(("scene", "view"), None, None),
        P(("scene", "view"), None, None),
        P(),
        P(("scene", "view"), None, None),
        P(("scene", "view"), None, None),
        P(("scene", "view"), None),
        P(("scene", "view"), None),
        P(),
        P(),
    )
    out_specs = P(("scene", "view"), None, None)
    return jax.shard_map(body, mesh=mesh, in_specs=in_specs, out_specs=out_specs, check_vma=False)
```

```python
import functools

import jax
import jax.numpy as jnp
from jax import lax
from jax.experimental import pallas as pl
from jax.experimental.pallas import tpu as pltpu
from jax.sharding import PartitionSpec as P

GROUPS = 8
DEPTH = 64
TROWS = 4


def with_halo(block, sides, width):
    for axis, dim in sides:
        count = lax.axis_size(axis)
        forward = [(i, i + 1) for i in range(count - 1)]
        backward = [(target, source) for source, target in forward]
        low = lax.ppermute(
            lax.slice_in_dim(block, block.shape[dim] - width, None, axis=dim), axis, forward
        )
        high = lax.ppermute(lax.slice_in_dim(block, 0, width, axis=dim), axis, backward)
        block = jnp.concatenate([low, block, high], axis=dim)
    return block


def convolve_full(padded, kernel):
    rows_out = padded.shape[0] - 2
    depth_len = padded.shape[2]
    columns = padded.shape[3]
    framed = jnp.pad(padded, ((0, 0), (0, 0), (1, 1), (1, 1)))
    carried = jnp.zeros((rows_out, kernel.shape[-1], depth_len, columns), jnp.float32)
    for depth_off in range(3):
        for row_off in range(3):
            for col_off in range(3):
                window = framed[
                    row_off : row_off + rows_out,
                    :,
                    depth_off : depth_off + depth_len,
                    col_off : col_off + columns,
                ]
                carried = carried + jnp.einsum(
                    "rcdw,ce->redw",
                    window,
                    kernel[depth_off, row_off, col_off],
                    preferred_element_type=jnp.float32,
                )
    return carried


def convolve_final(padded, kernel):
    rows_out = padded.shape[0] - 2
    depth_len = padded.shape[2]
    columns = padded.shape[3]
    framed = jnp.pad(padded, ((0, 0), (0, 0), (1, 1), (1, 1)))
    carried = jnp.zeros((rows_out, depth_len, columns), jnp.float32)
    for depth_off in range(3):
        for row_off in range(3):
            for col_off in range(3):
                window = framed[
                    row_off : row_off + rows_out,
                    :,
                    depth_off : depth_off + depth_len,
                    col_off : col_off + columns,
                ]
                carried = carried + jnp.einsum(
                    "rcdw,c->rdw",
                    window,
                    kernel[depth_off, row_off, col_off],
                    preferred_element_type=jnp.float32,
                )
    return carried


def correlate_kernel(blk_ref, blocks_ref, table_ref, ref_ref, out_ref, arranged, products):
    chunk = 64
    slots = table_ref.shape[0] // blocks_ref.shape[2]
    width = blocks_ref.shape[2]
    channels = blocks_ref.shape[1]
    units = out_ref.shape[0] // GROUPS
    cap = units // ref_ref.shape[0]
    group_size = channels // GROUPS
    rows = chunk * channels

    def step(c, carry):
        for u in range(chunk):
            unit = c * chunk + u
            for w in range(slots):
                arranged[u * channels : (u + 1) * channels, w * width : (w + 1) * width] = blocks_ref[
                    blk_ref[unit * slots + w]
                ]
        warped = jnp.dot(arranged[...], table_ref[...], preferred_element_type=jnp.float32)
        warped = warped.astype(jnp.bfloat16).astype(jnp.float32)
        lanes = products.shape[0]
        for u in range(chunk):
            unit = c * chunk + u
            tile = ref_ref[unit // cap].astype(jnp.float32)
            for j in range(lanes):
                products[j, u * channels : (u + 1) * channels, :] = (
                    warped[u * channels : (u + 1) * channels, j * 128 : (j + 1) * 128]
                    * tile[:, j * 128 : (j + 1) * 128]
                )
        start = pl.multiple_of(c * (chunk * GROUPS), chunk * GROUPS)
        for j in range(lanes):
            total = products[j, pl.ds(0, rows // group_size, stride=group_size), :]
            for k in range(1, group_size):
                total = total + products[j, pl.ds(k, rows // group_size, stride=group_size), :]
            out_ref[pl.ds(start, chunk * GROUPS), j * 128 : (j + 1) * 128] = (
                total * (GROUPS / channels)
            ).astype(out_ref.dtype)
        return carry

    lax.fori_loop(0, units // chunk, step, 0, unroll=True)


def correlate(blk, blocks, table, refs, units):
    channels, width = blocks.shape[1], blocks.shape[2]
    tpix = table.shape[1]
    chunk = 64
    return pl.pallas_call(
        correlate_kernel,
        out_shape=jax.ShapeDtypeStruct((units * GROUPS, tpix), jnp.bfloat16),
        in_specs=[
            pl.BlockSpec(memory_space=pltpu.SMEM),
            pl.BlockSpec(memory_space=pltpu.VMEM),
            pl.BlockSpec(memory_space=pltpu.VMEM),
            pl.BlockSpec(memory_space=pltpu.VMEM),
        ],
        out_specs=pl.BlockSpec(memory_space=pltpu.VMEM),
        scratch_shapes=[
            pltpu.VMEM((chunk * channels, table.shape[0]), jnp.bfloat16),
            pltpu.VMEM((tpix // 128, chunk * channels, 128), jnp.float32),
        ],
    )(blk, blocks, table, refs)


def conv_body(x_ref, m_ref, out_ref, ends_ref, *, relu, rows, cols, groups, chunk):
    width = rows * cols
    outs = m_ref.shape[2]
    depth = x_ref.shape[0] // groups - 2
    lane = lax.broadcasted_iota(jnp.int32, (outs, width), 1) % cols
    for k in range(depth // chunk):
        acc = None
        for e in range(3):
            y = None
            for b in range(3):
                window = x_ref[k * chunk * groups : (k * chunk + chunk + 2) * groups, b * cols : b * cols + width]
                part = jnp.dot(m_ref[b, e], window, preferred_element_type=jnp.float32)
                y = part if y is None else y + part
            if e == 0:
                y = jnp.where(lane >= 1, pltpu.roll(y, 1, 1), 0.0)
            elif e == 2:
                y = jnp.where(lane <= cols - 2, pltpu.roll(y, width - 1, 1), 0.0)
            acc = y if acc is None else acc + y
        if relu:
            block = lax.broadcasted_iota(jnp.int32, (outs, width), 1) // cols
            outside = ((block == 0) & (ends_ref[0] > 0)) | ((block == rows - 1) & (ends_ref[1] > 0))
            acc = jnp.where(outside, 0.0, acc)
            out_ref[(k * chunk + 1) * outs // chunk : (k * chunk + chunk + 1) * outs // chunk, :] = (
                jnp.maximum(acc, 0.0).astype(out_ref.dtype)
            )
        else:
            for r in range(rows):
                out_ref[r, k * chunk : (k + 1) * chunk, :] = acc[:, r * cols : (r + 1) * cols]
    if relu:
        pad = jnp.zeros((outs // chunk, width), out_ref.dtype)
        out_ref[: outs // chunk, :] = pad
        out_ref[out_ref.shape[0] - outs // chunk :, :] = pad


def banded(kernel, chunk):
    groups = kernel.shape[3]
    cols = (chunk + 2) * groups
    taps = kernel.reshape((3, 9) + kernel.shape[3:])
    col = lax.iota(jnp.int32, cols)
    spread = (col[None, :] % groups == jnp.arange(groups)[:, None]).astype(kernel.dtype)
    if kernel.ndim == 5:
        outs = kernel.shape[4]
        rows = chunk * outs
        row = lax.iota(jnp.int32, rows)
        lanes = jnp.einsum("xyio,ic->xyoc", taps, spread, preferred_element_type=jnp.float32)
        tiles = jnp.broadcast_to(lanes[:, :, None], (3, 9, chunk, outs, cols)).reshape(3, 9, rows, cols)
        depth_of_row = row // outs
    else:
        rows = chunk
        lanes = jnp.einsum("xyi,ic->xyc", taps, spread, preferred_element_type=jnp.float32)
        tiles = lanes[:, :, None, :]
        depth_of_row = lax.iota(jnp.int32, rows)
    band = col[None, None, :] // groups == depth_of_row[None, :, None] + jnp.arange(3)[:, None, None]
    mats = jnp.sum(jnp.where(band[:, None], tiles, 0.0), axis=0)
    return mats.astype(kernel.dtype).reshape(3, 3, rows, cols)


def conv_pair_kernel(
    ends_ref, low_ref, vol_ref, high_ref, m1_ref, m2_ref, out_ref, framed, hidden, *, rows, cols, groups
):
    halo = low_ref.shape[1]
    middle = vol_ref.shape[1]
    framed[:, :halo] = low_ref[...]
    framed[:, halo : halo + middle] = vol_ref[...]
    framed[:, halo + middle :] = high_ref[...]
    depth = framed.shape[0] // groups - 2
    first = m1_ref.shape[3] // groups - 2
    conv_body(
        framed, m1_ref, hidden, ends_ref, relu=True, rows=rows + 2, cols=cols, groups=groups, chunk=first
    )
    conv_body(
        hidden,
        m2_ref,
        out_ref,
        None,
        relu=False,
        rows=rows,
        cols=cols,
        groups=groups,
        chunk=m2_ref.shape[2],
    )


def conv_pair(ends, low, volume, high, first, second, rows, cols):
    groups = second.shape[3] // (second.shape[2] + 2)
    depth = volume.shape[0] // groups - 2
    outs = first.shape[2] * depth // (first.shape[3] // groups - 2)
    vmem = pl.BlockSpec(memory_space=pltpu.VMEM)
    return pl.pallas_call(
        functools.partial(conv_pair_kernel, rows=rows, cols=cols, groups=groups),
        out_shape=jax.ShapeDtypeStruct((rows, depth, cols), jnp.float32),
        in_specs=[pl.BlockSpec(memory_space=pltpu.SMEM)] + [vmem] * 5,
        out_specs=vmem,
        scratch_shapes=[
            pltpu.VMEM((volume.shape[0], volume.shape[1] + low.shape[1] + high.shape[1]), volume.dtype),
            pltpu.VMEM(((depth + 2) * outs // depth, (rows + 2) * cols), jnp.bfloat16),
        ],
    )(ends, low, volume, high, first, second)


def halo_cols(block, cols):
    count = lax.axis_size("view")
    forward = [(i, i + 1) for i in range(count - 1)]
    backward = [(target, source) for source, target in forward]
    low = lax.ppermute(block[:, block.shape[1] - cols :], "view", forward)
    high = lax.ppermute(block[:, :cols], "view", backward)
    return jnp.concatenate([low, block, high], axis=1)


def gather_view(block):
    count = lax.axis_size("view")
    if count & (count - 1):
        return lax.all_to_all(
            jnp.broadcast_to(block, (count,) + block.shape[1:]), "view", 0, 0, tiled=True
        )
    index = lax.axis_index("view")
    gathered = block[0]
    level = 0
    stride = count // 2
    if count >= 4:
        top = count // 4
        parts = [gathered] + [
            lax.ppermute(gathered, "view", [(i, i ^ (m * top)) for i in range(count)])
            for m in (1, 2, 3)
        ]
        order = jnp.arange(4) ^ ((index // top) % 4)
        gathered = jnp.take(jnp.stack(parts), order, axis=0).reshape((2, 2) + gathered.shape)
        level = 2
        stride = top // 2
    while stride >= 1:
        other = lax.ppermute(gathered, "view", [(i, i ^ stride) for i in range(count)])
        low = (index // stride) % 2 == 0
        gathered = jnp.where(
            low, jnp.stack([gathered, other], axis=level), jnp.stack([other, gathered], axis=level)
        )
        level += 1
        stride //= 2
    return gathered.reshape((count,) + block.shape[1:])


def pad_rows(volume):
    return with_halo(volume, (("view", 0),), 1)


def body(
    src_feat,
    ref_feat,
    weight_table,
    src_block,
    table_index,
    block_count,
    depth_plane,
    kern_one,
    kern_two,
):
    owners = lax.axis_size("view")
    features = src_feat[0]
    channels, spix = features.shape
    slots, block_width, tpix = weight_table.shape
    blocks = features.reshape(channels, spix // block_width, block_width).transpose(1, 0, 2)
    units = src_block.shape[1]
    cap = units // owners
    counts = block_count[0]
    nblocks = spix // block_width
    blocks = jnp.concatenate([blocks, jnp.zeros_like(blocks[:1])], axis=0)
    matches = table_index[0][:, :, None] == jnp.arange(slots)[None, None, :]
    live = (jnp.arange(slots)[None, :] < counts[:, None])[:, :, None] & matches
    picked = jnp.sum(jnp.where(matches, src_block[0][:, :, None], 0), axis=1)
    alive = jnp.any(live, axis=1)
    blk = jnp.where(alive, picked, nblocks).reshape(-1).astype(jnp.int32)
    depth_code = jnp.where(counts > 0, depth_plane[0], -1).astype(jnp.bfloat16)

    tag_block = jnp.pad(depth_code, (0, channels * 128 - units)).reshape(channels, 128)
    ref_all = gather_view(jnp.concatenate([ref_feat[0], tag_block], axis=1)[None])
    corr_all = correlate(
        blk, blocks, weight_table.reshape(slots * block_width, tpix), ref_all, units
    )
    corr_all, kern_one, kern_two = lax.optimization_barrier((corr_all, kern_one, kern_two))
    first = banded(kern_one, DEPTH // 4)
    second = banded(kern_two, DEPTH // 4)
    arriving = lax.all_to_all(
        corr_all.reshape(owners, cap * GROUPS, tpix),
        "view",
        split_axis=0,
        concat_axis=0,
        tiled=True,
    ).reshape(owners * cap, GROUPS, tpix)
    arriving, first, second = lax.optimization_barrier((arriving, first, second))
    depth_tags = lax.dynamic_slice_in_dim(
        ref_all[:, :, tpix:].reshape(owners, channels * 128), lax.axis_index("view") * cap, cap, axis=1
    ).reshape(owners * cap)
    labels = jnp.arange(-1, DEPTH + 1).at[0].set(-2)
    onehot = (
        depth_tags[None, :] == labels.astype(jnp.bfloat16)[:, None]
    ).astype(jnp.bfloat16)
    summed = jnp.einsum("dn,ngp->dgp", onehot, arriving, preferred_element_type=jnp.float32)
    tallies = jnp.sum(onehot.astype(jnp.float32), axis=1)
    cost_volume = (summed / jnp.maximum(tallies, 1.0)[:, None, None]).astype(jnp.bfloat16)
    columns = tpix // TROWS
    volume = cost_volume.reshape((DEPTH + 2) * GROUPS, TROWS * columns)
    count = lax.axis_size("view")
    place = lax.axis_index("view")
    ends = jnp.stack([place == 0, place == count - 1]).astype(jnp.int32)
    count = lax.axis_size("view")
    forward = [(i, i + 1) for i in range(count - 1)]
    backward = [(target, source) for source, target in forward]
    low = lax.ppermute(volume[:, volume.shape[1] - 2 * columns :], "view", forward)
    high = lax.ppermute(volume[:, : 2 * columns], "view", backward)
    scores = conv_pair(
        ends,
        low,
        volume,
        high,
        first,
        second,
        TROWS,
        columns,
    )
    return scores


def solution(mesh):
    in_specs = (
        P(("scene", "view"), None, None),
        P(("scene", "view"), None, None),
        P(),
        P(("scene", "view"), None, None),
        P(("scene", "view"), None, None),
        P(("scene", "view"), None),
        P(("scene", "view"), None),
        P(),
        P(),
    )
    out_specs = P(("scene", "view"), None, None)
    return jax.shard_map(body, mesh=mesh, in_specs=in_specs, out_specs=out_specs, check_vma=False)
```

```python
import functools

import jax
import jax.numpy as jnp
from jax import lax
from jax.experimental import pallas as pl
from jax.experimental.pallas import tpu as pltpu
from jax.sharding import PartitionSpec as P

GROUPS = 8
DEPTH = 64
TROWS = 4


def with_halo(block, sides, width):
    for axis, dim in sides:
        count = lax.axis_size(axis)
        forward = [(i, i + 1) for i in range(count - 1)]
        backward = [(target, source) for source, target in forward]
        low = lax.ppermute(
            lax.slice_in_dim(block, block.shape[dim] - width, None, axis=dim), axis, forward
        )
        high = lax.ppermute(lax.slice_in_dim(block, 0, width, axis=dim), axis, backward)
        block = jnp.concatenate([low, block, high], axis=dim)
    return block


def convolve_full(padded, kernel):
    rows_out = padded.shape[0] - 2
    depth_len = padded.shape[2]
    columns = padded.shape[3]
    framed = jnp.pad(padded, ((0, 0), (0, 0), (1, 1), (1, 1)))
    carried = jnp.zeros((rows_out, kernel.shape[-1], depth_len, columns), jnp.float32)
    for depth_off in range(3):
        for row_off in range(3):
            for col_off in range(3):
                window = framed[
                    row_off : row_off + rows_out,
                    :,
                    depth_off : depth_off + depth_len,
                    col_off : col_off + columns,
                ]
                carried = carried + jnp.einsum(
                    "rcdw,ce->redw",
                    window,
                    kernel[depth_off, row_off, col_off],
                    preferred_element_type=jnp.float32,
                )
    return carried


def convolve_final(padded, kernel):
    rows_out = padded.shape[0] - 2
    depth_len = padded.shape[2]
    columns = padded.shape[3]
    framed = jnp.pad(padded, ((0, 0), (0, 0), (1, 1), (1, 1)))
    carried = jnp.zeros((rows_out, depth_len, columns), jnp.float32)
    for depth_off in range(3):
        for row_off in range(3):
            for col_off in range(3):
                window = framed[
                    row_off : row_off + rows_out,
                    :,
                    depth_off : depth_off + depth_len,
                    col_off : col_off + columns,
                ]
                carried = carried + jnp.einsum(
                    "rcdw,c->rdw",
                    window,
                    kernel[depth_off, row_off, col_off],
                    preferred_element_type=jnp.float32,
                )
    return carried


def correlate_kernel(blk_ref, blocks_ref, table_ref, ref_ref, out_ref, arranged, products):
    chunk = 32
    slots = table_ref.shape[0] // blocks_ref.shape[2]
    width = blocks_ref.shape[2]
    channels = blocks_ref.shape[1]
    units = out_ref.shape[0] // GROUPS
    cap = units // ref_ref.shape[0]
    group_size = channels // GROUPS
    rows = chunk * channels

    def step(c, carry):
        for u in range(chunk):
            unit = c * chunk + u
            for w in range(slots):
                arranged[u * channels : (u + 1) * channels, w * width : (w + 1) * width] = blocks_ref[
                    blk_ref[unit * slots + w]
                ]
        warped = jnp.dot(arranged[...], table_ref[...], preferred_element_type=jnp.float32)
        warped = warped.astype(jnp.bfloat16).astype(jnp.float32)
        lanes = products.shape[0]
        for u in range(chunk):
            unit = c * chunk + u
            tile = ref_ref[unit // cap].astype(jnp.float32)
            for j in range(lanes):
                products[j, u * channels : (u + 1) * channels, :] = (
                    warped[u * channels : (u + 1) * channels, j * 128 : (j + 1) * 128]
                    * tile[:, j * 128 : (j + 1) * 128]
                )
        start = pl.multiple_of(c * (chunk * GROUPS), chunk * GROUPS)
        for j in range(lanes):
            total = products[j, pl.ds(0, rows // group_size, stride=group_size), :]
            for k in range(1, group_size):
                total = total + products[j, pl.ds(k, rows // group_size, stride=group_size), :]
            out_ref[pl.ds(start, chunk * GROUPS), j * 128 : (j + 1) * 128] = (
                total * (GROUPS / channels)
            ).astype(out_ref.dtype)
        return carry

    lax.fori_loop(0, units // chunk, step, 0, unroll=True)


def correlate(blk, blocks, table, refs, units):
    channels, width = blocks.shape[1], blocks.shape[2]
    tpix = table.shape[1]
    chunk = 32
    return pl.pallas_call(
        correlate_kernel,
        out_shape=jax.ShapeDtypeStruct((units * GROUPS, tpix), jnp.bfloat16),
        in_specs=[
            pl.BlockSpec(memory_space=pltpu.SMEM),
            pl.BlockSpec(memory_space=pltpu.VMEM),
            pl.BlockSpec(memory_space=pltpu.VMEM),
            pl.BlockSpec(memory_space=pltpu.VMEM),
        ],
        out_specs=pl.BlockSpec(memory_space=pltpu.VMEM),
        scratch_shapes=[
            pltpu.VMEM((chunk * channels, table.shape[0]), jnp.bfloat16),
            pltpu.VMEM((tpix // 128, chunk * channels, 128), jnp.float32),
        ],
    )(blk, blocks, table, refs)


def conv_body(x_ref, m_ref, out_ref, ends_ref, *, relu, rows, cols, groups, chunk):
    width = rows * cols
    outs = m_ref.shape[2]
    depth = x_ref.shape[0] // groups - 2
    lane = lax.broadcasted_iota(jnp.int32, (outs, width), 1) % cols
    for k in range(depth // chunk):
        acc = None
        for e in range(3):
            y = None
            for b in range(3):
                window = x_ref[k * chunk * groups : (k * chunk + chunk + 2) * groups, b * cols : b * cols + width]
                part = jnp.dot(m_ref[b, e], window, preferred_element_type=jnp.float32)
                y = part if y is None else y + part
            if e == 0:
                y = jnp.where(lane >= 1, pltpu.roll(y, 1, 1), 0.0)
            elif e == 2:
                y = jnp.where(lane <= cols - 2, pltpu.roll(y, width - 1, 1), 0.0)
            acc = y if acc is None else acc + y
        if relu:
            block = lax.broadcasted_iota(jnp.int32, (outs, width), 1) // cols
            outside = ((block == 0) & (ends_ref[0] > 0)) | ((block == rows - 1) & (ends_ref[1] > 0))
            acc = jnp.where(outside, 0.0, acc)
            out_ref[(k * chunk + 1) * outs // chunk : (k * chunk + chunk + 1) * outs // chunk, :] = (
                jnp.maximum(acc, 0.0).astype(out_ref.dtype)
            )
        else:
            for r in range(rows):
                out_ref[r, k * chunk : (k + 1) * chunk, :] = acc[:, r * cols : (r + 1) * cols]
    if relu:
        pad = jnp.zeros((outs // chunk, width), out_ref.dtype)
        out_ref[: outs // chunk, :] = pad
        out_ref[out_ref.shape[0] - outs // chunk :, :] = pad


def banded(kernel, chunk):
    groups = kernel.shape[3]
    cols = (chunk + 2) * groups
    taps = kernel.reshape((3, 9) + kernel.shape[3:])
    col = lax.iota(jnp.int32, cols)
    spread = (col[None, :] % groups == jnp.arange(groups)[:, None]).astype(kernel.dtype)
    if kernel.ndim == 5:
        outs = kernel.shape[4]
        rows = chunk * outs
        row = lax.iota(jnp.int32, rows)
        lanes = jnp.einsum("xyio,ic->xyoc", taps, spread, preferred_element_type=jnp.float32)
        tiles = jnp.broadcast_to(lanes[:, :, None], (3, 9, chunk, outs, cols)).reshape(3, 9, rows, cols)
        depth_of_row = row // outs
    else:
        rows = chunk
        lanes = jnp.einsum("xyi,ic->xyc", taps, spread, preferred_element_type=jnp.float32)
        tiles = lanes[:, :, None, :]
        depth_of_row = lax.iota(jnp.int32, rows)
    band = col[None, None, :] // groups == depth_of_row[None, :, None] + jnp.arange(3)[:, None, None]
    mats = jnp.sum(jnp.where(band[:, None], tiles, 0.0), axis=0)
    return mats.astype(kernel.dtype).reshape(3, 3, rows, cols)


def conv_pair_kernel(
    ends_ref, low_ref, vol_ref, high_ref, m1_ref, m2_ref, out_ref, framed, hidden, *, rows, cols, groups
):
    halo = low_ref.shape[1]
    middle = vol_ref.shape[1]
    framed[:, :halo] = low_ref[...]
    framed[:, halo : halo + middle] = vol_ref[...]
    framed[:, halo + middle :] = high_ref[...]
    depth = framed.shape[0] // groups - 2
    first = m1_ref.shape[3] // groups - 2
    conv_body(
        framed, m1_ref, hidden, ends_ref, relu=True, rows=rows + 2, cols=cols, groups=groups, chunk=first
    )
    conv_body(
        hidden,
        m2_ref,
        out_ref,
        None,
        relu=False,
        rows=rows,
        cols=cols,
        groups=groups,
        chunk=m2_ref.shape[2],
    )


def conv_pair(ends, low, volume, high, first, second, rows, cols):
    groups = second.shape[3] // (second.shape[2] + 2)
    depth = volume.shape[0] // groups - 2
    outs = first.shape[2] * depth // (first.shape[3] // groups - 2)
    vmem = pl.BlockSpec(memory_space=pltpu.VMEM)
    return pl.pallas_call(
        functools.partial(conv_pair_kernel, rows=rows, cols=cols, groups=groups),
        out_shape=jax.ShapeDtypeStruct((rows, depth, cols), jnp.float32),
        in_specs=[pl.BlockSpec(memory_space=pltpu.SMEM)] + [vmem] * 5,
        out_specs=vmem,
        scratch_shapes=[
            pltpu.VMEM((volume.shape[0], volume.shape[1] + low.shape[1] + high.shape[1]), volume.dtype),
            pltpu.VMEM(((depth + 2) * outs // depth, (rows + 2) * cols), jnp.bfloat16),
        ],
    )(ends, low, volume, high, first, second)


def halo_cols(block, cols):
    count = lax.axis_size("view")
    forward = [(i, i + 1) for i in range(count - 1)]
    backward = [(target, source) for source, target in forward]
    low = lax.ppermute(block[:, block.shape[1] - cols :], "view", forward)
    high = lax.ppermute(block[:, :cols], "view", backward)
    return jnp.concatenate([low, block, high], axis=1)


def gather_view(block):
    count = lax.axis_size("view")
    if count & (count - 1):
        return lax.all_to_all(
            jnp.broadcast_to(block, (count,) + block.shape[1:]), "view", 0, 0, tiled=True
        )
    index = lax.axis_index("view")
    gathered = block[0]
    level = 0
    stride = count // 2
    if count >= 4:
        top = count // 4
        parts = [gathered] + [
            lax.ppermute(gathered, "view", [(i, i ^ (m * top)) for i in range(count)])
            for m in (1, 2, 3)
        ]
        order = jnp.arange(4) ^ ((index // top) % 4)
        gathered = jnp.take(jnp.stack(parts), order, axis=0).reshape((2, 2) + gathered.shape)
        level = 2
        stride = top // 2
    while stride >= 1:
        other = lax.ppermute(gathered, "view", [(i, i ^ stride) for i in range(count)])
        low = (index // stride) % 2 == 0
        gathered = jnp.where(
            low, jnp.stack([gathered, other], axis=level), jnp.stack([other, gathered], axis=level)
        )
        level += 1
        stride //= 2
    return gathered.reshape((count,) + block.shape[1:])


def pad_rows(volume):
    return with_halo(volume, (("view", 0),), 1)


def body(
    src_feat,
    ref_feat,
    weight_table,
    src_block,
    table_index,
    block_count,
    depth_plane,
    kern_one,
    kern_two,
):
    owners = lax.axis_size("view")
    features = src_feat[0]
    channels, spix = features.shape
    slots, block_width, tpix = weight_table.shape
    blocks = features.reshape(channels, spix // block_width, block_width).transpose(1, 0, 2)
    units = src_block.shape[1]
    cap = units // owners
    counts = block_count[0]
    nblocks = spix // block_width
    blocks = jnp.concatenate([blocks, jnp.zeros_like(blocks[:1])], axis=0)
    matches = table_index[0][:, :, None] == jnp.arange(slots)[None, None, :]
    live = (jnp.arange(slots)[None, :] < counts[:, None])[:, :, None] & matches
    picked = jnp.sum(jnp.where(matches, src_block[0][:, :, None], 0), axis=1)
    alive = jnp.any(live, axis=1)
    blk = jnp.where(alive, picked, nblocks).reshape(-1).astype(jnp.int32)
    depth_code = jnp.where(counts > 0, depth_plane[0], -1).astype(jnp.bfloat16)

    if units <= 128:
        code_row = jnp.where(block_count > 0, depth_plane, -1).astype(jnp.bfloat16)
        tag_block = jnp.pad(code_row, ((0, channels - 1), (0, 128 - units)))
    else:
        tag_block = jnp.pad(depth_code, (0, channels * 128 - units)).reshape(channels, 128)
    ref_all = gather_view(jnp.concatenate([ref_feat[0], tag_block], axis=1)[None])
    corr_all = correlate(
        blk, blocks, weight_table.reshape(slots * block_width, tpix), ref_all, units
    )
    corr_all, kern_one, kern_two = lax.optimization_barrier((corr_all, kern_one, kern_two))
    first = banded(kern_one, DEPTH // 4)
    second = banded(kern_two, DEPTH // 4)
    arriving = lax.all_to_all(
        corr_all.reshape(owners, cap * GROUPS, tpix),
        "view",
        split_axis=0,
        concat_axis=0,
        tiled=True,
    ).reshape(owners * cap, GROUPS, tpix)
    arriving, first, second = lax.optimization_barrier((arriving, first, second))
    depth_tags = lax.dynamic_slice_in_dim(
        ref_all[:, :, tpix:].reshape(owners, channels * 128), lax.axis_index("view") * cap, cap, axis=1
    ).reshape(owners * cap)
    labels = jnp.arange(-1, DEPTH + 1).at[0].set(-2)
    onehot = (
        depth_tags[None, :] == labels.astype(jnp.bfloat16)[:, None]
    ).astype(jnp.bfloat16)
    summed = jnp.einsum("dn,ngp->dgp", onehot, arriving, preferred_element_type=jnp.float32)
    tallies = jnp.sum(onehot.astype(jnp.float32), axis=1)
    cost_volume = (summed / jnp.maximum(tallies, 1.0)[:, None, None]).astype(jnp.bfloat16)
    columns = tpix // TROWS
    volume = cost_volume.reshape((DEPTH + 2) * GROUPS, TROWS * columns)
    count = lax.axis_size("view")
    place = lax.axis_index("view")
    ends = jnp.stack([place == 0, place == count - 1]).astype(jnp.int32)
    count = lax.axis_size("view")
    forward = [(i, i + 1) for i in range(count - 1)]
    backward = [(target, source) for source, target in forward]
    low = lax.ppermute(volume[:, volume.shape[1] - 2 * columns :], "view", forward)
    high = lax.ppermute(volume[:, : 2 * columns], "view", backward)
    scores = conv_pair(
        ends,
        low,
        volume,
        high,
        first,
        second,
        TROWS,
        columns,
    )
    return scores


def solution(mesh):
    in_specs = (
        P(("scene", "view"), None, None),
        P(("scene", "view"), None, None),
        P(),
        P(("scene", "view"), None, None),
        P(("scene", "view"), None, None),
        P(("scene", "view"), None),
        P(("scene", "view"), None),
        P(),
        P(),
    )
    out_specs = P(("scene", "view"), None, None)
    return jax.shard_map(body, mesh=mesh, in_specs=in_specs, out_specs=out_specs, check_vma=False)
```

```python
import functools

import jax
import jax.numpy as jnp
from jax import lax
from jax.experimental import pallas as pl
from jax.experimental.pallas import tpu as pltpu
from jax.sharding import PartitionSpec as P

GROUPS = 8
DEPTH = 64
TROWS = 4


def with_halo(block, sides, width):
    for axis, dim in sides:
        count = lax.axis_size(axis)
        forward = [(i, i + 1) for i in range(count - 1)]
        backward = [(target, source) for source, target in forward]
        low = lax.ppermute(
            lax.slice_in_dim(block, block.shape[dim] - width, None, axis=dim), axis, forward
        )
        high = lax.ppermute(lax.slice_in_dim(block, 0, width, axis=dim), axis, backward)
        block = jnp.concatenate([low, block, high], axis=dim)
    return block


def convolve_full(padded, kernel):
    rows_out = padded.shape[0] - 2
    depth_len = padded.shape[2]
    columns = padded.shape[3]
    framed = jnp.pad(padded, ((0, 0), (0, 0), (1, 1), (1, 1)))
    carried = jnp.zeros((rows_out, kernel.shape[-1], depth_len, columns), jnp.float32)
    for depth_off in range(3):
        for row_off in range(3):
            for col_off in range(3):
                window = framed[
                    row_off : row_off + rows_out,
                    :,
                    depth_off : depth_off + depth_len,
                    col_off : col_off + columns,
                ]
                carried = carried + jnp.einsum(
                    "rcdw,ce->redw",
                    window,
                    kernel[depth_off, row_off, col_off],
                    preferred_element_type=jnp.float32,
                )
    return carried


def convolve_final(padded, kernel):
    rows_out = padded.shape[0] - 2
    depth_len = padded.shape[2]
    columns = padded.shape[3]
    framed = jnp.pad(padded, ((0, 0), (0, 0), (1, 1), (1, 1)))
    carried = jnp.zeros((rows_out, depth_len, columns), jnp.float32)
    for depth_off in range(3):
        for row_off in range(3):
            for col_off in range(3):
                window = framed[
                    row_off : row_off + rows_out,
                    :,
                    depth_off : depth_off + depth_len,
                    col_off : col_off + columns,
                ]
                carried = carried + jnp.einsum(
                    "rcdw,c->rdw",
                    window,
                    kernel[depth_off, row_off, col_off],
                    preferred_element_type=jnp.float32,
                )
    return carried


def correlate_kernel(blk_ref, blocks_ref, table_ref, ref_ref, out_ref, arranged, products):
    chunk = 32
    slots = table_ref.shape[0] // blocks_ref.shape[2]
    width = blocks_ref.shape[2]
    channels = blocks_ref.shape[1]
    units = out_ref.shape[0] // GROUPS
    cap = units // ref_ref.shape[0]
    group_size = channels // GROUPS
    rows = chunk * channels

    def step(c, carry):
        for u in range(chunk):
            unit = c * chunk + u
            for w in range(slots):
                arranged[u * channels : (u + 1) * channels, w * width : (w + 1) * width] = blocks_ref[
                    blk_ref[unit * slots + w]
                ]
        warped = jnp.dot(arranged[...], table_ref[...], preferred_element_type=jnp.float32)
        warped = warped.astype(jnp.bfloat16).astype(jnp.float32)
        lanes = products.shape[0]
        for u in range(chunk):
            unit = c * chunk + u
            tile = ref_ref[unit // cap].astype(jnp.float32)
            for j in range(lanes):
                products[j, u * channels : (u + 1) * channels, :] = (
                    warped[u * channels : (u + 1) * channels, j * 128 : (j + 1) * 128]
                    * tile[:, j * 128 : (j + 1) * 128]
                )
        start = pl.multiple_of(c * (chunk * GROUPS), chunk * GROUPS)
        for j in range(lanes):
            total = products[j, pl.ds(0, rows // group_size, stride=group_size), :]
            for k in range(1, group_size):
                total = total + products[j, pl.ds(k, rows // group_size, stride=group_size), :]
            out_ref[pl.ds(start, chunk * GROUPS), j * 128 : (j + 1) * 128] = (
                total * (GROUPS / channels)
            ).astype(out_ref.dtype)
        return carry

    lax.fori_loop(0, units // chunk, step, 0, unroll=True)


def correlate(blk, blocks, table, refs, units):
    channels, width = blocks.shape[1], blocks.shape[2]
    tpix = table.shape[1]
    chunk = 32
    return pl.pallas_call(
        correlate_kernel,
        out_shape=jax.ShapeDtypeStruct((units * GROUPS, tpix), jnp.bfloat16),
        in_specs=[
            pl.BlockSpec(memory_space=pltpu.SMEM),
            pl.BlockSpec(memory_space=pltpu.VMEM),
            pl.BlockSpec(memory_space=pltpu.VMEM),
            pl.BlockSpec(memory_space=pltpu.VMEM),
        ],
        out_specs=pl.BlockSpec(memory_space=pltpu.VMEM),
        scratch_shapes=[
            pltpu.VMEM((chunk * channels, table.shape[0]), jnp.bfloat16),
            pltpu.VMEM((tpix // 128, chunk * channels, 128), jnp.float32),
        ],
    )(blk, blocks, table, refs)


def conv_body(x_ref, m_ref, out_ref, ends_ref, *, relu, rows, cols, groups, chunk):
    width = rows * cols
    outs = m_ref.shape[2]
    depth = x_ref.shape[0] // groups - 2
    lane = lax.broadcasted_iota(jnp.int32, (outs, width), 1) % cols
    for k in range(depth // chunk):
        acc = None
        for e in range(3):
            y = None
            for b in range(3):
                window = x_ref[k * chunk * groups : (k * chunk + chunk + 2) * groups, b * cols : b * cols + width]
                part = jnp.dot(m_ref[b, e], window, preferred_element_type=jnp.float32)
                y = part if y is None else y + part
            if e == 0:
                y = jnp.where(lane >= 1, pltpu.roll(y, 1, 1), 0.0)
            elif e == 2:
                y = jnp.where(lane <= cols - 2, pltpu.roll(y, width - 1, 1), 0.0)
            acc = y if acc is None else acc + y
        if relu:
            block = lax.broadcasted_iota(jnp.int32, (outs, width), 1) // cols
            outside = ((block == 0) & (ends_ref[0] > 0)) | ((block == rows - 1) & (ends_ref[1] > 0))
            acc = jnp.where(outside, 0.0, acc)
            out_ref[(k * chunk + 1) * outs // chunk : (k * chunk + chunk + 1) * outs // chunk, :] = (
                jnp.maximum(acc, 0.0).astype(out_ref.dtype)
            )
        else:
            for r in range(rows):
                out_ref[r, k * chunk : (k + 1) * chunk, :] = acc[:, r * cols : (r + 1) * cols]
    if relu:
        pad = jnp.zeros((outs // chunk, width), out_ref.dtype)
        out_ref[: outs // chunk, :] = pad
        out_ref[out_ref.shape[0] - outs // chunk :, :] = pad


def banded(kernel, chunk):
    groups = kernel.shape[3]
    cols = (chunk + 2) * groups
    taps = kernel.reshape((3, 9) + kernel.shape[3:])
    col = lax.iota(jnp.int32, cols)
    spread = (col[None, :] % groups == jnp.arange(groups)[:, None]).astype(kernel.dtype)
    if kernel.ndim == 5:
        outs = kernel.shape[4]
        rows = chunk * outs
        row = lax.iota(jnp.int32, rows)
        lanes = jnp.einsum("xyio,ic->xyoc", taps, spread, preferred_element_type=jnp.float32)
        tiles = jnp.broadcast_to(lanes[:, :, None], (3, 9, chunk, outs, cols)).reshape(3, 9, rows, cols)
        depth_of_row = row // outs
    else:
        rows = chunk
        lanes = jnp.einsum("xyi,ic->xyc", taps, spread, preferred_element_type=jnp.float32)
        tiles = lanes[:, :, None, :]
        depth_of_row = lax.iota(jnp.int32, rows)
    band = col[None, None, :] // groups == depth_of_row[None, :, None] + jnp.arange(3)[:, None, None]
    mats = jnp.sum(jnp.where(band[:, None], tiles, 0.0), axis=0)
    return mats.astype(kernel.dtype).reshape(3, 3, rows, cols)


def conv_pair_kernel(
    ends_ref, low_ref, vol_ref, high_ref, m1_ref, m2_ref, out_ref, framed, hidden, *, rows, cols, groups
):
    halo = low_ref.shape[1]
    middle = vol_ref.shape[1]
    framed[:, :halo] = low_ref[...]
    framed[:, halo : halo + middle] = vol_ref[...]
    framed[:, halo + middle :] = high_ref[...]
    depth = framed.shape[0] // groups - 2
    first = m1_ref.shape[3] // groups - 2
    conv_body(
        framed, m1_ref, hidden, ends_ref, relu=True, rows=rows + 2, cols=cols, groups=groups, chunk=first
    )
    conv_body(
        hidden,
        m2_ref,
        out_ref,
        None,
        relu=False,
        rows=rows,
        cols=cols,
        groups=groups,
        chunk=m2_ref.shape[2],
    )


def conv_pair(ends, low, volume, high, first, second, rows, cols):
    groups = second.shape[3] // (second.shape[2] + 2)
    depth = volume.shape[0] // groups - 2
    outs = first.shape[2] * depth // (first.shape[3] // groups - 2)
    vmem = pl.BlockSpec(memory_space=pltpu.VMEM)
    return pl.pallas_call(
        functools.partial(conv_pair_kernel, rows=rows, cols=cols, groups=groups),
        out_shape=jax.ShapeDtypeStruct((rows, depth, cols), jnp.float32),
        in_specs=[pl.BlockSpec(memory_space=pltpu.SMEM)] + [vmem] * 5,
        out_specs=vmem,
        scratch_shapes=[
            pltpu.VMEM((volume.shape[0], volume.shape[1] + low.shape[1] + high.shape[1]), volume.dtype),
            pltpu.VMEM(((depth + 2) * outs // depth, (rows + 2) * cols), jnp.bfloat16),
        ],
    )(ends, low, volume, high, first, second)


def halo_cols(block, cols):
    count = lax.axis_size("view")
    forward = [(i, i + 1) for i in range(count - 1)]
    backward = [(target, source) for source, target in forward]
    low = lax.ppermute(block[:, block.shape[1] - cols :], "view", forward)
    high = lax.ppermute(block[:, :cols], "view", backward)
    return jnp.concatenate([low, block, high], axis=1)


def gather_view(block):
    count = lax.axis_size("view")
    if count & (count - 1):
        return lax.all_to_all(
            jnp.broadcast_to(block, (count,) + block.shape[1:]), "view", 0, 0, tiled=True
        )
    index = lax.axis_index("view")
    gathered = block[0]
    level = 0
    stride = count // 2
    if count >= 4:
        top = count // 4
        parts = [gathered] + [
            lax.ppermute(gathered, "view", [(i, i ^ (m * top)) for i in range(count)])
            for m in (1, 2, 3)
        ]
        order = jnp.arange(4) ^ ((index // top) % 4)
        gathered = jnp.take(jnp.stack(parts), order, axis=0).reshape((2, 2) + gathered.shape)
        level = 2
        stride = top // 2
    while stride >= 1:
        other = lax.ppermute(gathered, "view", [(i, i ^ stride) for i in range(count)])
        low = (index // stride) % 2 == 0
        gathered = jnp.where(
            low, jnp.stack([gathered, other], axis=level), jnp.stack([other, gathered], axis=level)
        )
        level += 1
        stride //= 2
    return gathered.reshape((count,) + block.shape[1:])


def pad_rows(volume):
    return with_halo(volume, (("view", 0),), 1)


def body(
    src_feat,
    ref_feat,
    weight_table,
    src_block,
    table_index,
    block_count,
    depth_plane,
    kern_one,
    kern_two,
):
    owners = lax.axis_size("view")
    features = src_feat[0]
    channels, spix = features.shape
    slots, block_width, tpix = weight_table.shape
    blocks = features.reshape(channels, spix // block_width, block_width).transpose(1, 0, 2)
    units = src_block.shape[1]
    cap = units // owners
    counts = block_count[0]
    nblocks = spix // block_width
    blocks = jnp.concatenate([blocks, jnp.zeros_like(blocks[:1])], axis=0)
    matches = table_index[0][:, :, None] == jnp.arange(slots)[None, None, :]
    live = (jnp.arange(slots)[None, :] < counts[:, None])[:, :, None] & matches
    picked = jnp.sum(jnp.where(matches, src_block[0][:, :, None], 0), axis=1)
    alive = jnp.any(live, axis=1)
    blk = jnp.where(alive, picked, nblocks).reshape(-1).astype(jnp.int32)
    depth_code = jnp.where(counts > 0, depth_plane[0], -1).astype(jnp.bfloat16)

    tag_block = jnp.pad(depth_code, (0, channels * 128 - units)).reshape(channels, 128)
    ref_all = gather_view(jnp.concatenate([ref_feat[0], tag_block], axis=1)[None])
    corr_all = correlate(
        blk, blocks, weight_table.reshape(slots * block_width, tpix), ref_all, units
    )
    corr_all, kern_one, kern_two = lax.optimization_barrier((corr_all, kern_one, kern_two))
    first = banded(kern_one, DEPTH // 4)
    second = banded(kern_two, DEPTH // 8)
    arriving = lax.all_to_all(
        corr_all.reshape(owners, cap * GROUPS, tpix),
        "view",
        split_axis=0,
        concat_axis=0,
        tiled=True,
    ).reshape(owners * cap, GROUPS, tpix)
    arriving, first, second = lax.optimization_barrier((arriving, first, second))
    depth_tags = lax.dynamic_slice_in_dim(
        ref_all[:, :, tpix:].reshape(owners, channels * 128), lax.axis_index("view") * cap, cap, axis=1
    ).reshape(owners * cap)
    labels = jnp.arange(-1, DEPTH + 1).at[0].set(-2)
    onehot = (
        depth_tags[None, :] == labels.astype(jnp.bfloat16)[:, None]
    ).astype(jnp.bfloat16)
    summed = jnp.einsum("dn,ngp->dgp", onehot, arriving, preferred_element_type=jnp.float32)
    tallies = jnp.sum(onehot.astype(jnp.float32), axis=1)
    cost_volume = (summed / jnp.maximum(tallies, 1.0)[:, None, None]).astype(jnp.bfloat16)
    columns = tpix // TROWS
    volume = cost_volume.reshape((DEPTH + 2) * GROUPS, TROWS * columns)
    count = lax.axis_size("view")
    place = lax.axis_index("view")
    ends = jnp.stack([place == 0, place == count - 1]).astype(jnp.int32)
    count = lax.axis_size("view")
    forward = [(i, i + 1) for i in range(count - 1)]
    backward = [(target, source) for source, target in forward]
    low = lax.ppermute(volume[:, volume.shape[1] - 2 * columns :], "view", forward)
    high = lax.ppermute(volume[:, : 2 * columns], "view", backward)
    scores = conv_pair(
        ends,
        low,
        volume,
        high,
        first,
        second,
        TROWS,
        columns,
    )
    return scores


def solution(mesh):
    in_specs = (
        P(("scene", "view"), None, None),
        P(("scene", "view"), None, None),
        P(),
        P(("scene", "view"), None, None),
        P(("scene", "view"), None, None),
        P(("scene", "view"), None),
        P(("scene", "view"), None),
        P(),
        P(),
    )
    out_specs = P(("scene", "view"), None, None)
    return jax.shard_map(body, mesh=mesh, in_specs=in_specs, out_specs=out_specs, check_vma=False)
```

```python
import functools

import jax
import jax.numpy as jnp
from jax import lax
from jax.experimental import pallas as pl
from jax.experimental.pallas import tpu as pltpu
from jax.sharding import PartitionSpec as P

GROUPS = 8
DEPTH = 64
TROWS = 4


def with_halo(block, sides, width):
    for axis, dim in sides:
        count = lax.axis_size(axis)
        forward = [(i, i + 1) for i in range(count - 1)]
        backward = [(target, source) for source, target in forward]
        low = lax.ppermute(
            lax.slice_in_dim(block, block.shape[dim] - width, None, axis=dim), axis, forward
        )
        high = lax.ppermute(lax.slice_in_dim(block, 0, width, axis=dim), axis, backward)
        block = jnp.concatenate([low, block, high], axis=dim)
    return block


def convolve_full(padded, kernel):
    rows_out = padded.shape[0] - 2
    depth_len = padded.shape[2]
    columns = padded.shape[3]
    framed = jnp.pad(padded, ((0, 0), (0, 0), (1, 1), (1, 1)))
    carried = jnp.zeros((rows_out, kernel.shape[-1], depth_len, columns), jnp.float32)
    for depth_off in range(3):
        for row_off in range(3):
            for col_off in range(3):
                window = framed[
                    row_off : row_off + rows_out,
                    :,
                    depth_off : depth_off + depth_len,
                    col_off : col_off + columns,
                ]
                carried = carried + jnp.einsum(
                    "rcdw,ce->redw",
                    window,
                    kernel[depth_off, row_off, col_off],
                    preferred_element_type=jnp.float32,
                )
    return carried


def convolve_final(padded, kernel):
    rows_out = padded.shape[0] - 2
    depth_len = padded.shape[2]
    columns = padded.shape[3]
    framed = jnp.pad(padded, ((0, 0), (0, 0), (1, 1), (1, 1)))
    carried = jnp.zeros((rows_out, depth_len, columns), jnp.float32)
    for depth_off in range(3):
        for row_off in range(3):
            for col_off in range(3):
                window = framed[
                    row_off : row_off + rows_out,
                    :,
                    depth_off : depth_off + depth_len,
                    col_off : col_off + columns,
                ]
                carried = carried + jnp.einsum(
                    "rcdw,c->rdw",
                    window,
                    kernel[depth_off, row_off, col_off],
                    preferred_element_type=jnp.float32,
                )
    return carried


def correlate_kernel(blk_ref, bit_ref, blocks_ref, table_ref, ref_ref, partner_ref, out_ref, arranged, products, *, pairs):
    chunk = 32
    slots = table_ref.shape[0] // blocks_ref.shape[2]
    width = blocks_ref.shape[2]
    channels = blocks_ref.shape[1]
    units = out_ref.shape[0] // GROUPS
    cap = units // (ref_ref.shape[0] * (2 if pairs else 1))
    group_size = channels // GROUPS
    rows = chunk * channels

    def step(c, carry):
        for u in range(chunk):
            unit = c * chunk + u
            for w in range(slots):
                arranged[u * channels : (u + 1) * channels, w * width : (w + 1) * width] = blocks_ref[
                    blk_ref[unit * slots + w]
                ]
        warped = jnp.dot(arranged[...], table_ref[...], preferred_element_type=jnp.float32)
        warped = warped.astype(jnp.bfloat16).astype(jnp.float32)
        lanes = products.shape[0]
        for u in range(chunk):
            unit = c * chunk + u
            if pairs:
                owner = unit // cap
                tile = jnp.where(
                    owner % 2 == bit_ref[0], ref_ref[owner // 2], partner_ref[owner // 2]
                ).astype(jnp.float32)
            else:
                tile = ref_ref[unit // cap].astype(jnp.float32)
            for j in range(lanes):
                products[j, u * channels : (u + 1) * channels, :] = (
                    warped[u * channels : (u + 1) * channels, j * 128 : (j + 1) * 128]
                    * tile[:, j * 128 : (j + 1) * 128]
                )
        start = pl.multiple_of(c * (chunk * GROUPS), chunk * GROUPS)
        for j in range(lanes):
            total = products[j, pl.ds(0, rows // group_size, stride=group_size), :]
            for k in range(1, group_size):
                total = total + products[j, pl.ds(k, rows // group_size, stride=group_size), :]
            out_ref[pl.ds(start, chunk * GROUPS), j * 128 : (j + 1) * 128] = (
                total * (GROUPS / channels)
            ).astype(out_ref.dtype)
        return carry

    lax.fori_loop(0, units // chunk, step, 0, unroll=True)


def correlate(blk, blocks, table, mine, partner, bit, units):
    channels = blocks.shape[1]
    tpix = table.shape[1]
    chunk = 32
    pairs = bit is not None
    bits = jnp.reshape(bit if pairs else 0, (1,)).astype(jnp.int32)
    return pl.pallas_call(
        functools.partial(correlate_kernel, pairs=pairs),
        out_shape=jax.ShapeDtypeStruct((units * GROUPS, tpix), jnp.bfloat16),
        in_specs=[
            pl.BlockSpec(memory_space=pltpu.SMEM),
            pl.BlockSpec(memory_space=pltpu.SMEM),
            pl.BlockSpec(memory_space=pltpu.VMEM),
            pl.BlockSpec(memory_space=pltpu.VMEM),
            pl.BlockSpec(memory_space=pltpu.VMEM),
            pl.BlockSpec(memory_space=pltpu.VMEM),
        ],
        out_specs=pl.BlockSpec(memory_space=pltpu.VMEM),
        scratch_shapes=[
            pltpu.VMEM((chunk * channels, table.shape[0]), jnp.bfloat16),
            pltpu.VMEM((tpix // 128, chunk * channels, 128), jnp.float32),
        ],
    )(blk, bits, blocks, table, mine, partner)


def conv_body(x_ref, m_ref, out_ref, ends_ref, *, relu, rows, cols, groups, chunk):
    width = rows * cols
    outs = m_ref.shape[2]
    depth = x_ref.shape[0] // groups - 2
    lane = lax.broadcasted_iota(jnp.int32, (outs, width), 1) % cols
    for k in range(depth // chunk):
        acc = None
        for e in range(3):
            y = None
            for b in range(3):
                window = x_ref[k * chunk * groups : (k * chunk + chunk + 2) * groups, b * cols : b * cols + width]
                part = jnp.dot(m_ref[b, e], window, preferred_element_type=jnp.float32)
                y = part if y is None else y + part
            if e == 0:
                y = jnp.where(lane >= 1, pltpu.roll(y, 1, 1), 0.0)
            elif e == 2:
                y = jnp.where(lane <= cols - 2, pltpu.roll(y, width - 1, 1), 0.0)
            acc = y if acc is None else acc + y
        if relu:
            block = lax.broadcasted_iota(jnp.int32, (outs, width), 1) // cols
            outside = ((block == 0) & (ends_ref[0] > 0)) | ((block == rows - 1) & (ends_ref[1] > 0))
            acc = jnp.where(outside, 0.0, acc)
            out_ref[(k * chunk + 1) * outs // chunk : (k * chunk + chunk + 1) * outs // chunk, :] = (
                jnp.maximum(acc, 0.0).astype(out_ref.dtype)
            )
        else:
            for r in range(rows):
                out_ref[r, k * chunk : (k + 1) * chunk, :] = acc[:, r * cols : (r + 1) * cols]
    if relu:
        pad = jnp.zeros((outs // chunk, width), out_ref.dtype)
        out_ref[: outs // chunk, :] = pad
        out_ref[out_ref.shape[0] - outs // chunk :, :] = pad


def banded(kernel, chunk):
    groups = kernel.shape[3]
    cols = (chunk + 2) * groups
    taps = kernel.reshape((3, 9) + kernel.shape[3:])
    col = lax.iota(jnp.int32, cols)
    spread = (col[None, :] % groups == jnp.arange(groups)[:, None]).astype(kernel.dtype)
    if kernel.ndim == 5:
        outs = kernel.shape[4]
        rows = chunk * outs
        row = lax.iota(jnp.int32, rows)
        lanes = jnp.einsum("xyio,ic->xyoc", taps, spread, preferred_element_type=jnp.float32)
        tiles = jnp.broadcast_to(lanes[:, :, None], (3, 9, chunk, outs, cols)).reshape(3, 9, rows, cols)
        depth_of_row = row // outs
    else:
        rows = chunk
        lanes = jnp.einsum("xyi,ic->xyc", taps, spread, preferred_element_type=jnp.float32)
        tiles = lanes[:, :, None, :]
        depth_of_row = lax.iota(jnp.int32, rows)
    band = col[None, None, :] // groups == depth_of_row[None, :, None] + jnp.arange(3)[:, None, None]
    mats = jnp.sum(jnp.where(band[:, None], tiles, 0.0), axis=0)
    return mats.astype(kernel.dtype).reshape(3, 3, rows, cols)


def conv_pair_kernel(
    ends_ref, low_ref, vol_ref, high_ref, m1_ref, m2_ref, out_ref, framed, hidden, *, rows, cols, groups
):
    halo = low_ref.shape[1]
    middle = vol_ref.shape[1]
    framed[:, :halo] = low_ref[...]
    framed[:, halo : halo + middle] = vol_ref[...]
    framed[:, halo + middle :] = high_ref[...]
    depth = framed.shape[0] // groups - 2
    first = m1_ref.shape[3] // groups - 2
    conv_body(
        framed, m1_ref, hidden, ends_ref, relu=True, rows=rows + 2, cols=cols, groups=groups, chunk=first
    )
    conv_body(
        hidden,
        m2_ref,
        out_ref,
        None,
        relu=False,
        rows=rows,
        cols=cols,
        groups=groups,
        chunk=m2_ref.shape[2],
    )


def conv_pair(ends, low, volume, high, first, second, rows, cols):
    groups = second.shape[3] // (second.shape[2] + 2)
    depth = volume.shape[0] // groups - 2
    outs = first.shape[2] * depth // (first.shape[3] // groups - 2)
    vmem = pl.BlockSpec(memory_space=pltpu.VMEM)
    return pl.pallas_call(
        functools.partial(conv_pair_kernel, rows=rows, cols=cols, groups=groups),
        out_shape=jax.ShapeDtypeStruct((rows, depth, cols), jnp.float32),
        in_specs=[pl.BlockSpec(memory_space=pltpu.SMEM)] + [vmem] * 5,
        out_specs=vmem,
        scratch_shapes=[
            pltpu.VMEM((volume.shape[0], volume.shape[1] + low.shape[1] + high.shape[1]), volume.dtype),
            pltpu.VMEM(((depth + 2) * outs // depth, (rows + 2) * cols), jnp.bfloat16),
        ],
    )(ends, low, volume, high, first, second)


def halo_cols(block, cols):
    count = lax.axis_size("view")
    forward = [(i, i + 1) for i in range(count - 1)]
    backward = [(target, source) for source, target in forward]
    low = lax.ppermute(block[:, block.shape[1] - cols :], "view", forward)
    high = lax.ppermute(block[:, :cols], "view", backward)
    return jnp.concatenate([low, block, high], axis=1)


def gather_view(block, split=False):
    count = lax.axis_size("view")
    if count & (count - 1) or (split and count < 8):
        whole = lax.all_to_all(
            jnp.broadcast_to(block, (count,) + block.shape[1:]), "view", 0, 0, tiled=True
        )
        return (whole, whole, None) if split else whole
    index = lax.axis_index("view")
    gathered = block[0]
    level = 0
    stride = count // 2
    if count >= 4:
        top = count // 4
        parts = [gathered] + [
            lax.ppermute(gathered, "view", [(i, i ^ (m * top)) for i in range(count)])
            for m in (1, 2, 3)
        ]
        order = jnp.arange(4) ^ ((index // top) % 4)
        gathered = jnp.take(jnp.stack(parts), order, axis=0).reshape((2, 2) + gathered.shape)
        level = 2
        stride = top // 2
    while stride >= 1:
        other = lax.ppermute(gathered, "view", [(i, i ^ stride) for i in range(count)])
        if split and stride == 1:
            half = (count // 2,) + block.shape[1:]
            return gathered.reshape(half), other.reshape(half), index % 2
        low = (index // stride) % 2 == 0
        gathered = jnp.where(
            low, jnp.stack([gathered, other], axis=level), jnp.stack([other, gathered], axis=level)
        )
        level += 1
        stride //= 2
    return gathered.reshape((count,) + block.shape[1:])


def pad_rows(volume):
    return with_halo(volume, (("view", 0),), 1)


def body(
    src_feat,
    ref_feat,
    weight_table,
    src_block,
    table_index,
    block_count,
    depth_plane,
    kern_one,
    kern_two,
):
    owners = lax.axis_size("view")
    features = src_feat[0]
    channels, spix = features.shape
    slots, block_width, tpix = weight_table.shape
    blocks = features.reshape(channels, spix // block_width, block_width).transpose(1, 0, 2)
    units = src_block.shape[1]
    cap = units // owners
    counts = block_count[0]
    nblocks = spix // block_width
    blocks = jnp.concatenate([blocks, jnp.zeros_like(blocks[:1])], axis=0)
    matches = table_index[0][:, :, None] == jnp.arange(slots)[None, None, :]
    live = (jnp.arange(slots)[None, :] < counts[:, None])[:, :, None] & matches
    picked = jnp.sum(jnp.where(matches, src_block[0][:, :, None], 0), axis=1)
    alive = jnp.any(live, axis=1)
    blk = jnp.where(alive, picked, nblocks).reshape(-1).astype(jnp.int32)
    depth_code = jnp.where(counts > 0, depth_plane[0], -1).astype(jnp.bfloat16)

    if units <= 128:
        code_row = jnp.where(block_count > 0, depth_plane, -1).astype(jnp.bfloat16)
        tag_block = jnp.pad(code_row, ((0, channels - 1), (0, 128 - units)))
    else:
        tag_block = jnp.pad(depth_code, (0, channels * 128 - units)).reshape(channels, 128)
    mine, partner, bit = gather_view(
        jnp.concatenate([ref_feat[0], tag_block], axis=1)[None], split=True
    )
    corr_all = correlate(
        blk, blocks, weight_table.reshape(slots * block_width, tpix), mine, partner, bit, units
    )
    corr_all, kern_one, kern_two = lax.optimization_barrier((corr_all, kern_one, kern_two))
    first = banded(kern_one, DEPTH // 4)
    second = banded(kern_two, DEPTH // 4)
    arriving = lax.all_to_all(
        corr_all.reshape(owners, cap * GROUPS, tpix),
        "view",
        split_axis=0,
        concat_axis=0,
        tiled=True,
    ).reshape(owners * cap, GROUPS, tpix)
    arriving, first, second = lax.optimization_barrier((arriving, first, second))
    if bit is None:
        tag_rows = mine[:, :, tpix:]
    else:
        own, other = mine[:, :, tpix:], partner[:, :, tpix:]
        tag_rows = jnp.where(
            bit == 0, jnp.stack([own, other], axis=1), jnp.stack([other, own], axis=1)
        )
    depth_tags = lax.dynamic_slice_in_dim(
        tag_rows.reshape(owners, channels * 128), lax.axis_index("view") * cap, cap, axis=1
    ).reshape(owners * cap)
    labels = jnp.arange(-1, DEPTH + 1).at[0].set(-2)
    onehot = (
        depth_tags[None, :] == labels.astype(jnp.bfloat16)[:, None]
    ).astype(jnp.bfloat16)
    summed = jnp.einsum("dn,ngp->dgp", onehot, arriving, preferred_element_type=jnp.float32)
    tallies = jnp.sum(onehot.astype(jnp.float32), axis=1)
    cost_volume = (summed / jnp.maximum(tallies, 1.0)[:, None, None]).astype(jnp.bfloat16)
    columns = tpix // TROWS
    volume = cost_volume.reshape((DEPTH + 2) * GROUPS, TROWS * columns)
    count = lax.axis_size("view")
    place = lax.axis_index("view")
    ends = jnp.stack([place == 0, place == count - 1]).astype(jnp.int32)
    count = lax.axis_size("view")
    forward = [(i, i + 1) for i in range(count - 1)]
    backward = [(target, source) for source, target in forward]
    low = lax.ppermute(volume[:, volume.shape[1] - 2 * columns :], "view", forward)
    high = lax.ppermute(volume[:, : 2 * columns], "view", backward)
    scores = conv_pair(
        ends,
        low,
        volume,
        high,
        first,
        second,
        TROWS,
        columns,
    )
    return scores


def solution(mesh):
    in_specs = (
        P(("scene", "view"), None, None),
        P(("scene", "view"), None, None),
        P(),
        P(("scene", "view"), None, None),
        P(("scene", "view"), None, None),
        P(("scene", "view"), None),
        P(("scene", "view"), None),
        P(),
        P(),
    )
    out_specs = P(("scene", "view"), None, None)
    return jax.shard_map(body, mesh=mesh, in_specs=in_specs, out_specs=out_specs, check_vma=False)
```
